32 devices in a mesh: ctx: 8 (over z, y), ch: 4 (over x, core).
Axes of the slice: x: 2, y: 2, z: 4, core: 2. Of those that a mesh axis runs over, the one named last changes fastest.
Arguments:
- projected: bfloat16 [3, 8192, 4096], P(None, 'ctx', 'ch'), may hold values from -6 to 6
- tap_weights: bfloat16 [3, 3, 4096], P(None, None, 'ch'), may hold values from -3.59375 to 3.59375
- pole_rates: float32 [16, 4096], P(None, 'ch'), may hold values from 1.2207031e-05 to 0.0625
- residues: float32 [16, 4096], P(None, 'ch'), may hold values from -1.4143862 to 1.4143862
- long_bias: float32 [4096], P('ch'), may hold values from -4 to 4
- out_weight: bfloat16 [4096, 4096], P(None, 'ch'), may hold values from -0.09375 to 0.09375
Outputs:
- mixed_out: bfloat16 [8192, 4096], P('ctx', 'ch')
The draws below stay inside these ranges and needn't reach their ends.
All inputs are finite; a program needn't handle non-finite values.
Results may differ from the reference program's by a relative error of at most 0.012.
Values may be sent and summed in bfloat16 or wider, within the bound.
No kernel may reach another device: no remote copies, remote signals or barrier semaphores. Data moves between devices by JAX's collectives and lax.ppermute only.
A program may use at most 256 MiB of HBM per device.

```python
import math
import jax
import jax.numpy as jnp
from jax import lax

D = 4096
POLES = 16
TAPS = 3
BLOCK = 64
SEQ = 8192
N_CH = 4


def pole_pair(key):
    base_key = jax.random.fold_in(key, 11)
    slow_key, fast_key, pick_key, sign_key = jax.random.split(base_key, 4)
    slow_rates = jnp.exp(jax.random.uniform(slow_key, (POLES, D), jnp.float32, math.log(0.1 / SEQ), math.log(2.0 / SEQ)))
    fast_rates = jnp.exp(jax.random.uniform(fast_key, (POLES, D), jnp.float32, math.log(1.0 / BLOCK), math.log(4.0 / BLOCK)))
    keeping = 0.5
    chosen = jax.random.bernoulli(pick_key, keeping, (POLES, D))
    pole_rates = jnp.clip(jnp.where(chosen, slow_rates, fast_rates), 0.1 / SEQ, 4.0 / BLOCK)
    bound_value = 4.0 * math.sqrt(2.0 / POLES) * math.sqrt(1.0 + 2.0 / SEQ)
    spread_scale = jnp.sqrt(1.0 - jnp.exp(-2.0 * pole_rates) + 2.0 / SEQ) * math.sqrt(2.0 / POLES)
    residues = jax.random.truncated_normal(sign_key, -4.0, 4.0, (POLES, D), jnp.float32) * spread_scale
    residues = jnp.clip(residues, -bound_value, bound_value)
    return (pole_rates, residues)


def draw_pole_rates(key, part):
    return pole_pair(key)[0]


def draw_residues(key, part):
    return pole_pair(key)[1]


def level_of(own_key, shape, pieces, low, top_value):
    loudness = 1.0
    for dim, blocks in pieces:
        steps = jax.random.uniform(jax.random.fold_in(jax.random.fold_in(own_key, 6), dim), (blocks,), jnp.float32, low / len(pieces), top_value / len(pieces))
        loudness = loudness * jnp.repeat(jnp.exp(steps), shape[dim] // blocks).reshape((-1,) + (1,) * (len(shape) - 1 - dim))
    return loudness


def bell_draw(own_key, shape, spread, limit, cuts=(), held_as=jnp.bfloat16):
    entries = jax.random.normal(own_key, shape, jnp.float32) * spread
    if len(cuts) > 0:
        entries = level_of(own_key, shape, cuts, -0.22, 0.18) * entries
    return jnp.clip(entries, min=-limit, max=limit).astype(held_as)


def setup_inputs(seed: int = 0) -> dict:
    seeds = jax.random.split(jax.random.key(seed), 7)
    return {
        "projected": bell_draw(seeds[0], (3, SEQ, D), 1.0, 6.0, ((1, 8), (2, 4))),
        "tap_weights": bell_draw(seeds[1], (TAPS, 3, D), 0.6, 3.59375, ((2, 4),)),
        "pole_rates": draw_pole_rates(jax.random.fold_in(seeds[6], 71), 0),
        "residues": draw_residues(jax.random.fold_in(seeds[6], 71), 0),
        "long_bias": bell_draw(seeds[4], (D,), 1.0, 4.0, ((0, 4),), jnp.float32),
        "out_weight": bell_draw(seeds[5], (D, D), D ** -0.5, 0.09375, ((1, 4),)),
    }


def make_tables(pole_rates, residues, block_size):
    lag_steps = jnp.arange(block_size, dtype=jnp.float32)
    powers = jnp.exp(-pole_rates[None, :, :] * lag_steps[:, None, None])
    kernel = jnp.sum(powers * residues[None, :, :], axis=1)
    offsets = jnp.arange(block_size, dtype=jnp.int32)[:, None] - jnp.arange(block_size, dtype=jnp.int32)[None, :]
    toeplitz = jnp.where((offsets >= 0)[:, :, None], kernel[jnp.maximum(offsets, 0)], jnp.float32(0.0))
    end_weights = powers[::-1]
    read_weights = powers * jnp.exp(-pole_rates)[None, :, :] * residues[None, :, :]
    block_decay = jnp.exp(-pole_rates * block_size)
    return toeplitz, end_weights, read_weights, block_decay


def reference(projected, tap_weights, pole_rates, residues, long_bias, out_weight):
    group_width = D // N_CH
    highest = lax.Precision.HIGHEST

    def one_group(group_index):
        first_channel = (group_index * group_width).astype(jnp.int32)
        inputs = lax.dynamic_slice_in_dim(projected, first_channel, group_width, 2)
        taps_here = lax.dynamic_slice_in_dim(tap_weights, first_channel, group_width, 2)
        rates_here = lax.dynamic_slice_in_dim(pole_rates, first_channel, group_width, 1)
        residues_here = lax.dynamic_slice_in_dim(residues, first_channel, group_width, 1)
        bias_here = lax.dynamic_slice_in_dim(long_bias, first_channel, group_width, 0)
        padded = jnp.concatenate([jnp.zeros((3, TAPS - 1, group_width), jnp.bfloat16), inputs], 1)
        featured = jnp.zeros((3, SEQ, group_width), jnp.float32)
        for tap_index in range(TAPS):
            lead_row = TAPS - 1 - tap_index
            featured = featured + taps_here[tap_index].astype(jnp.float32)[:, None, :] * padded[:, lead_row:lead_row + SEQ].astype(jnp.float32)
        mixed_input = (featured[1] * featured[2]).astype(jnp.bfloat16)
        toeplitz, end_weights, read_weights, block_decay = make_tables(rates_here, residues_here, BLOCK)
        blocks = mixed_input.astype(jnp.float32).reshape(SEQ // BLOCK, BLOCK, group_width)

        def advance(state, block_values):
            inner_part = jnp.einsum("ijc,jc->ic", toeplitz, block_values, precision=highest)
            carried = jnp.einsum("ipc,pc->ic", read_weights, state, precision=highest)
            updated = block_decay * state + jnp.einsum("jpc,jc->pc", end_weights, block_values, precision=highest)
            return updated, inner_part + carried

        _, outputs = lax.scan(advance, jnp.zeros((POLES, group_width), jnp.float32), blocks)
        long_mix = outputs.reshape(SEQ, group_width).astype(jnp.bfloat16)
        gated = featured[0] * (long_mix.astype(jnp.float32) + bias_here[None, :] * mixed_input.astype(jnp.float32))
        return gated.astype(jnp.bfloat16)

    groups = lax.map(one_group, jnp.arange(N_CH, dtype=jnp.int32))
    gated_all = jnp.transpose(groups, (1, 0, 2)).reshape(SEQ, D)
    return jnp.dot(gated_all, out_weight, preferred_element_type=jnp.float32).astype(jnp.bfloat16)
```

```python
import jax
import jax.numpy as jnp
from jax import lax
from jax.experimental import pallas as pl
from jax.experimental.pallas import tpu as pltpu
from jax.sharding import PartitionSpec as P

LANES = 128
ROWS_PER_STEP = 128


def shifted(value, axis, steps):
    count = lax.axis_size(axis)
    initial, last = (max(0, -steps), min(count, count - steps))
    return lax.ppermute(value, axis, [(source, source + steps) for source in range(initial, last)])


def recurrence_kernel(x_ref, decay_ref, residue_ref, start_ref, y_ref, end_ref, state_ref):
    pole_count = decay_ref.shape[0]
    step_count = x_ref.shape[0]

    @pl.when(pl.program_id(0) == 0)
    def _():
        state_ref[...] = start_ref[...]

    def body(t, states):
        x = x_ref[t]
        updated = []
        total = None
        for p in range(pole_count):
            h = decay_ref[p] * states[p] + x
            updated.append(h)
            term = residue_ref[p] * h
            total = term if total is None else total + term
        y_ref[t] = total
        return tuple(updated)

    states = tuple(state_ref[p] for p in range(pole_count))
    states = lax.fori_loop(0, step_count, body, states, unroll=4)
    for p in range(pole_count):
        state_ref[p] = states[p]
    end_ref[...] = state_ref[...]


def end_state_kernel(x_ref, decay_ref, end_ref, state_ref):
    pole_count = decay_ref.shape[0]
    step_count = x_ref.shape[0]

    @pl.when(pl.program_id(0) == 0)
    def _():
        state_ref[...] = jnp.zeros(state_ref.shape, state_ref.dtype)

    def body(t, states):
        x = x_ref[t]
        return tuple(decay_ref[p] * states[p] + x for p in range(pole_count))

    states = tuple(state_ref[p] for p in range(pole_count))
    states = lax.fori_loop(0, step_count, body, states, unroll=4)
    for p in range(pole_count):
        state_ref[p] = states[p]
    end_ref[...] = state_ref[...]


def run_recurrence(x3, decay3, residue3, start3):
    length, rows, lanes = x3.shape
    pole_count = decay3.shape[0]
    chunk = min(ROWS_PER_STEP, length)
    row_spec = pl.BlockSpec((chunk, rows, lanes), lambda i: (i, 0, 0))
    pole_spec = pl.BlockSpec((pole_count, rows, lanes), lambda i: (0, 0, 0))
    return pl.pallas_call(
        recurrence_kernel,
        grid=(length // chunk,),
        in_specs=[row_spec, pole_spec, pole_spec, pole_spec],
        out_specs=[row_spec, pole_spec],
        out_shape=[
            jax.ShapeDtypeStruct(x3.shape, jnp.float32),
            jax.ShapeDtypeStruct(decay3.shape, jnp.float32),
        ],
        scratch_shapes=[pltpu.VMEM(decay3.shape, jnp.float32)],
    )(x3, decay3, residue3, start3)


def run_end_state(x3, decay3):
    length, rows, lanes = x3.shape
    pole_count = decay3.shape[0]
    chunk = min(ROWS_PER_STEP, length)
    row_spec = pl.BlockSpec((chunk, rows, lanes), lambda i: (i, 0, 0))
    pole_spec = pl.BlockSpec((pole_count, rows, lanes), lambda i: (0, 0, 0))
    return pl.pallas_call(
        end_state_kernel,
        grid=(length // chunk,),
        in_specs=[row_spec, pole_spec],
        out_specs=pole_spec,
        out_shape=jax.ShapeDtypeStruct(decay3.shape, jnp.float32),
        scratch_shapes=[pltpu.VMEM(decay3.shape, jnp.float32)],
    )(x3, decay3)


def shards(projected, tap_weights, pole_rates, residues, long_bias, out_weight):
    row_count = projected.shape[1]
    width = projected.shape[2]
    rows = width // LANES
    pole_count = pole_rates.shape[0]
    rim_rows = tap_weights.shape[0] - 1
    prior_rows = shifted(projected[:, row_count - rim_rows :], "ctx", 1)
    extended = jnp.concatenate([prior_rows, projected], 1)
    featured = jnp.zeros(projected.shape, jnp.float32)
    for tap_index in range(rim_rows + 1):
        lead_row = rim_rows - tap_index
        featured = featured + tap_weights[tap_index].astype(jnp.float32)[:, None, :] * extended[
            :, lead_row : lead_row + row_count
        ].astype(jnp.float32)
    mixed_input = (featured[1] * featured[2]).astype(jnp.bfloat16)
    x3 = mixed_input.astype(jnp.float32).reshape(row_count, rows, LANES)

    decay = jnp.exp(-pole_rates)
    decay3 = decay.reshape(pole_count, rows, LANES)
    residue3 = residues.reshape(pole_count, rows, LANES)
    local_end = run_end_state(x3, decay3).reshape(pole_count, width)

    ends = lax.all_gather(local_end, "ctx", axis=0, tiled=False)
    ctx_count = ends.shape[0]
    here = lax.axis_index("ctx")
    earlier = jnp.arange(ctx_count, dtype=jnp.int32)
    gaps = (here - 1 - earlier).astype(jnp.float32)
    weights = jnp.where(
        (earlier < here)[:, None, None],
        jnp.exp(-pole_rates[None] * (jnp.float32(row_count) * jnp.maximum(gaps, 0.0))[:, None, None]),
        jnp.float32(0.0),
    )
    start = jnp.sum(weights * ends, axis=0)

    long_part, _ = run_recurrence(x3, decay3, residue3, start.reshape(pole_count, rows, LANES))
    long_mix = long_part.reshape(row_count, width).astype(jnp.bfloat16)
    gated_mix = featured[0] * (
        long_mix.astype(jnp.float32) + long_bias[None, :] * mixed_input.astype(jnp.float32)
    )
    gated_mix = gated_mix.astype(jnp.bfloat16)
    mixed_out = jnp.dot(
        lax.all_gather(gated_mix, "ch", axis=1, tiled=True),
        out_weight,
        preferred_element_type=jnp.float32,
    )
    return mixed_out.astype(jnp.bfloat16)


def solution(mesh):
    in_specs = (
        P(None, "ctx", "ch"),
        P(None, None, "ch"),
        P(None, "ch"),
        P(None, "ch"),
        P("ch"),
        P(None, "ch"),
    )
    out_specs = P("ctx", "ch")
    return jax.shard_map(shards, mesh=mesh, in_specs=in_specs, out_specs=out_specs, check_vma=False)
```

```python
import jax
import jax.numpy as jnp
from jax import lax
from jax.experimental import pallas as pl
from jax.experimental.pallas import tpu as pltpu
from jax.sharding import PartitionSpec as P

LANES = 128
ROWS_PER_STEP = 128
CHUNKS = 4


def shifted(value, axis, steps):
    count = lax.axis_size(axis)
    initial, last = (max(0, -steps), min(count, count - steps))
    return lax.ppermute(value, axis, [(source, source + steps) for source in range(initial, last)])


def recurrence_kernel(x_ref, decay_ref, residue_ref, start_ref, y_ref, end_ref, state_ref):
    pole_count = decay_ref.shape[0]
    step_count = x_ref.shape[0]

    @pl.when(pl.program_id(0) == 0)
    def _():
        state_ref[...] = start_ref[...]

    def body(t, states):
        x = x_ref[t]
        updated = []
        total = None
        for p in range(pole_count):
            h = decay_ref[p] * states[p] + x
            updated.append(h)
            term = residue_ref[p] * h
            total = term if total is None else total + term
        y_ref[t] = total
        return tuple(updated)

    states = tuple(state_ref[p] for p in range(pole_count))
    states = lax.fori_loop(0, step_count, body, states, unroll=4)
    for p in range(pole_count):
        state_ref[p] = states[p]
    end_ref[...] = state_ref[...]


def end_state_kernel(x_ref, decay_ref, end_ref, state_ref):
    pole_count = decay_ref.shape[0]
    step_count = x_ref.shape[0]

    @pl.when(pl.program_id(0) == 0)
    def _():
        state_ref[...] = jnp.zeros(state_ref.shape, state_ref.dtype)

    def body(t, states):
        x = x_ref[t]
        return tuple(decay_ref[p] * states[p] + x for p in range(pole_count))

    states = tuple(state_ref[p] for p in range(pole_count))
    states = lax.fori_loop(0, step_count, body, states, unroll=4)
    for p in range(pole_count):
        state_ref[p] = states[p]
    end_ref[...] = state_ref[...]


def run_recurrence(x3, decay3, residue3, start3):
    length, rows, lanes = x3.shape
    pole_count = decay3.shape[0]
    chunk = min(ROWS_PER_STEP, length)
    row_spec = pl.BlockSpec((chunk, rows, lanes), lambda i: (i, 0, 0))
    pole_spec = pl.BlockSpec((pole_count, rows, lanes), lambda i: (0, 0, 0))
    return pl.pallas_call(
        recurrence_kernel,
        grid=(length // chunk,),
        in_specs=[row_spec, pole_spec, pole_spec, pole_spec],
        out_specs=[row_spec, pole_spec],
        out_shape=[
            jax.ShapeDtypeStruct(x3.shape, jnp.float32),
            jax.ShapeDtypeStruct(decay3.shape, jnp.float32),
        ],
        scratch_shapes=[pltpu.VMEM(decay3.shape, jnp.float32)],
    )(x3, decay3, residue3, start3)


def run_end_state(x3, decay3):
    length, rows, lanes = x3.shape
    pole_count = decay3.shape[0]
    chunk = min(ROWS_PER_STEP, length)
    row_spec = pl.BlockSpec((chunk, rows, lanes), lambda i: (i, 0, 0))
    pole_spec = pl.BlockSpec((pole_count, rows, lanes), lambda i: (0, 0, 0))
    return pl.pallas_call(
        end_state_kernel,
        grid=(length // chunk,),
        in_specs=[row_spec, pole_spec],
        out_specs=pole_spec,
        out_shape=jax.ShapeDtypeStruct(decay3.shape, jnp.float32),
        scratch_shapes=[pltpu.VMEM(decay3.shape, jnp.float32)],
    )(x3, decay3)


def incoming_state(local_end, pole_rates, row_count):
    ctx_count = lax.axis_size("ctx")
    here = lax.axis_index("ctx")
    later = jnp.arange(ctx_count, dtype=jnp.int32)
    gaps = (later - 1 - here).astype(jnp.float32)
    weights = jnp.where(
        (later > here)[:, None, None],
        jnp.exp(-pole_rates[None] * (jnp.float32(row_count) * jnp.maximum(gaps, 0.0))[:, None, None]),
        jnp.float32(0.0),
    )
    shares = weights * local_end[None]
    return lax.psum_scatter(shares, "ctx", scatter_dimension=0, tiled=True)[0]


def featurize(extended, tap_weights, stream, first, count):
    taps = tap_weights.shape[0]
    total = None
    for tap_index in range(taps):
        lead_row = taps - 1 - tap_index
        term = tap_weights[tap_index, stream].astype(jnp.float32)[None, :] * extended[
            stream, first + lead_row : first + lead_row + count
        ].astype(jnp.float32)
        total = term if total is None else total + term
    return total


def shards(projected, tap_weights, pole_rates, residues, long_bias, out_weight):
    row_count = projected.shape[1]
    width = projected.shape[2]
    rows = width // LANES
    pole_count = pole_rates.shape[0]
    rim_rows = tap_weights.shape[0] - 1
    prior_rows = shifted(projected[:, row_count - rim_rows :], "ctx", 1)
    extended = jnp.concatenate([prior_rows, projected], 1)
    mixed_input = (
        featurize(extended, tap_weights, 1, 0, row_count) * featurize(extended, tap_weights, 2, 0, row_count)
    ).astype(jnp.bfloat16)
    x3 = mixed_input.astype(jnp.float32).reshape(row_count, rows, LANES)

    decay = jnp.exp(-pole_rates)
    decay3 = decay.reshape(pole_count, rows, LANES)
    residue3 = residues.reshape(pole_count, rows, LANES)
    local_end = run_end_state(x3, decay3).reshape(pole_count, width)
    state = incoming_state(local_end, pole_rates, row_count).reshape(pole_count, rows, LANES)

    chunk_count = CHUNKS if row_count % (CHUNKS * 8) == 0 else 1
    chunk = row_count // chunk_count
    outputs = []
    for index in range(chunk_count):
        first = index * chunk
        long_part, state = run_recurrence(x3[first : first + chunk], decay3, residue3, state)
        long_mix = long_part.reshape(chunk, width).astype(jnp.bfloat16)
        inputs_here = mixed_input[first : first + chunk].astype(jnp.float32)
        gated_mix = featurize(extended, tap_weights, 0, first, chunk) * (
            long_mix.astype(jnp.float32) + long_bias[None, :] * inputs_here
        )
        gated_mix = gated_mix.astype(jnp.bfloat16)
        mixed_out = jnp.dot(
            lax.all_gather(gated_mix, "ch", axis=1, tiled=True),
            out_weight,
            preferred_element_type=jnp.float32,
        )
        outputs.append(mixed_out.astype(jnp.bfloat16))
    return jnp.concatenate(outputs, 0)


def solution(mesh):
    in_specs = (
        P(None, "ctx", "ch"),
        P(None, None, "ch"),
        P(None, "ch"),
        P(None, "ch"),
        P("ch"),
        P(None, "ch"),
    )
    out_specs = P("ctx", "ch")
    return jax.shard_map(shards, mesh=mesh, in_specs=in_specs, out_specs=out_specs, check_vma=False)
```

```python
import jax
import jax.numpy as jnp
from jax import lax
from jax.experimental import pallas as pl
from jax.experimental.pallas import tpu as pltpu
from jax.sharding import PartitionSpec as P

LANES = 128
ROWS_PER_STEP = 128


def shifted(value, axis, steps):
    count = lax.axis_size(axis)
    initial, last = (max(0, -steps), min(count, count - steps))
    return lax.ppermute(value, axis, [(source, source + steps) for source in range(initial, last)])


def recurrence_kernel(x_ref, decay_ref, residue_ref, start_ref, y_ref, end_ref, state_ref):
    pole_count = decay_ref.shape[0]
    step_count = x_ref.shape[0]

    @pl.when(pl.program_id(0) == 0)
    def _():
        state_ref[...] = start_ref[...]

    def body(t, states):
        x = x_ref[t]
        updated = []
        total = None
        for p in range(pole_count):
            h = decay_ref[p] * states[p] + x
            updated.append(h)
            term = residue_ref[p] * h
            total = term if total is None else total + term
        y_ref[t] = total
        return tuple(updated)

    states = tuple(state_ref[p] for p in range(pole_count))
    states = lax.fori_loop(0, step_count, body, states, unroll=4)
    for p in range(pole_count):
        state_ref[p] = states[p]
    end_ref[...] = state_ref[...]


def end_state_kernel(x_ref, decay_ref, end_ref, state_ref):
    pole_count = decay_ref.shape[0]
    step_count = x_ref.shape[0]

    @pl.when(pl.program_id(0) == 0)
    def _():
        state_ref[...] = jnp.zeros(state_ref.shape, state_ref.dtype)

    def body(t, states):
        x = x_ref[t]
        return tuple(decay_ref[p] * states[p] + x for p in range(pole_count))

    states = tuple(state_ref[p] for p in range(pole_count))
    states = lax.fori_loop(0, step_count, body, states, unroll=4)
    for p in range(pole_count):
        state_ref[p] = states[p]
    end_ref[...] = state_ref[...]


def run_recurrence(x3, decay3, residue3, start3):
    length, rows, lanes = x3.shape
    pole_count = decay3.shape[0]
    chunk = min(ROWS_PER_STEP, length)
    row_spec = pl.BlockSpec((chunk, rows, lanes), lambda i: (i, 0, 0))
    pole_spec = pl.BlockSpec((pole_count, rows, lanes), lambda i: (0, 0, 0))
    return pl.pallas_call(
        recurrence_kernel,
        grid=(length // chunk,),
        in_specs=[row_spec, pole_spec, pole_spec, pole_spec],
        out_specs=[row_spec, pole_spec],
        out_shape=[
            jax.ShapeDtypeStruct(x3.shape, jnp.float32),
            jax.ShapeDtypeStruct(decay3.shape, jnp.float32),
        ],
        scratch_shapes=[pltpu.VMEM(decay3.shape, jnp.float32)],
    )(x3, decay3, residue3, start3)


def run_end_state(x3, decay3):
    length, rows, lanes = x3.shape
    pole_count = decay3.shape[0]
    chunk = min(ROWS_PER_STEP, length)
    row_spec = pl.BlockSpec((chunk, rows, lanes), lambda i: (i, 0, 0))
    pole_spec = pl.BlockSpec((pole_count, rows, lanes), lambda i: (0, 0, 0))
    return pl.pallas_call(
        end_state_kernel,
        grid=(length // chunk,),
        in_specs=[row_spec, pole_spec],
        out_specs=pole_spec,
        out_shape=jax.ShapeDtypeStruct(decay3.shape, jnp.float32),
        scratch_shapes=[pltpu.VMEM(decay3.shape, jnp.float32)],
    )(x3, decay3)


def incoming_state(local_end, pole_rates, row_count):
    ctx_count = lax.axis_size("ctx")
    total = jnp.zeros_like(local_end)
    for distance in range(1, ctx_count):
        received = shifted(local_end, "ctx", distance)
        total = total + jnp.exp(-pole_rates * jnp.float32(row_count * (distance - 1))) * received
    return total


def featurize(extended, tap_weights, stream, count):
    taps = tap_weights.shape[0]
    total = None
    for tap_index in range(taps):
        lead_row = taps - 1 - tap_index
        term = tap_weights[tap_index, stream].astype(jnp.float32)[None, :] * extended[
            stream, lead_row : lead_row + count
        ].astype(jnp.float32)
        total = term if total is None else total + term
    return total


def project(gated_mix, out_weight):
    ch_count = lax.axis_size("ch")
    width = gated_mix.shape[1]
    if ch_count != 4:
        gathered = lax.all_gather(gated_mix, "ch", axis=1, tiled=True)
        return jnp.dot(gathered, out_weight, preferred_element_type=jnp.float32)
    here = lax.axis_index("ch")
    far = lax.ppermute(gated_mix, "ch", [(i, i ^ 2) for i in range(ch_count)])
    near = lax.ppermute(gated_mix, "ch", [(i, i ^ 1) for i in range(ch_count)])
    near_far = lax.ppermute(far, "ch", [(i, i ^ 1) for i in range(ch_count)])
    total = None
    for piece, owner in ((gated_mix, here), (near, here ^ 1), (far, here ^ 2), (near_far, here ^ 3)):
        rows = lax.dynamic_slice_in_dim(out_weight, owner * width, width, 0)
        part = jnp.dot(piece, rows, preferred_element_type=jnp.float32)
        total = part if total is None else total + part
    return total


def shards(projected, tap_weights, pole_rates, residues, long_bias, out_weight):
    row_count = projected.shape[1]
    width = projected.shape[2]
    rows = width // LANES
    pole_count = pole_rates.shape[0]
    rim_rows = tap_weights.shape[0] - 1
    prior_rows = shifted(projected[:, row_count - rim_rows :], "ctx", 1)
    extended = jnp.concatenate([prior_rows, projected], 1)
    mixed_input = (
        featurize(extended, tap_weights, 1, row_count) * featurize(extended, tap_weights, 2, row_count)
    ).astype(jnp.bfloat16)
    x3 = mixed_input.astype(jnp.float32).reshape(row_count, rows, LANES)

    decay = jnp.exp(-pole_rates)
    decay3 = decay.reshape(pole_count, rows, LANES)
    residue3 = residues.reshape(pole_count, rows, LANES)
    local_end = run_end_state(x3, decay3).reshape(pole_count, width)
    start = incoming_state(local_end, pole_rates, row_count)

    long_part, _ = run_recurrence(x3, decay3, residue3, start.reshape(pole_count, rows, LANES))
    long_mix = long_part.reshape(row_count, width).astype(jnp.bfloat16)
    gated_mix = featurize(extended, tap_weights, 0, row_count) * (
        long_mix.astype(jnp.float32) + long_bias[None, :] * mixed_input.astype(jnp.float32)
    )
    gated_mix = gated_mix.astype(jnp.bfloat16)
    return project(gated_mix, out_weight).astype(jnp.bfloat16)


def solution(mesh):
    in_specs = (
        P(None, "ctx", "ch"),
        P(None, None, "ch"),
        P(None, "ch"),
        P(None, "ch"),
        P("ch"),
        P(None, "ch"),
    )
    out_specs = P("ctx", "ch")
    return jax.shard_map(shards, mesh=mesh, in_specs=in_specs, out_specs=out_specs, check_vma=False)
```

```python
import jax
import jax.numpy as jnp
from jax import lax
from jax.experimental import pallas as pl
from jax.experimental.pallas import tpu as pltpu
from jax.sharding import PartitionSpec as P

LANES = 128
SEGMENTS = 8


def shifted(value, axis, steps):
    count = lax.axis_size(axis)
    initial, last = (max(0, -steps), min(count, count - steps))
    return lax.ppermute(value, axis, [(source, source + steps) for source in range(initial, last)])


def segment_pass(x_ref, decay_ref, residue_ref, start_ref, y_ref, end_ref):
    pole_count = decay_ref.shape[0]
    segments = SEGMENTS
    span = x_ref.shape[0] // segments
    lanes = x_ref.shape[1]
    decays = [jnp.broadcast_to(decay_ref[p : p + 1, :], (segments, lanes)) for p in range(pole_count)]
    if residue_ref is not None:
        residues = [jnp.broadcast_to(residue_ref[p : p + 1, :], (segments, lanes)) for p in range(pole_count)]
    if start_ref is None:
        states = tuple(jnp.zeros((segments, lanes), jnp.float32) for _ in range(pole_count))
    else:
        states = tuple(start_ref[p] for p in range(pole_count))

    def body(t, states):
        x = x_ref[pl.ds(t, segments, stride=span), :]
        updated = []
        total = None
        for p in range(pole_count):
            h = decays[p] * states[p] + x
            updated.append(h)
            if y_ref is not None:
                term = residues[p] * h
                total = term if total is None else total + term
        if y_ref is not None:
            y_ref[pl.ds(t, segments, stride=span), :] = total
        return tuple(updated)

    states = lax.fori_loop(0, span, body, states, unroll=4)
    if end_ref is not None:
        for p in range(pole_count):
            end_ref[p] = states[p]


def end_state_kernel(x_ref, decay_ref, end_ref):
    segment_pass(x_ref, decay_ref, None, None, None, end_ref)


def recurrence_kernel(x_ref, decay_ref, residue_ref, start_ref, y_ref):
    segment_pass(x_ref, decay_ref, residue_ref, start_ref, y_ref, None)


def run_end_state(x, decay):
    length, width = x.shape
    pole_count = decay.shape[0]
    return pl.pallas_call(
        end_state_kernel,
        grid=(width // LANES,),
        in_specs=[
            pl.BlockSpec((length, LANES), lambda g: (0, g)),
            pl.BlockSpec((pole_count, LANES), lambda g: (0, g)),
        ],
        out_specs=pl.BlockSpec((pole_count, SEGMENTS, LANES), lambda g: (0, 0, g)),
        out_shape=jax.ShapeDtypeStruct((pole_count, SEGMENTS, width), jnp.float32),
    )(x, decay)


def run_recurrence(x, decay, residue, start):
    length, width = x.shape
    pole_count = decay.shape[0]
    pole_spec = pl.BlockSpec((pole_count, LANES), lambda g: (0, g))
    return pl.pallas_call(
        recurrence_kernel,
        grid=(width // LANES,),
        in_specs=[
            pl.BlockSpec((length, LANES), lambda g: (0, g)),
            pole_spec,
            pole_spec,
            pl.BlockSpec((pole_count, SEGMENTS, LANES), lambda g: (0, 0, g)),
        ],
        out_specs=pl.BlockSpec((length, LANES), lambda g: (0, g)),
        out_shape=jax.ShapeDtypeStruct(x.shape, jnp.float32),
    )(x, decay, residue, start)


def segment_starts(ends, incoming, pole_rates, span):
    segments = ends.shape[1]
    index = jnp.arange(segments, dtype=jnp.int32)
    gaps = (index[:, None] - 1 - index[None, :]).astype(jnp.float32)
    weights = jnp.where(
        (index[None, :] < index[:, None])[:, :, None, None],
        jnp.exp(-pole_rates[None, None] * (jnp.float32(span) * jnp.maximum(gaps, 0.0))[:, :, None, None]),
        jnp.float32(0.0),
    )
    carried = jnp.einsum("abpc,pbc->pac", weights, ends, precision=lax.Precision.HIGHEST)
    lead = jnp.exp(-pole_rates[:, None, :] * (jnp.float32(span) * index.astype(jnp.float32))[None, :, None])
    return carried + lead * incoming[:, None, :]


def device_end(ends, pole_rates, span):
    segments = ends.shape[1]
    index = jnp.arange(segments, dtype=jnp.float32)
    weights = jnp.exp(-pole_rates[:, None, :] * (jnp.float32(span) * (segments - 1 - index))[None, :, None])
    return jnp.sum(weights * ends, axis=1)


def incoming_state(local_end, pole_rates, row_count):
    ctx_count = lax.axis_size("ctx")
    total = jnp.zeros_like(local_end)
    for distance in range(1, ctx_count):
        received = shifted(local_end, "ctx", distance)
        total = total + jnp.exp(-pole_rates * jnp.float32(row_count * (distance - 1))) * received
    return total


def featurize(extended, tap_weights, stream, count):
    taps = tap_weights.shape[0]
    total = None
    for tap_index in range(taps):
        lead_row = taps - 1 - tap_index
        term = tap_weights[tap_index, stream].astype(jnp.float32)[None, :] * extended[
            stream, lead_row : lead_row + count
        ].astype(jnp.float32)
        total = term if total is None else total + term
    return total


def project(gated_mix, out_weight):
    ch_count = lax.axis_size("ch")
    width = gated_mix.shape[1]
    if ch_count != 4:
        gathered = lax.all_gather(gated_mix, "ch", axis=1, tiled=True)
        return jnp.dot(gathered, out_weight, preferred_element_type=jnp.float32)
    here = lax.axis_index("ch")
    far = lax.ppermute(gated_mix, "ch", [(i, i ^ 2) for i in range(ch_count)])
    near = lax.ppermute(gated_mix, "ch", [(i, i ^ 1) for i in range(ch_count)])
    near_far = lax.ppermute(far, "ch", [(i, i ^ 1) for i in range(ch_count)])
    total = None
    for piece, owner in ((gated_mix, here), (near, here ^ 1), (far, here ^ 2), (near_far, here ^ 3)):
        rows = lax.dynamic_slice_in_dim(out_weight, owner * width, width, 0)
        part = jnp.dot(piece, rows, preferred_element_type=jnp.float32)
        total = part if total is None else total + part
    return total


def shards(projected, tap_weights, pole_rates, residues, long_bias, out_weight):
    row_count = projected.shape[1]
    width = projected.shape[2]
    rows = width // LANES
    pole_count = pole_rates.shape[0]
    rim_rows = tap_weights.shape[0] - 1
    prior_rows = shifted(projected[:, row_count - rim_rows :], "ctx", 1)
    extended = jnp.concatenate([prior_rows, projected], 1)
    mixed_input = (
        featurize(extended, tap_weights, 1, row_count) * featurize(extended, tap_weights, 2, row_count)
    ).astype(jnp.bfloat16)
    x = mixed_input.astype(jnp.float32)
    span = row_count // SEGMENTS

    decay = jnp.exp(-pole_rates)
    ends = run_end_state(x, decay)
    start = incoming_state(device_end(ends, pole_rates, span), pole_rates, row_count)
    long_part = run_recurrence(x, decay, residues, segment_starts(ends, start, pole_rates, span))
    long_mix = long_part.astype(jnp.bfloat16)
    gated_mix = featurize(extended, tap_weights, 0, row_count) * (
        long_mix.astype(jnp.float32) + long_bias[None, :] * mixed_input.astype(jnp.float32)
    )
    gated_mix = gated_mix.astype(jnp.bfloat16)
    return project(gated_mix, out_weight).astype(jnp.bfloat16)


def solution(mesh):
    in_specs = (
        P(None, "ctx", "ch"),
        P(None, None, "ch"),
        P(None, "ch"),
        P(None, "ch"),
        P("ch"),
        P(None, "ch"),
    )
    out_specs = P("ctx", "ch")
    return jax.shard_map(shards, mesh=mesh, in_specs=in_specs, out_specs=out_specs, check_vma=False)
```

```python
import jax
import jax.numpy as jnp
from jax import lax
from jax.experimental import pallas as pl
from jax.experimental.pallas import tpu as pltpu
from jax.sharding import PartitionSpec as P

LANES = 128
SEGMENTS = 8


def shifted(value, axis, steps):
    count = lax.axis_size(axis)
    initial, last = (max(0, -steps), min(count, count - steps))
    return lax.ppermute(value, axis, [(source, source + steps) for source in range(initial, last)])


def segment_pass(x_ref, decay_ref, residue_ref, start_ref, y_ref, end_ref):
    pole_count = decay_ref.shape[0]
    segments = SEGMENTS
    span = x_ref.shape[0] // segments
    lanes = x_ref.shape[1]
    decays = [jnp.broadcast_to(decay_ref[p : p + 1, :], (segments, lanes)) for p in range(pole_count)]
    if residue_ref is not None:
        residues = [jnp.broadcast_to(residue_ref[p : p + 1, :], (segments, lanes)) for p in range(pole_count)]
    if start_ref is None:
        states = tuple(jnp.zeros((segments, lanes), jnp.float32) for _ in range(pole_count))
    else:
        states = tuple(start_ref[p] for p in range(pole_count))

    def body(t, states):
        x = x_ref[pl.ds(t, segments, stride=span), :]
        updated = []
        total = None
        for p in range(pole_count):
            h = decays[p] * states[p] + x
            updated.append(h)
            if y_ref is not None:
                term = residues[p] * h
                total = term if total is None else total + term
        if y_ref is not None:
            y_ref[pl.ds(t, segments, stride=span), :] = total
        return tuple(updated)

    states = lax.fori_loop(0, span, body, states, unroll=4)
    if end_ref is not None:
        for p in range(pole_count):
            end_ref[p] = states[p]


def end_state_kernel(x_ref, decay_ref, end_ref):
    segment_pass(x_ref, decay_ref, None, None, None, end_ref)


def recurrence_kernel(x_ref, decay_ref, residue_ref, start_ref, y_ref):
    segment_pass(x_ref, decay_ref, residue_ref, start_ref, y_ref, None)


def run_end_state(x, decay):
    length, width = x.shape
    pole_count = decay.shape[0]
    return pl.pallas_call(
        end_state_kernel,
        grid=(width // LANES,),
        in_specs=[
            pl.BlockSpec((length, LANES), lambda g: (0, g)),
            pl.BlockSpec((pole_count, LANES), lambda g: (0, g)),
        ],
        out_specs=pl.BlockSpec((pole_count, SEGMENTS, LANES), lambda g: (0, 0, g)),
        out_shape=jax.ShapeDtypeStruct((pole_count, SEGMENTS, width), jnp.float32),
    )(x, decay)


def run_recurrence(x, decay, residue, start):
    length, width = x.shape
    pole_count = decay.shape[0]
    pole_spec = pl.BlockSpec((pole_count, LANES), lambda g: (0, g))
    return pl.pallas_call(
        recurrence_kernel,
        grid=(width // LANES,),
        in_specs=[
            pl.BlockSpec((length, LANES), lambda g: (0, g)),
            pole_spec,
            pole_spec,
            pl.BlockSpec((pole_count, SEGMENTS, LANES), lambda g: (0, 0, g)),
        ],
        out_specs=pl.BlockSpec((length, LANES), lambda g: (0, g)),
        out_shape=jax.ShapeDtypeStruct(x.shape, jnp.float32),
    )(x, decay, residue, start)


def segment_starts(ends, incoming, pole_rates, span):
    segments = ends.shape[1]
    index = jnp.arange(segments, dtype=jnp.int32)
    gaps = (index[:, None] - 1 - index[None, :]).astype(jnp.float32)
    weights = jnp.where(
        (index[None, :] < index[:, None])[:, :, None, None],
        jnp.exp(-pole_rates[None, None] * (jnp.float32(span) * jnp.maximum(gaps, 0.0))[:, :, None, None]),
        jnp.float32(0.0),
    )
    carried = jnp.einsum("abpc,pbc->pac", weights, ends, precision=lax.Precision.HIGHEST)
    lead = jnp.exp(-pole_rates[:, None, :] * (jnp.float32(span) * index.astype(jnp.float32))[None, :, None])
    return carried + lead * incoming[:, None, :]


def device_end(ends, pole_rates, span):
    segments = ends.shape[1]
    index = jnp.arange(segments, dtype=jnp.float32)
    weights = jnp.exp(-pole_rates[:, None, :] * (jnp.float32(span) * (segments - 1 - index))[None, :, None])
    return jnp.sum(weights * ends, axis=1)


def incoming_state(local_end, pole_rates, row_count):
    ctx_count = lax.axis_size("ctx")
    total = jnp.zeros_like(local_end)
    for distance in range(1, ctx_count):
        received = shifted(local_end, "ctx", distance)
        total = total + jnp.exp(-pole_rates * jnp.float32(row_count * (distance - 1))) * received
    return total


def featurize(extended, tap_weights, stream, count):
    taps = tap_weights.shape[0]
    total = None
    for tap_index in range(taps):
        lead_row = taps - 1 - tap_index
        term = tap_weights[tap_index, stream].astype(jnp.float32)[None, :] * extended[
            stream, lead_row : lead_row + count
        ].astype(jnp.float32)
        total = term if total is None else total + term
    return total


def project(gated_mix, out_weight):
    ch_count = lax.axis_size("ch")
    width = gated_mix.shape[1]
    if ch_count != 4:
        gathered = lax.all_gather(gated_mix, "ch", axis=1, tiled=True)
        return jnp.dot(gathered, out_weight, preferred_element_type=jnp.float32)
    here = lax.axis_index("ch")

    def part(piece, owner):
        rows = lax.dynamic_slice_in_dim(out_weight, owner * width, width, 0)
        return jnp.dot(piece, rows, preferred_element_type=jnp.float32)

    far = lax.ppermute(gated_mix, "ch", [(i, i ^ 2) for i in range(ch_count)])
    near = lax.ppermute(gated_mix, "ch", [(i, i ^ 1) for i in range(ch_count)])
    total = part(gated_mix, here) + part(near, here ^ 1)
    far, total = lax.optimization_barrier((far, total))
    near_far = lax.ppermute(far, "ch", [(i, i ^ 1) for i in range(ch_count)])
    total = total + part(far, here ^ 2)
    return total + part(near_far, here ^ 3)


def shards(projected, tap_weights, pole_rates, residues, long_bias, out_weight):
    row_count = projected.shape[1]
    width = projected.shape[2]
    rows = width // LANES
    pole_count = pole_rates.shape[0]
    rim_rows = tap_weights.shape[0] - 1
    prior_rows = shifted(projected[:, row_count - rim_rows :], "ctx", 1)
    extended = jnp.concatenate([prior_rows, projected], 1)
    mixed_input = (
        featurize(extended, tap_weights, 1, row_count) * featurize(extended, tap_weights, 2, row_count)
    ).astype(jnp.bfloat16)
    x = mixed_input.astype(jnp.float32)
    span = row_count // SEGMENTS

    decay = jnp.exp(-pole_rates)
    ends = run_end_state(x, decay)
    start = incoming_state(device_end(ends, pole_rates, span), pole_rates, row_count)
    long_part = run_recurrence(x, decay, residues, segment_starts(ends, start, pole_rates, span))
    long_mix = long_part.astype(jnp.bfloat16)
    gated_mix = featurize(extended, tap_weights, 0, row_count) * (
        long_mix.astype(jnp.float32) + long_bias[None, :] * mixed_input.astype(jnp.float32)
    )
    gated_mix = gated_mix.astype(jnp.bfloat16)
    return project(gated_mix, out_weight).astype(jnp.bfloat16)


def solution(mesh):
    in_specs = (
        P(None, "ctx", "ch"),
        P(None, None, "ch"),
        P(None, "ch"),
        P(None, "ch"),
        P("ch"),
        P(None, "ch"),
    )
    out_specs = P("ctx", "ch")
    return jax.shard_map(shards, mesh=mesh, in_specs=in_specs, out_specs=out_specs, check_vma=False)
```

```python
import jax
import jax.numpy as jnp
from jax import lax
from jax.experimental import pallas as pl
from jax.experimental.pallas import tpu as pltpu
from jax.sharding import PartitionSpec as P

LANES = 128
SEGMENTS = 8
CHANNEL_PIECES = 4
LAG = 2


def shifted(value, axis, steps):
    count = lax.axis_size(axis)
    initial, last = (max(0, -steps), min(count, count - steps))
    return lax.ppermute(value, axis, [(source, source + steps) for source in range(initial, last)])


def segment_pass(x_ref, decay_ref, residue_ref, start_ref, y_ref, end_ref):
    pole_count = decay_ref.shape[0]
    segments = SEGMENTS
    span = x_ref.shape[0] // segments
    lanes = x_ref.shape[1]
    decays = [jnp.broadcast_to(decay_ref[p : p + 1, :], (segments, lanes)) for p in range(pole_count)]
    if residue_ref is not None:
        residues = [jnp.broadcast_to(residue_ref[p : p + 1, :], (segments, lanes)) for p in range(pole_count)]
    if start_ref is None:
        states = tuple(jnp.zeros((segments, lanes), jnp.float32) for _ in range(pole_count))
    else:
        states = tuple(start_ref[p] for p in range(pole_count))

    def body(t, states):
        x = x_ref[pl.ds(t, segments, stride=span), :]
        updated = []
        total = None
        for p in range(pole_count):
            h = decays[p] * states[p] + x
            updated.append(h)
            if y_ref is not None:
                term = residues[p] * h
                total = term if total is None else total + term
        if y_ref is not None:
            y_ref[pl.ds(t, segments, stride=span), :] = total
        return tuple(updated)

    states = lax.fori_loop(0, span, body, states, unroll=4)
    if end_ref is not None:
        for p in range(pole_count):
            end_ref[p] = states[p]


def end_state_kernel(x_ref, decay_ref, end_ref):
    segment_pass(x_ref, decay_ref, None, None, None, end_ref)


def recurrence_kernel(x_ref, decay_ref, residue_ref, start_ref, y_ref):
    segment_pass(x_ref, decay_ref, residue_ref, start_ref, y_ref, None)


def run_end_state(x, decay):
    length, width = x.shape
    pole_count = decay.shape[0]
    return pl.pallas_call(
        end_state_kernel,
        grid=(width // LANES,),
        in_specs=[
            pl.BlockSpec((length, LANES), lambda g: (0, g)),
            pl.BlockSpec((pole_count, LANES), lambda g: (0, g)),
        ],
        out_specs=pl.BlockSpec((pole_count, SEGMENTS, LANES), lambda g: (0, 0, g)),
        out_shape=jax.ShapeDtypeStruct((pole_count, SEGMENTS, width), jnp.float32),
        cost_estimate=pl.CostEstimate(
            flops=2 * pole_count * length * width, transcendentals=0, bytes_accessed=4 * length * width
        ),
    )(x, decay)


def run_recurrence(x, decay, residue, start):
    length, width = x.shape
    pole_count = decay.shape[0]
    pole_spec = pl.BlockSpec((pole_count, LANES), lambda g: (0, g))
    return pl.pallas_call(
        recurrence_kernel,
        grid=(width // LANES,),
        in_specs=[
            pl.BlockSpec((length, LANES), lambda g: (0, g)),
            pole_spec,
            pole_spec,
            pl.BlockSpec((pole_count, SEGMENTS, LANES), lambda g: (0, 0, g)),
        ],
        out_specs=pl.BlockSpec((length, LANES), lambda g: (0, g)),
        out_shape=jax.ShapeDtypeStruct(x.shape, jnp.float32),
        cost_estimate=pl.CostEstimate(
            flops=4 * pole_count * length * width, transcendentals=0, bytes_accessed=8 * length * width
        ),
    )(x, decay, residue, start)


def segment_starts(ends, incoming, pole_rates, span):
    segments = ends.shape[1]
    index = jnp.arange(segments, dtype=jnp.int32)
    gaps = (index[:, None] - 1 - index[None, :]).astype(jnp.float32)
    weights = jnp.where(
        (index[None, :] < index[:, None])[:, :, None, None],
        jnp.exp(-pole_rates[None, None] * (jnp.float32(span) * jnp.maximum(gaps, 0.0))[:, :, None, None]),
        jnp.float32(0.0),
    )
    carried = jnp.einsum("abpc,pbc->pac", weights, ends, precision=lax.Precision.HIGHEST)
    lead = jnp.exp(-pole_rates[:, None, :] * (jnp.float32(span) * index.astype(jnp.float32))[None, :, None])
    return carried + lead * incoming[:, None, :]


def device_end(ends, pole_rates, span):
    segments = ends.shape[1]
    index = jnp.arange(segments, dtype=jnp.float32)
    weights = jnp.exp(-pole_rates[:, None, :] * (jnp.float32(span) * (segments - 1 - index))[None, :, None])
    return jnp.sum(weights * ends, axis=1)


def incoming_state(local_end, pole_rates, row_count):
    ctx_count = lax.axis_size("ctx")
    total = jnp.zeros_like(local_end)
    for distance in range(1, ctx_count):
        received = shifted(local_end, "ctx", distance)
        total = total + jnp.exp(-pole_rates * jnp.float32(row_count * (distance - 1))) * received
    return total


def featurize(extended, tap_weights, stream, count):
    taps = tap_weights.shape[0]
    total = None
    for tap_index in range(taps):
        lead_row = taps - 1 - tap_index
        term = tap_weights[tap_index, stream].astype(jnp.float32)[None, :] * extended[
            stream, lead_row : lead_row + count
        ].astype(jnp.float32)
        total = term if total is None else total + term
    return total


def project_whole(gated_mix, out_weight):
    gathered = lax.all_gather(gated_mix, "ch", axis=1, tiled=True)
    return jnp.dot(gathered, out_weight, preferred_element_type=jnp.float32)


def weight_rows(out_weight, owners, width):
    return jnp.concatenate([lax.dynamic_slice_in_dim(out_weight, owner * width, width, 0) for owner in owners], 0)


def shards(projected, tap_weights, pole_rates, residues, long_bias, out_weight):
    row_count = projected.shape[1]
    width = projected.shape[2]
    rim_rows = tap_weights.shape[0] - 1
    prior_rows = shifted(projected[:, row_count - rim_rows :], "ctx", 1)
    extended = jnp.concatenate([prior_rows, projected], 1)
    mixed_input = (
        featurize(extended, tap_weights, 1, row_count) * featurize(extended, tap_weights, 2, row_count)
    ).astype(jnp.bfloat16)
    x = mixed_input.astype(jnp.float32)
    span = row_count // SEGMENTS

    decay = jnp.exp(-pole_rates)
    ends = run_end_state(x, decay)
    start = incoming_state(device_end(ends, pole_rates, span), pole_rates, row_count)
    starts = segment_starts(ends, start, pole_rates, span)
    stream0 = featurize(extended, tap_weights, 0, row_count)

    ch_count = lax.axis_size("ch")
    pieces = CHANNEL_PIECES if (ch_count == 4 and width % (CHANNEL_PIECES * LANES) == 0) else 1
    piece = width // pieces
    here = lax.axis_index("ch")
    other_core = [(i, i ^ 1) for i in range(ch_count)]
    other_chip = [(i, i ^ 2) for i in range(ch_count)]
    gated = []
    far = []
    for index in range(pieces):
        cols = slice(index * piece, (index + 1) * piece)
        x_here = x[:, cols]
        if index >= LAG and pieces > 1:
            x_here, far[index - LAG] = lax.optimization_barrier((x_here, far[index - LAG]))
        long_part = run_recurrence(x_here, decay[:, cols], residues[:, cols], starts[:, :, cols])
        long_mix = long_part.astype(jnp.bfloat16)
        gated_mix = stream0[:, cols] * (
            long_mix.astype(jnp.float32) + long_bias[None, cols] * mixed_input[:, cols].astype(jnp.float32)
        )
        gated_mix = gated_mix.astype(jnp.bfloat16)
        gated.append(gated_mix)
        if ch_count == 4:
            far.append(lax.ppermute(gated_mix, "ch", other_chip))
    if ch_count != 4:
        return project_whole(jnp.concatenate(gated, 1), out_weight).astype(jnp.bfloat16)

    own = jnp.concatenate(gated, 1)
    near = lax.ppermute(own, "ch", other_core)
    local_rows = weight_rows(out_weight, (here, here ^ 1), width)
    remote_rows = weight_rows(out_weight, (here ^ 2, here ^ 3), width)
    total = jnp.dot(jnp.concatenate([own, near], 1), local_rows, preferred_element_type=jnp.float32)
    far, total = lax.optimization_barrier((far, total))
    far = jnp.concatenate(far, 1)
    near_far = lax.ppermute(far, "ch", other_core)
    total = total + jnp.dot(jnp.concatenate([far, near_far], 1), remote_rows, preferred_element_type=jnp.float32)
    return total.astype(jnp.bfloat16)


def solution(mesh):
    in_specs = (
        P(None, "ctx", "ch"),
        P(None, None, "ch"),
        P(None, "ch"),
        P(None, "ch"),
        P("ch"),
        P(None, "ch"),
    )
    out_specs = P("ctx", "ch")
    return jax.shard_map(shards, mesh=mesh, in_specs=in_specs, out_specs=out_specs, check_vma=False)
```

```python
import jax
import jax.numpy as jnp
from jax import lax
from jax.experimental import pallas as pl
from jax.experimental.pallas import tpu as pltpu
from jax.sharding import PartitionSpec as P

LANES = 128
SEGMENTS = 8


def shifted(value, axis, steps):
    count = lax.axis_size(axis)
    initial, last = (max(0, -steps), min(count, count - steps))
    return lax.ppermute(value, axis, [(source, source + steps) for source in range(initial, last)])


def segment_pass(x_ref, decay_ref, residue_ref, start_ref, y_ref, end_ref):
    pole_count = decay_ref.shape[0]
    segments = SEGMENTS
    span = x_ref.shape[0] // segments
    lanes = x_ref.shape[1]
    decays = [jnp.broadcast_to(decay_ref[p : p + 1, :], (segments, lanes)) for p in range(pole_count)]
    if residue_ref is not None:
        residues = [jnp.broadcast_to(residue_ref[p : p + 1, :], (segments, lanes)) for p in range(pole_count)]
    if start_ref is None:
        states = tuple(jnp.zeros((segments, lanes), jnp.float32) for _ in range(pole_count))
    else:
        states = tuple(start_ref[p] for p in range(pole_count))

    def body(t, states):
        x = x_ref[pl.ds(t, segments, stride=span), :]
        updated = []
        total = None
        for p in range(pole_count):
            h = decays[p] * states[p] + x
            updated.append(h)
            if y_ref is not None:
                term = residues[p] * h
                total = term if total is None else total + term
        if y_ref is not None:
            y_ref[pl.ds(t, segments, stride=span), :] = total
        return tuple(updated)

    states = lax.fori_loop(0, span, body, states, unroll=4)
    if end_ref is not None:
        for p in range(pole_count):
            end_ref[p] = states[p]


def end_state_kernel(x_ref, decay_ref, end_ref):
    segment_pass(x_ref, decay_ref, None, None, None, end_ref)


def recurrence_kernel(x_ref, decay_ref, residue_ref, start_ref, y_ref):
    segment_pass(x_ref, decay_ref, residue_ref, start_ref, y_ref, None)


def run_end_state(x, decay):
    length, width = x.shape
    pole_count = decay.shape[0]
    return pl.pallas_call(
        end_state_kernel,
        grid=(width // LANES,),
        in_specs=[
            pl.BlockSpec((length, LANES), lambda g: (0, g)),
            pl.BlockSpec((pole_count, LANES), lambda g: (0, g)),
        ],
        out_specs=pl.BlockSpec((pole_count, SEGMENTS, LANES), lambda g: (0, 0, g)),
        out_shape=jax.ShapeDtypeStruct((pole_count, SEGMENTS, width), jnp.float32),
    )(x, decay)


def run_recurrence(x, decay, residue, start):
    length, width = x.shape
    pole_count = decay.shape[0]
    pole_spec = pl.BlockSpec((pole_count, LANES), lambda g: (0, g))
    return pl.pallas_call(
        recurrence_kernel,
        grid=(width // LANES,),
        in_specs=[
            pl.BlockSpec((length, LANES), lambda g: (0, g)),
            pole_spec,
            pole_spec,
            pl.BlockSpec((pole_count, SEGMENTS, LANES), lambda g: (0, 0, g)),
        ],
        out_specs=pl.BlockSpec((length, LANES), lambda g: (0, g)),
        out_shape=jax.ShapeDtypeStruct(x.shape, jnp.float32),
    )(x, decay, residue, start)


def segment_starts(ends, incoming, pole_rates, span):
    segments = ends.shape[1]
    index = jnp.arange(segments, dtype=jnp.int32)
    gaps = (index[:, None] - 1 - index[None, :]).astype(jnp.float32)
    weights = jnp.where(
        (index[None, :] < index[:, None])[:, :, None, None],
        jnp.exp(-pole_rates[None, None] * (jnp.float32(span) * jnp.maximum(gaps, 0.0))[:, :, None, None]),
        jnp.float32(0.0),
    )
    carried = jnp.einsum("abpc,pbc->pac", weights, ends, precision=lax.Precision.HIGHEST)
    lead = jnp.exp(-pole_rates[:, None, :] * (jnp.float32(span) * index.astype(jnp.float32))[None, :, None])
    return carried + lead * incoming[:, None, :]


def device_end(ends, pole_rates, span):
    segments = ends.shape[1]
    index = jnp.arange(segments, dtype=jnp.float32)
    weights = jnp.exp(-pole_rates[:, None, :] * (jnp.float32(span) * (segments - 1 - index))[None, :, None])
    return jnp.sum(weights * ends, axis=1)


def incoming_state(local_end, pole_rates, row_count):
    ctx_count = lax.axis_size("ctx")
    width = local_end.shape[1]
    ends = lax.all_gather(local_end, "ctx", axis=1, tiled=True).reshape(local_end.shape[0], ctx_count, width)
    here = lax.axis_index("ctx")
    earlier = jnp.arange(ctx_count, dtype=jnp.int32)
    gaps = (here - 1 - earlier).astype(jnp.float32)
    weights = jnp.where(
        (earlier < here)[None, :, None],
        jnp.exp(-pole_rates[:, None, :] * (jnp.float32(row_count) * jnp.maximum(gaps, 0.0))[None, :, None]),
        jnp.float32(0.0),
    )
    return jnp.sum(weights * ends, axis=1)


def featurize(extended, tap_weights, stream, count):
    taps = tap_weights.shape[0]
    total = None
    for tap_index in range(taps):
        lead_row = taps - 1 - tap_index
        term = tap_weights[tap_index, stream].astype(jnp.float32)[None, :] * extended[
            stream, lead_row : lead_row + count
        ].astype(jnp.float32)
        total = term if total is None else total + term
    return total


def project(gated_mix, out_weight):
    ch_count = lax.axis_size("ch")
    width = gated_mix.shape[1]
    if ch_count != 4:
        gathered = lax.all_gather(gated_mix, "ch", axis=1, tiled=True)
        return jnp.dot(gathered, out_weight, preferred_element_type=jnp.float32)
    here = lax.axis_index("ch")

    def part(piece, owner):
        rows = lax.dynamic_slice_in_dim(out_weight, owner * width, width, 0)
        return jnp.dot(piece, rows, preferred_element_type=jnp.float32)

    far = lax.ppermute(gated_mix, "ch", [(i, i ^ 2) for i in range(ch_count)])
    near = lax.ppermute(gated_mix, "ch", [(i, i ^ 1) for i in range(ch_count)])
    total = part(gated_mix, here) + part(near, here ^ 1)
    far, total = lax.optimization_barrier((far, total))
    near_far = lax.ppermute(far, "ch", [(i, i ^ 1) for i in range(ch_count)])
    total = total + part(far, here ^ 2)
    return total + part(near_far, here ^ 3)


def shards(projected, tap_weights, pole_rates, residues, long_bias, out_weight):
    row_count = projected.shape[1]
    width = projected.shape[2]
    rows = width // LANES
    pole_count = pole_rates.shape[0]
    rim_rows = tap_weights.shape[0] - 1
    prior_rows = shifted(projected[:, row_count - rim_rows :], "ctx", 1)
    extended = jnp.concatenate([prior_rows, projected], 1)
    mixed_input = (
        featurize(extended, tap_weights, 1, row_count) * featurize(extended, tap_weights, 2, row_count)
    ).astype(jnp.bfloat16)
    x = mixed_input.astype(jnp.float32)
    span = row_count // SEGMENTS

    decay = jnp.exp(-pole_rates)
    ends = run_end_state(x, decay)
    start = incoming_state(device_end(ends, pole_rates, span), pole_rates, row_count)
    long_part = run_recurrence(x, decay, residues, segment_starts(ends, start, pole_rates, span))
    long_mix = long_part.astype(jnp.bfloat16)
    gated_mix = featurize(extended, tap_weights, 0, row_count) * (
        long_mix.astype(jnp.float32) + long_bias[None, :] * mixed_input.astype(jnp.float32)
    )
    gated_mix = gated_mix.astype(jnp.bfloat16)
    return project(gated_mix, out_weight).astype(jnp.bfloat16)


def solution(mesh):
    in_specs = (
        P(None, "ctx", "ch"),
        P(None, None, "ch"),
        P(None, "ch"),
        P(None, "ch"),
        P("ch"),
        P(None, "ch"),
    )
    out_specs = P("ctx", "ch")
    return jax.shard_map(shards, mesh=mesh, in_specs=in_specs, out_specs=out_specs, check_vma=False)
```

```python
import jax
import jax.numpy as jnp
from jax import lax
from jax.experimental import pallas as pl
from jax.experimental.pallas import tpu as pltpu
from jax.sharding import PartitionSpec as P

LANES = 128
SEGMENTS = 8


def shifted(value, axis, steps):
    count = lax.axis_size(axis)
    initial, last = (max(0, -steps), min(count, count - steps))
    return lax.ppermute(value, axis, [(source, source + steps) for source in range(initial, last)])


def segment_pass(x_ref, decay_ref, residue_ref, start_ref, y_ref, end_ref):
    pole_count = decay_ref.shape[0]
    segments = SEGMENTS
    span = x_ref.shape[0] // segments
    lanes = x_ref.shape[1]
    decays = [jnp.broadcast_to(decay_ref[p : p + 1, :], (segments, lanes)) for p in range(pole_count)]
    if residue_ref is not None:
        residues = [jnp.broadcast_to(residue_ref[p : p + 1, :], (segments, lanes)) for p in range(pole_count)]
    if start_ref is None:
        states = tuple(jnp.zeros((segments, lanes), jnp.float32) for _ in range(pole_count))
    else:
        states = tuple(start_ref[p] for p in range(pole_count))

    def body(t, states):
        x = x_ref[pl.ds(t, segments, stride=span), :]
        updated = []
        total = None
        for p in range(pole_count):
            h = decays[p] * states[p] + x
            updated.append(h)
            if y_ref is not None:
                term = residues[p] * h
                total = term if total is None else total + term
        if y_ref is not None:
            y_ref[pl.ds(t, segments, stride=span), :] = total
        return tuple(updated)

    states = lax.fori_loop(0, span, body, states, unroll=4)
    if end_ref is not None:
        for p in range(pole_count):
            end_ref[p] = states[p]


def end_state_kernel(x_ref, decay_ref, end_ref):
    segment_pass(x_ref, decay_ref, None, None, None, end_ref)


def recurrence_kernel(x_ref, decay_ref, residue_ref, start_ref, y_ref):
    segment_pass(x_ref, decay_ref, residue_ref, start_ref, y_ref, None)


def run_end_state(x, decay):
    length, width = x.shape
    pole_count = decay.shape[0]
    return pl.pallas_call(
        end_state_kernel,
        grid=(width // LANES,),
        in_specs=[
            pl.BlockSpec((length, LANES), lambda g: (0, g)),
            pl.BlockSpec((pole_count, LANES), lambda g: (0, g)),
        ],
        out_specs=pl.BlockSpec((pole_count, SEGMENTS, LANES), lambda g: (0, 0, g)),
        out_shape=jax.ShapeDtypeStruct((pole_count, SEGMENTS, width), jnp.float32),
    )(x, decay)


def run_recurrence(x, decay, residue, start):
    length, width = x.shape
    pole_count = decay.shape[0]
    pole_spec = pl.BlockSpec((pole_count, LANES), lambda g: (0, g))
    return pl.pallas_call(
        recurrence_kernel,
        grid=(width // LANES,),
        in_specs=[
            pl.BlockSpec((length, LANES), lambda g: (0, g)),
            pole_spec,
            pole_spec,
            pl.BlockSpec((pole_count, SEGMENTS, LANES), lambda g: (0, 0, g)),
        ],
        out_specs=pl.BlockSpec((length, LANES), lambda g: (0, g)),
        out_shape=jax.ShapeDtypeStruct(x.shape, jnp.float32),
    )(x, decay, residue, start)


def segment_starts(ends, incoming, pole_rates, span):
    segments = ends.shape[1]
    index = jnp.arange(segments, dtype=jnp.int32)
    gaps = (index[:, None] - 1 - index[None, :]).astype(jnp.float32)
    weights = jnp.where(
        (index[None, :] < index[:, None])[:, :, None, None],
        jnp.exp(-pole_rates[None, None] * (jnp.float32(span) * jnp.maximum(gaps, 0.0))[:, :, None, None]),
        jnp.float32(0.0),
    )
    carried = jnp.einsum("abpc,pbc->pac", weights, ends, precision=lax.Precision.HIGHEST)
    lead = jnp.exp(-pole_rates[:, None, :] * (jnp.float32(span) * index.astype(jnp.float32))[None, :, None])
    return carried + lead * incoming[:, None, :]


def device_end(ends, pole_rates, span):
    segments = ends.shape[1]
    index = jnp.arange(segments, dtype=jnp.float32)
    weights = jnp.exp(-pole_rates[:, None, :] * (jnp.float32(span) * (segments - 1 - index))[None, :, None])
    return jnp.sum(weights * ends, axis=1)


def incoming_state(local_end, pole_rates, row_count):
    ctx_count = lax.axis_size("ctx")
    total = jnp.zeros_like(local_end)
    for distance in range(1, ctx_count):
        received = shifted(local_end, "ctx", distance)
        total = total + jnp.exp(-pole_rates * jnp.float32(row_count * (distance - 1))) * received
    return total


def featurize(extended, tap_weights, stream, count):
    taps = tap_weights.shape[0]
    total = None
    for tap_index in range(taps):
        lead_row = taps - 1 - tap_index
        term = tap_weights[tap_index, stream].astype(jnp.float32)[None, :] * extended[
            stream, lead_row : lead_row + count
        ].astype(jnp.float32)
        total = term if total is None else total + term
    return total


def project(gated_mix, out_weight):
    ch_count = lax.axis_size("ch")
    width = gated_mix.shape[1]
    if ch_count != 4:
        gathered = lax.all_gather(gated_mix, "ch", axis=1, tiled=True)
        return jnp.dot(gathered, out_weight, preferred_element_type=jnp.float32)
    here = lax.axis_index("ch")

    def part(piece, owner):
        rows = lax.dynamic_slice_in_dim(out_weight, owner * width, width, 0)
        return jnp.dot(piece, rows, preferred_element_type=jnp.float32)

    far = lax.ppermute(gated_mix, "ch", [(i, i ^ 2) for i in range(ch_count)])
    near = lax.ppermute(gated_mix, "ch", [(i, i ^ 1) for i in range(ch_count)])
    total = part(gated_mix, here) + part(near, here ^ 1)
    far, total = lax.optimization_barrier((far, total))
    near_far = lax.ppermute(far, "ch", [(i, i ^ 1) for i in range(ch_count)])
    total = total + part(far, here ^ 2)
    return total + part(near_far, here ^ 3)


def shards(projected, tap_weights, pole_rates, residues, long_bias, out_weight):
    row_count = projected.shape[1]
    width = projected.shape[2]
    rows = width // LANES
    pole_count = pole_rates.shape[0]
    rim_rows = tap_weights.shape[0] - 1
    prior_rows = shifted(projected[:, row_count - rim_rows :], "ctx", 1)
    extended = jnp.concatenate([prior_rows, projected], 1)
    mixed_input = (
        featurize(extended, tap_weights, 1, row_count) * featurize(extended, tap_weights, 2, row_count)
    ).astype(jnp.bfloat16)
    x = mixed_input.astype(jnp.float32)
    span = row_count // SEGMENTS

    decay = jnp.exp(-pole_rates)
    ends = run_end_state(x, decay)
    start = incoming_state(device_end(ends, pole_rates, span), pole_rates, row_count)
    starts = segment_starts(ends, start, pole_rates, span)
    stream0 = featurize(extended, tap_weights, 0, row_count)
    ch_count = lax.axis_size("ch")
    pieces = 2 if (ch_count == 4 and width % (2 * LANES) == 0) else 1
    piece = width // pieces
    gated = []
    x_next = x[:, :piece]
    for index in range(pieces):
        cols = slice(index * piece, (index + 1) * piece)
        long_part = run_recurrence(x_next, decay[:, cols], residues[:, cols], starts[:, :, cols])
        long_mix = long_part.astype(jnp.bfloat16)
        gated_mix = stream0[:, cols] * (
            long_mix.astype(jnp.float32) + long_bias[None, cols] * mixed_input[:, cols].astype(jnp.float32)
        )
        gated_mix = gated_mix.astype(jnp.bfloat16)
        if index + 1 < pieces:
            x_next, gated_mix = lax.optimization_barrier((x[:, cols.stop : cols.stop + piece], gated_mix))
        gated.append(gated_mix)
    if pieces == 1:
        return project(gated[0], out_weight).astype(jnp.bfloat16)
    return project_pieces(gated, out_weight).astype(jnp.bfloat16)


def project_pieces(gated, out_weight):
    ch_count = lax.axis_size("ch")
    piece = gated[0].shape[1]
    width = piece * len(gated)
    here = lax.axis_index("ch")
    other_core = [(i, i ^ 1) for i in range(ch_count)]
    other_chip = [(i, i ^ 2) for i in range(ch_count)]

    def part(value, owner, index):
        rows = lax.dynamic_slice_in_dim(out_weight, owner * width + index * piece, value.shape[1], 0)
        return jnp.dot(value, rows, preferred_element_type=jnp.float32)

    far = [lax.ppermute(g, "ch", other_chip) for g in gated]
    own = jnp.concatenate(gated, 1)
    own, far[0] = lax.optimization_barrier((own, far[0]))
    near = lax.ppermute(own, "ch", other_core)
    near_far = [lax.ppermute(far[0], "ch", other_core)]
    total = part(own, here, 0) + part(far[0], here ^ 2, 0)
    total = total + part(near, here ^ 1, 0)
    for index in range(1, len(far)):
        far[index], total = lax.optimization_barrier((far[index], total))
        near_far.append(lax.ppermute(far[index], "ch", other_core))
        total = total + part(far[index], here ^ 2, index)
    for index in range(len(far)):
        total = total + part(near_far[index], here ^ 3, index)
    return total


def solution(mesh):
    in_specs = (
        P(None, "ctx", "ch"),
        P(None, None, "ch"),
        P(None, "ch"),
        P(None, "ch"),
        P("ch"),
        P(None, "ch"),
    )
    out_specs = P("ctx", "ch")
    return jax.shard_map(shards, mesh=mesh, in_specs=in_specs, out_specs=out_specs, check_vma=False)
```

```python
import jax
import jax.numpy as jnp
from jax import lax
from jax.experimental import pallas as pl
from jax.experimental.pallas import tpu as pltpu
from jax.sharding import PartitionSpec as P

LANES = 128
SEGMENTS = 8


def shifted(value, axis, steps):
    count = lax.axis_size(axis)
    initial, last = (max(0, -steps), min(count, count - steps))
    return lax.ppermute(value, axis, [(source, source + steps) for source in range(initial, last)])


def segment_pass(x_ref, decay_ref, residue_ref, start_ref, y_ref, end_ref):
    pole_count = decay_ref.shape[0]
    segments = SEGMENTS
    span = x_ref.shape[0] // segments
    lanes = x_ref.shape[1]
    decays = [jnp.broadcast_to(decay_ref[p : p + 1, :], (segments, lanes)) for p in range(pole_count)]
    if residue_ref is not None:
        residues = [jnp.broadcast_to(residue_ref[p : p + 1, :], (segments, lanes)) for p in range(pole_count)]
    if start_ref is None:
        states = tuple(jnp.zeros((segments, lanes), jnp.float32) for _ in range(pole_count))
    else:
        states = tuple(start_ref[p] for p in range(pole_count))

    def body(t, states):
        x = x_ref[pl.ds(t, segments, stride=span), :]
        updated = []
        total = None
        for p in range(pole_count):
            h = decays[p] * states[p] + x
            updated.append(h)
            if y_ref is not None:
                term = residues[p] * h
                total = term if total is None else total + term
        if y_ref is not None:
            y_ref[pl.ds(t, segments, stride=span), :] = total
        return tuple(updated)

    states = lax.fori_loop(0, span, body, states, unroll=4)
    if end_ref is not None:
        for p in range(pole_count):
            end_ref[p] = states[p]


def end_state_kernel(x_ref, decay_ref, end_ref):
    segment_pass(x_ref, decay_ref, None, None, None, end_ref)


def recurrence_kernel(x_ref, decay_ref, residue_ref, start_ref, y_ref):
    segment_pass(x_ref, decay_ref, residue_ref, start_ref, y_ref, None)


def run_end_state(x, decay):
    length, width = x.shape
    pole_count = decay.shape[0]
    return pl.pallas_call(
        end_state_kernel,
        grid=(width // LANES,),
        in_specs=[
            pl.BlockSpec((length, LANES), lambda g: (0, g)),
            pl.BlockSpec((pole_count, LANES), lambda g: (0, g)),
        ],
        out_specs=pl.BlockSpec((pole_count, SEGMENTS, LANES), lambda g: (0, 0, g)),
        out_shape=jax.ShapeDtypeStruct((pole_count, SEGMENTS, width), jnp.float32),
    )(x, decay)


def run_recurrence(x, decay, residue, start, first_group, group_count):
    length = x.shape[0]
    pole_count = decay.shape[0]
    pole_spec = pl.BlockSpec((pole_count, LANES), lambda g: (0, g + first_group))
    return pl.pallas_call(
        recurrence_kernel,
        grid=(group_count,),
        in_specs=[
            pl.BlockSpec((length, LANES), lambda g: (0, g + first_group)),
            pole_spec,
            pole_spec,
            pl.BlockSpec((pole_count, SEGMENTS, LANES), lambda g: (0, 0, g + first_group)),
        ],
        out_specs=pl.BlockSpec((length, LANES), lambda g: (0, g)),
        out_shape=jax.ShapeDtypeStruct((length, group_count * LANES), jnp.float32),
    )(x, decay, residue, start)


def segment_starts(ends, incoming, pole_rates, span):
    segments = ends.shape[1]
    index = jnp.arange(segments, dtype=jnp.int32)
    gaps = (index[:, None] - 1 - index[None, :]).astype(jnp.float32)
    weights = jnp.where(
        (index[None, :] < index[:, None])[:, :, None, None],
        jnp.exp(-pole_rates[None, None] * (jnp.float32(span) * jnp.maximum(gaps, 0.0))[:, :, None, None]),
        jnp.float32(0.0),
    )
    carried = jnp.einsum("abpc,pbc->pac", weights, ends, precision=lax.Precision.HIGHEST)
    lead = jnp.exp(-pole_rates[:, None, :] * (jnp.float32(span) * index.astype(jnp.float32))[None, :, None])
    return carried + lead * incoming[:, None, :]


def device_end(ends, pole_rates, span):
    segments = ends.shape[1]
    index = jnp.arange(segments, dtype=jnp.float32)
    weights = jnp.exp(-pole_rates[:, None, :] * (jnp.float32(span) * (segments - 1 - index))[None, :, None])
    return jnp.sum(weights * ends, axis=1)


def incoming_state(local_end, pole_rates, row_count):
    ctx_count = lax.axis_size("ctx")
    total = jnp.zeros_like(local_end)
    for distance in range(1, ctx_count):
        received = shifted(local_end, "ctx", distance)
        total = total + jnp.exp(-pole_rates * jnp.float32(row_count * (distance - 1))) * received
    return total


def featurize(extended, tap_weights, stream, count):
    taps = tap_weights.shape[0]
    total = None
    for tap_index in range(taps):
        lead_row = taps - 1 - tap_index
        term = tap_weights[tap_index, stream].astype(jnp.float32)[None, :] * extended[
            stream, lead_row : lead_row + count
        ].astype(jnp.float32)
        total = term if total is None else total + term
    return total


def project(gated_mix, out_weight):
    ch_count = lax.axis_size("ch")
    width = gated_mix.shape[1]
    if ch_count != 4:
        gathered = lax.all_gather(gated_mix, "ch", axis=1, tiled=True)
        return jnp.dot(gathered, out_weight, preferred_element_type=jnp.float32)
    here = lax.axis_index("ch")

    def part(piece, owner):
        rows = lax.dynamic_slice_in_dim(out_weight, owner * width, width, 0)
        return jnp.dot(piece, rows, preferred_element_type=jnp.float32)

    far = lax.ppermute(gated_mix, "ch", [(i, i ^ 2) for i in range(ch_count)])
    near = lax.ppermute(gated_mix, "ch", [(i, i ^ 1) for i in range(ch_count)])
    total = part(gated_mix, here) + part(near, here ^ 1)
    far, total = lax.optimization_barrier((far, total))
    near_far = lax.ppermute(far, "ch", [(i, i ^ 1) for i in range(ch_count)])
    total = total + part(far, here ^ 2)
    return total + part(near_far, here ^ 3)


def shards(projected, tap_weights, pole_rates, residues, long_bias, out_weight):
    row_count = projected.shape[1]
    width = projected.shape[2]
    rows = width // LANES
    pole_count = pole_rates.shape[0]
    rim_rows = tap_weights.shape[0] - 1
    prior_rows = shifted(projected[:, row_count - rim_rows :], "ctx", 1)
    extended = jnp.concatenate([prior_rows, projected], 1)
    mixed_input = (
        featurize(extended, tap_weights, 1, row_count) * featurize(extended, tap_weights, 2, row_count)
    ).astype(jnp.bfloat16)
    x = mixed_input.astype(jnp.float32)
    span = row_count // SEGMENTS

    decay = jnp.exp(-pole_rates)
    ends = run_end_state(x, decay)
    start = incoming_state(device_end(ends, pole_rates, span), pole_rates, row_count)
    starts = segment_starts(ends, start, pole_rates, span)
    ch_count = lax.axis_size("ch")
    pieces = 2 if (ch_count == 4 and width % (2 * LANES) == 0) else 1
    piece = width // pieces
    gated = []
    x_next = x
    for index in range(pieces):
        cols = slice(index * piece, (index + 1) * piece)
        long_part = run_recurrence(x_next, decay, residues, starts, index * piece // LANES, piece // LANES)
        long_mix = long_part.astype(jnp.bfloat16)
        stream0 = featurize(extended[:, :, cols], tap_weights[:, :, cols], 0, row_count)
        gated_mix = stream0 * (
            long_mix.astype(jnp.float32) + long_bias[None, cols] * mixed_input[:, cols].astype(jnp.float32)
        )
        gated_mix = gated_mix.astype(jnp.bfloat16)
        if index + 1 < pieces:
            x_next, gated_mix = lax.optimization_barrier((x, gated_mix))
        gated.append(gated_mix)
    if pieces == 1:
        return project(gated[0], out_weight).astype(jnp.bfloat16)
    return project_pieces(gated, out_weight).astype(jnp.bfloat16)


def project_pieces(gated, out_weight):
    ch_count = lax.axis_size("ch")
    piece = gated[0].shape[1]
    width = piece * len(gated)
    here = lax.axis_index("ch")
    other_core = [(i, i ^ 1) for i in range(ch_count)]
    other_chip = [(i, i ^ 2) for i in range(ch_count)]

    def part(value, owner, index):
        rows = lax.dynamic_slice_in_dim(out_weight, owner * width + index * piece, value.shape[1], 0)
        return jnp.dot(value, rows, preferred_element_type=jnp.float32)

    far = [lax.ppermute(g, "ch", other_chip) for g in gated]
    own = jnp.concatenate(gated, 1)
    own, far[0] = lax.optimization_barrier((own, far[0]))
    near = lax.ppermute(own, "ch", other_core)
    near_far = [lax.ppermute(far[0], "ch", other_core)]
    total = part(own, here, 0) + part(far[0], here ^ 2, 0)
    total = total + part(near, here ^ 1, 0)
    for index in range(1, len(far)):
        far[index], total = lax.optimization_barrier((far[index], total))
        near_far.append(lax.ppermute(far[index], "ch", other_core))
        total = total + part(far[index], here ^ 2, index)
    for index in range(len(far)):
        total = total + part(near_far[index], here ^ 3, index)
    return total


def solution(mesh):
    in_specs = (
        P(None, "ctx", "ch"),
        P(None, None, "ch"),
        P(None, "ch"),
        P(None, "ch"),
        P("ch"),
        P(None, "ch"),
    )
    out_specs = P("ctx", "ch")
    return jax.shard_map(shards, mesh=mesh, in_specs=in_specs, out_specs=out_specs, check_vma=False)
```

```python
import jax
import jax.numpy as jnp
from jax import lax
from jax.experimental import pallas as pl
from jax.experimental.pallas import tpu as pltpu
from jax.sharding import PartitionSpec as P

LANES = 128
SEGMENTS = 8


def shifted(value, axis, steps):
    count = lax.axis_size(axis)
    initial, last = (max(0, -steps), min(count, count - steps))
    return lax.ppermute(value, axis, [(source, source + steps) for source in range(initial, last)])


def segment_pass(x_ref, decay_ref, residue_ref, start_ref, y_ref, end_ref):
    pole_count = decay_ref.shape[0]
    segments = SEGMENTS
    span = x_ref.shape[0] // segments
    lanes = x_ref.shape[1]
    decays = [jnp.broadcast_to(decay_ref[p : p + 1, :], (segments, lanes)) for p in range(pole_count)]
    if residue_ref is not None:
        residues = [jnp.broadcast_to(residue_ref[p : p + 1, :], (segments, lanes)) for p in range(pole_count)]
    if start_ref is None:
        states = tuple(jnp.zeros((segments, lanes), jnp.float32) for _ in range(pole_count))
    else:
        states = tuple(start_ref[p] for p in range(pole_count))

    def body(t, states):
        x = x_ref[pl.ds(t, segments, stride=span), :]
        updated = []
        total = None
        for p in range(pole_count):
            h = decays[p] * states[p] + x
            updated.append(h)
            if y_ref is not None:
                term = residues[p] * h
                total = term if total is None else total + term
        if y_ref is not None:
            y_ref[pl.ds(t, segments, stride=span), :] = total
        return tuple(updated)

    states = lax.fori_loop(0, span, body, states, unroll=4)
    if end_ref is not None:
        for p in range(pole_count):
            end_ref[p] = states[p]


def end_state_kernel(x_ref, decay_ref, end_ref):
    segment_pass(x_ref, decay_ref, None, None, None, end_ref)


def recurrence_kernel(x_ref, decay_ref, residue_ref, start_ref, y_ref):
    segment_pass(x_ref, decay_ref, residue_ref, start_ref, y_ref, None)


def run_end_state(x, decay):
    length, width = x.shape
    pole_count = decay.shape[0]
    return pl.pallas_call(
        end_state_kernel,
        grid=(width // LANES,),
        in_specs=[
            pl.BlockSpec((length, LANES), lambda g: (0, g)),
            pl.BlockSpec((pole_count, LANES), lambda g: (0, g)),
        ],
        out_specs=pl.BlockSpec((pole_count, SEGMENTS, LANES), lambda g: (0, 0, g)),
        out_shape=jax.ShapeDtypeStruct((pole_count, SEGMENTS, width), jnp.float32),
    )(x, decay)


def run_recurrence(x, decay, residue, start, first_group, group_count):
    length = x.shape[0]
    pole_count = decay.shape[0]
    pole_spec = pl.BlockSpec((pole_count, LANES), lambda g: (0, g + first_group))
    return pl.pallas_call(
        recurrence_kernel,
        grid=(group_count,),
        in_specs=[
            pl.BlockSpec((length, LANES), lambda g: (0, g + first_group)),
            pole_spec,
            pole_spec,
            pl.BlockSpec((pole_count, SEGMENTS, LANES), lambda g: (0, 0, g + first_group)),
        ],
        out_specs=pl.BlockSpec((length, LANES), lambda g: (0, g)),
        out_shape=jax.ShapeDtypeStruct((length, group_count * LANES), jnp.float32),
    )(x, decay, residue, start)


def segment_starts(ends, incoming, pole_rates, span):
    segments = ends.shape[1]
    index = jnp.arange(segments, dtype=jnp.int32)
    gaps = (index[:, None] - 1 - index[None, :]).astype(jnp.float32)
    weights = jnp.where(
        (index[None, :] < index[:, None])[:, :, None, None],
        jnp.exp(-pole_rates[None, None] * (jnp.float32(span) * jnp.maximum(gaps, 0.0))[:, :, None, None]),
        jnp.float32(0.0),
    )
    carried = jnp.einsum("abpc,pbc->pac", weights, ends, precision=lax.Precision.HIGHEST)
    lead = jnp.exp(-pole_rates[:, None, :] * (jnp.float32(span) * index.astype(jnp.float32))[None, :, None])
    return carried + lead * incoming[:, None, :]


def device_end(ends, pole_rates, span):
    segments = ends.shape[1]
    index = jnp.arange(segments, dtype=jnp.float32)
    weights = jnp.exp(-pole_rates[:, None, :] * (jnp.float32(span) * (segments - 1 - index))[None, :, None])
    return jnp.sum(weights * ends, axis=1)


def incoming_state(local_end, pole_rates, row_count):
    ctx_count = lax.axis_size("ctx")
    total = jnp.zeros_like(local_end)
    for distance in range(1, ctx_count):
        received = shifted(local_end, "ctx", distance)
        total = total + jnp.exp(-pole_rates * jnp.float32(row_count * (distance - 1))) * received
    return total


def featurize(extended, tap_weights, stream, count):
    taps = tap_weights.shape[0]
    total = None
    for tap_index in range(taps):
        lead_row = taps - 1 - tap_index
        term = tap_weights[tap_index, stream].astype(jnp.float32)[None, :] * extended[
            stream, lead_row : lead_row + count
        ].astype(jnp.float32)
        total = term if total is None else total + term
    return total


def project(gated_mix, out_weight):
    ch_count = lax.axis_size("ch")
    width = gated_mix.shape[1]
    if ch_count != 4:
        gathered = lax.all_gather(gated_mix, "ch", axis=1, tiled=True)
        return jnp.dot(gathered, out_weight, preferred_element_type=jnp.float32)
    here = lax.axis_index("ch")

    def part(piece, owner):
        rows = lax.dynamic_slice_in_dim(out_weight, owner * width, width, 0)
        return jnp.dot(piece, rows, preferred_element_type=jnp.float32)

    far = lax.ppermute(gated_mix, "ch", [(i, i ^ 2) for i in range(ch_count)])
    near = lax.ppermute(gated_mix, "ch", [(i, i ^ 1) for i in range(ch_count)])
    total = part(gated_mix, here) + part(near, here ^ 1)
    far, total = lax.optimization_barrier((far, total))
    near_far = lax.ppermute(far, "ch", [(i, i ^ 1) for i in range(ch_count)])
    total = total + part(far, here ^ 2)
    return total + part(near_far, here ^ 3)


def shards(projected, tap_weights, pole_rates, residues, long_bias, out_weight):
    row_count = projected.shape[1]
    width = projected.shape[2]
    rows = width // LANES
    pole_count = pole_rates.shape[0]
    rim_rows = tap_weights.shape[0] - 1
    prior_rows = shifted(projected[:, row_count - rim_rows :], "ctx", 1)
    extended = jnp.concatenate([prior_rows, projected], 1)
    mixed_input = (
        featurize(extended, tap_weights, 1, row_count) * featurize(extended, tap_weights, 2, row_count)
    ).astype(jnp.bfloat16)
    x = mixed_input.astype(jnp.float32)
    span = row_count // SEGMENTS

    decay = jnp.exp(-pole_rates)
    ends = run_end_state(x, decay)
    start = incoming_state(device_end(ends, pole_rates, span), pole_rates, row_count)
    starts = segment_starts(ends, start, pole_rates, span)
    ch_count = lax.axis_size("ch")
    groups = width // LANES
    lead_groups = (3 * groups) // 8 if ch_count == 4 else 0
    bounds = [0, lead_groups * LANES, width] if lead_groups > 0 else [0, width]
    pieces = len(bounds) - 1
    gated = []
    x_next = x
    for index in range(pieces):
        cols = slice(bounds[index], bounds[index + 1])
        group_count = (cols.stop - cols.start) // LANES
        long_part = run_recurrence(x_next, decay, residues, starts, cols.start // LANES, group_count)
        long_mix = long_part.astype(jnp.bfloat16)
        stream0 = featurize(extended[:, :, cols], tap_weights[:, :, cols], 0, row_count)
        gated_mix = stream0 * (
            long_mix.astype(jnp.float32) + long_bias[None, cols] * mixed_input[:, cols].astype(jnp.float32)
        )
        gated_mix = gated_mix.astype(jnp.bfloat16)
        if index + 1 < pieces:
            x_next, gated_mix = lax.optimization_barrier((x, gated_mix))
        gated.append(gated_mix)
    if pieces == 1:
        return project(gated[0], out_weight).astype(jnp.bfloat16)
    return project_pieces(gated, out_weight).astype(jnp.bfloat16)


def project_pieces(gated, out_weight):
    ch_count = lax.axis_size("ch")
    offsets = [0]
    for value in gated:
        offsets.append(offsets[-1] + value.shape[1])
    width = offsets[-1]
    here = lax.axis_index("ch")
    other_core = [(i, i ^ 1) for i in range(ch_count)]
    other_chip = [(i, i ^ 2) for i in range(ch_count)]

    def part(value, owner, index):
        rows = lax.dynamic_slice_in_dim(out_weight, owner * width + offsets[index], value.shape[1], 0)
        return jnp.dot(value, rows, preferred_element_type=jnp.float32)

    far = [lax.ppermute(g, "ch", other_chip) for g in gated]
    own = jnp.concatenate(gated, 1)
    own, far[0] = lax.optimization_barrier((own, far[0]))
    near = lax.ppermute(own, "ch", other_core)
    near_far = [lax.ppermute(far[0], "ch", other_core)]
    rows_own = lax.dynamic_slice_in_dim(out_weight, here * width, width, 0)
    rows_near = lax.dynamic_slice_in_dim(out_weight, (here ^ 1) * width, width, 0)
    total = jnp.dot(own, rows_own, preferred_element_type=jnp.float32) + part(far[0], here ^ 2, 0)
    total = total + jnp.dot(near, rows_near, preferred_element_type=jnp.float32)
    total = total + part(near_far[0], here ^ 3, 0)
    for index in range(1, len(far)):
        far[index], total = lax.optimization_barrier((far[index], total))
        near_far.append(lax.ppermute(far[index], "ch", other_core))
        total = total + part(far[index], here ^ 2, index)
    for index in range(1, len(far)):
        total = total + part(near_far[index], here ^ 3, index)
    return total


def solution(mesh):
    in_specs = (
        P(None, "ctx", "ch"),
        P(None, None, "ch"),
        P(None, "ch"),
        P(None, "ch"),
        P("ch"),
        P(None, "ch"),
    )
    out_specs = P("ctx", "ch")
    return jax.shard_map(shards, mesh=mesh, in_specs=in_specs, out_specs=out_specs, check_vma=False)
```

```python
import jax
import jax.numpy as jnp
from jax import lax
from jax.experimental import pallas as pl
from jax.experimental.pallas import tpu as pltpu
from jax.sharding import PartitionSpec as P

LANES = 128
SEGMENTS = 8


def shifted(value, axis, steps):
    count = lax.axis_size(axis)
    initial, last = (max(0, -steps), min(count, count - steps))
    return lax.ppermute(value, axis, [(source, source + steps) for source in range(initial, last)])


def segment_pass(x_ref, decay_ref, residue_ref, start_ref, y_ref, end_ref):
    pole_count = decay_ref.shape[0]
    segments = SEGMENTS
    span = x_ref.shape[0] // segments
    lanes = x_ref.shape[1]
    decays = [jnp.broadcast_to(decay_ref[p : p + 1, :], (segments, lanes)) for p in range(pole_count)]
    if residue_ref is not None:
        residues = [jnp.broadcast_to(residue_ref[p : p + 1, :], (segments, lanes)) for p in range(pole_count)]
    if start_ref is None:
        states = tuple(jnp.zeros((segments, lanes), jnp.float32) for _ in range(pole_count))
    else:
        states = tuple(start_ref[p] for p in range(pole_count))

    def body(t, states):
        x = x_ref[pl.ds(t, segments, stride=span), :]
        updated = []
        total = None
        for p in range(pole_count):
            h = decays[p] * states[p] + x
            updated.append(h)
            if y_ref is not None:
                term = residues[p] * h
                total = term if total is None else total + term
        if y_ref is not None:
            y_ref[pl.ds(t, segments, stride=span), :] = total
        return tuple(updated)

    states = lax.fori_loop(0, span, body, states, unroll=4)
    if end_ref is not None:
        for p in range(pole_count):
            end_ref[p] = states[p]


def end_state_kernel(x_ref, decay_ref, end_ref):
    segment_pass(x_ref, decay_ref, None, None, None, end_ref)


def recurrence_kernel(x_ref, decay_ref, residue_ref, start_ref, y_ref):
    segment_pass(x_ref, decay_ref, residue_ref, start_ref, y_ref, None)


def run_end_state(x, decay):
    length, width = x.shape
    pole_count = decay.shape[0]
    return pl.pallas_call(
        end_state_kernel,
        grid=(width // LANES,),
        in_specs=[
            pl.BlockSpec((length, LANES), lambda g: (0, g)),
            pl.BlockSpec((pole_count, LANES), lambda g: (0, g)),
        ],
        out_specs=pl.BlockSpec((pole_count, SEGMENTS, LANES), lambda g: (0, 0, g)),
        out_shape=jax.ShapeDtypeStruct((pole_count, SEGMENTS, width), jnp.float32),
    )(x, decay)


def run_recurrence(x, decay, residue, start, first_group, group_count):
    length = x.shape[0]
    pole_count = decay.shape[0]
    pole_spec = pl.BlockSpec((pole_count, LANES), lambda g: (0, g + first_group))
    return pl.pallas_call(
        recurrence_kernel,
        grid=(group_count,),
        in_specs=[
            pl.BlockSpec((length, LANES), lambda g: (0, g + first_group)),
            pole_spec,
            pole_spec,
            pl.BlockSpec((pole_count, SEGMENTS, LANES), lambda g: (0, 0, g + first_group)),
        ],
        out_specs=pl.BlockSpec((length, LANES), lambda g: (0, g)),
        out_shape=jax.ShapeDtypeStruct((length, group_count * LANES), jnp.float32),
    )(x, decay, residue, start)


def segment_starts(ends, incoming, pole_rates, span):
    segments = ends.shape[1]
    index = jnp.arange(segments, dtype=jnp.int32)
    gaps = (index[:, None] - 1 - index[None, :]).astype(jnp.float32)
    weights = jnp.where(
        (index[None, :] < index[:, None])[:, :, None, None],
        jnp.exp(-pole_rates[None, None] * (jnp.float32(span) * jnp.maximum(gaps, 0.0))[:, :, None, None]),
        jnp.float32(0.0),
    )
    carried = jnp.einsum("abpc,pbc->pac", weights, ends, precision=lax.Precision.HIGHEST)
    lead = jnp.exp(-pole_rates[:, None, :] * (jnp.float32(span) * index.astype(jnp.float32))[None, :, None])
    return carried + lead * incoming[:, None, :]


def device_end(ends, pole_rates, span):
    segments = ends.shape[1]
    index = jnp.arange(segments, dtype=jnp.float32)
    weights = jnp.exp(-pole_rates[:, None, :] * (jnp.float32(span) * (segments - 1 - index))[None, :, None])
    return jnp.sum(weights * ends, axis=1)


def incoming_state(local_end, pole_rates, row_count):
    ctx_count = lax.axis_size("ctx")
    total = jnp.zeros_like(local_end)
    for distance in range(1, ctx_count):
        received = shifted(local_end, "ctx", distance)
        total = total + jnp.exp(-pole_rates * jnp.float32(row_count * (distance - 1))) * received
    return total


def featurize(extended, tap_weights, stream, count):
    taps = tap_weights.shape[0]
    total = None
    for tap_index in range(taps):
        lead_row = taps - 1 - tap_index
        term = tap_weights[tap_index, stream].astype(jnp.float32)[None, :] * extended[
            stream, lead_row : lead_row + count
        ].astype(jnp.float32)
        total = term if total is None else total + term
    return total


def project(gated_mix, out_weight):
    ch_count = lax.axis_size("ch")
    width = gated_mix.shape[1]
    if ch_count != 4:
        gathered = lax.all_gather(gated_mix, "ch", axis=1, tiled=True)
        return jnp.dot(gathered, out_weight, preferred_element_type=jnp.float32)
    here = lax.axis_index("ch")

    def part(piece, owner):
        rows = lax.dynamic_slice_in_dim(out_weight, owner * width, width, 0)
        return jnp.dot(piece, rows, preferred_element_type=jnp.float32)

    far = lax.ppermute(gated_mix, "ch", [(i, i ^ 2) for i in range(ch_count)])
    near = lax.ppermute(gated_mix, "ch", [(i, i ^ 1) for i in range(ch_count)])
    total = part(gated_mix, here) + part(near, here ^ 1)
    far, total = lax.optimization_barrier((far, total))
    near_far = lax.ppermute(far, "ch", [(i, i ^ 1) for i in range(ch_count)])
    total = total + part(far, here ^ 2)
    return total + part(near_far, here ^ 3)


def shards(projected, tap_weights, pole_rates, residues, long_bias, out_weight):
    row_count = projected.shape[1]
    width = projected.shape[2]
    rows = width // LANES
    pole_count = pole_rates.shape[0]
    rim_rows = tap_weights.shape[0] - 1
    prior_rows = shifted(projected[:, row_count - rim_rows :], "ctx", 1)
    extended = jnp.concatenate([prior_rows, projected], 1)
    mixed_input = (
        featurize(extended, tap_weights, 1, row_count) * featurize(extended, tap_weights, 2, row_count)
    ).astype(jnp.bfloat16)
    x = mixed_input.astype(jnp.float32)
    span = row_count // SEGMENTS

    decay = jnp.exp(-pole_rates)
    ends = run_end_state(x, decay)
    start = incoming_state(device_end(ends, pole_rates, span), pole_rates, row_count)
    starts = segment_starts(ends, start, pole_rates, span)
    ch_count = lax.axis_size("ch")
    groups = width // LANES
    if ch_count == 4 and groups >= 8:
        bounds = [0, (2 * groups) // 8 * LANES, (5 * groups) // 8 * LANES, width]
    else:
        bounds = [0, width]
    pieces = len(bounds) - 1
    gated = []
    far = []
    x_next = x
    for index in range(pieces):
        cols = slice(bounds[index], bounds[index + 1])
        group_count = (cols.stop - cols.start) // LANES
        long_part = run_recurrence(x_next, decay, residues, starts, cols.start // LANES, group_count)
        long_mix = long_part.astype(jnp.bfloat16)
        stream0 = featurize(extended[:, :, cols], tap_weights[:, :, cols], 0, row_count)
        gated_mix = stream0 * (
            long_mix.astype(jnp.float32) + long_bias[None, cols] * mixed_input[:, cols].astype(jnp.float32)
        )
        gated_mix = gated_mix.astype(jnp.bfloat16)
        if index + 1 < pieces:
            x_next, gated_mix = lax.optimization_barrier((x, gated_mix))
        gated.append(gated_mix)
        if pieces > 1:
            far.append(lax.ppermute(gated_mix, "ch", [(i, i ^ 2) for i in range(ch_count)]))
        if index + 1 < pieces and index >= 1:
            x_next, far[index - 1] = lax.optimization_barrier((x_next, far[index - 1]))
    if pieces == 1:
        return project(gated[0], out_weight).astype(jnp.bfloat16)
    return project_pieces(gated, far, out_weight).astype(jnp.bfloat16)


def project_pieces(gated, far, out_weight):
    ch_count = lax.axis_size("ch")
    offsets = [0]
    for value in gated:
        offsets.append(offsets[-1] + value.shape[1])
    width = offsets[-1]
    here = lax.axis_index("ch")
    other_core = [(i, i ^ 1) for i in range(ch_count)]
    other_chip = [(i, i ^ 2) for i in range(ch_count)]

    def part(value, owner, index):
        rows = lax.dynamic_slice_in_dim(out_weight, owner * width + offsets[index], value.shape[1], 0)
        return jnp.dot(value, rows, preferred_element_type=jnp.float32)

    far = list(far)
    own = jnp.concatenate(gated, 1)
    early = len(far) - 1
    own, early_far = lax.optimization_barrier((own, far[:early]))
    far[:early] = early_far
    near = lax.ppermute(own, "ch", other_core)
    near_far = [lax.ppermute(f, "ch", other_core) for f in far[:early]]
    rows_own = lax.dynamic_slice_in_dim(out_weight, here * width, width, 0)
    rows_near = lax.dynamic_slice_in_dim(out_weight, (here ^ 1) * width, width, 0)
    total = jnp.dot(own, rows_own, preferred_element_type=jnp.float32)
    for index in range(early):
        total = total + part(far[index], here ^ 2, index)
    total = total + jnp.dot(near, rows_near, preferred_element_type=jnp.float32)
    for index in range(early):
        total = total + part(near_far[index], here ^ 3, index)
    last = far[early]
    last, total = lax.optimization_barrier((last, total))
    near_last = lax.ppermute(last, "ch", other_core)
    total = total + part(last, here ^ 2, early)
    total = total + part(near_last, here ^ 3, early)
    return total


def solution(mesh):
    in_specs = (
        P(None, "ctx", "ch"),
        P(None, None, "ch"),
        P(None, "ch"),
        P(None, "ch"),
        P("ch"),
        P(None, "ch"),
    )
    out_specs = P("ctx", "ch")
    return jax.shard_map(shards, mesh=mesh, in_specs=in_specs, out_specs=out_specs, check_vma=False)
```

```python
import jax
import jax.numpy as jnp
from jax import lax
from jax.experimental import pallas as pl
from jax.experimental.pallas import tpu as pltpu
from jax.sharding import PartitionSpec as P

LANES = 128
SEGMENTS = 8


def shifted(value, axis, steps):
    count = lax.axis_size(axis)
    initial, last = (max(0, -steps), min(count, count - steps))
    return lax.ppermute(value, axis, [(source, source + steps) for source in range(initial, last)])


def segment_pass(x_ref, decay_ref, residue_ref, start_ref, y_ref, end_ref):
    pole_count = decay_ref.shape[0]
    segments = SEGMENTS
    span = x_ref.shape[0] // segments
    lanes = x_ref.shape[1]
    decays = [jnp.broadcast_to(decay_ref[p : p + 1, :], (segments, lanes)) for p in range(pole_count)]
    if residue_ref is not None:
        residues = [jnp.broadcast_to(residue_ref[p : p + 1, :], (segments, lanes)) for p in range(pole_count)]
    if start_ref is None:
        states = tuple(jnp.zeros((segments, lanes), jnp.float32) for _ in range(pole_count))
    else:
        states = tuple(start_ref[p] for p in range(pole_count))

    def body(t, states):
        x = x_ref[pl.ds(t, segments, stride=span), :]
        updated = []
        total = None
        for p in range(pole_count):
            h = decays[p] * states[p] + x
            updated.append(h)
            if y_ref is not None:
                term = residues[p] * h
                total = term if total is None else total + term
        if y_ref is not None:
            y_ref[pl.ds(t, segments, stride=span), :] = total
        return tuple(updated)

    states = lax.fori_loop(0, span, body, states, unroll=4)
    if end_ref is not None:
        for p in range(pole_count):
            end_ref[p] = states[p]


def end_state_kernel(x_ref, decay_ref, end_ref):
    segment_pass(x_ref, decay_ref, None, None, None, end_ref)


def recurrence_kernel(x_ref, decay_ref, residue_ref, start_ref, y_ref):
    segment_pass(x_ref, decay_ref, residue_ref, start_ref, y_ref, None)


def run_end_state(x, decay):
    length, width = x.shape
    pole_count = decay.shape[0]
    return pl.pallas_call(
        end_state_kernel,
        grid=(width // LANES,),
        in_specs=[
            pl.BlockSpec((length, LANES), lambda g: (0, g)),
            pl.BlockSpec((pole_count, LANES), lambda g: (0, g)),
        ],
        out_specs=pl.BlockSpec((pole_count, SEGMENTS, LANES), lambda g: (0, 0, g)),
        out_shape=jax.ShapeDtypeStruct((pole_count, SEGMENTS, width), jnp.float32),
    )(x, decay)


def run_recurrence(x, decay, residue, start, first_group, group_count):
    length = x.shape[0]
    pole_count = decay.shape[0]
    pole_spec = pl.BlockSpec((pole_count, LANES), lambda g: (0, g + first_group))
    return pl.pallas_call(
        recurrence_kernel,
        grid=(group_count,),
        in_specs=[
            pl.BlockSpec((length, LANES), lambda g: (0, g + first_group)),
            pole_spec,
            pole_spec,
            pl.BlockSpec((pole_count, SEGMENTS, LANES), lambda g: (0, 0, g + first_group)),
        ],
        out_specs=pl.BlockSpec((length, LANES), lambda g: (0, g)),
        out_shape=jax.ShapeDtypeStruct((length, group_count * LANES), jnp.float32),
    )(x, decay, residue, start)


def segment_starts(ends, incoming, pole_rates, span):
    segments = ends.shape[1]
    index = jnp.arange(segments, dtype=jnp.int32)
    gaps = (index[:, None] - 1 - index[None, :]).astype(jnp.float32)
    weights = jnp.where(
        (index[None, :] < index[:, None])[:, :, None, None],
        jnp.exp(-pole_rates[None, None] * (jnp.float32(span) * jnp.maximum(gaps, 0.0))[:, :, None, None]),
        jnp.float32(0.0),
    )
    carried = jnp.einsum("abpc,pbc->pac", weights, ends, precision=lax.Precision.HIGHEST)
    lead = jnp.exp(-pole_rates[:, None, :] * (jnp.float32(span) * index.astype(jnp.float32))[None, :, None])
    return carried + lead * incoming[:, None, :]


def device_end(ends, pole_rates, span):
    segments = ends.shape[1]
    index = jnp.arange(segments, dtype=jnp.float32)
    weights = jnp.exp(-pole_rates[:, None, :] * (jnp.float32(span) * (segments - 1 - index))[None, :, None])
    return jnp.sum(weights * ends, axis=1)


def incoming_state(local_end, pole_rates, row_count):
    ctx_count = lax.axis_size("ctx")
    total = jnp.zeros_like(local_end)
    for distance in range(1, ctx_count):
        received = shifted(local_end, "ctx", distance)
        total = total + jnp.exp(-pole_rates * jnp.float32(row_count * (distance - 1))) * received
    return total


def featurize(extended, tap_weights, stream, count):
    taps = tap_weights.shape[0]
    total = None
    for tap_index in range(taps):
        lead_row = taps - 1 - tap_index
        term = tap_weights[tap_index, stream].astype(jnp.float32)[None, :] * extended[
            stream, lead_row : lead_row + count
        ].astype(jnp.float32)
        total = term if total is None else total + term
    return total


def project(gated_mix, out_weight):
    ch_count = lax.axis_size("ch")
    width = gated_mix.shape[1]
    if ch_count != 4:
        gathered = lax.all_gather(gated_mix, "ch", axis=1, tiled=True)
        return jnp.dot(gathered, out_weight, preferred_element_type=jnp.float32)
    here = lax.axis_index("ch")

    def part(piece, owner):
        rows = lax.dynamic_slice_in_dim(out_weight, owner * width, width, 0)
        return jnp.dot(piece, rows, preferred_element_type=jnp.float32)

    far = lax.ppermute(gated_mix, "ch", [(i, i ^ 2) for i in range(ch_count)])
    near = lax.ppermute(gated_mix, "ch", [(i, i ^ 1) for i in range(ch_count)])
    total = part(gated_mix, here) + part(near, here ^ 1)
    far, total = lax.optimization_barrier((far, total))
    near_far = lax.ppermute(far, "ch", [(i, i ^ 1) for i in range(ch_count)])
    total = total + part(far, here ^ 2)
    return total + part(near_far, here ^ 3)


def shards(projected, tap_weights, pole_rates, residues, long_bias, out_weight):
    row_count = projected.shape[1]
    width = projected.shape[2]
    rows = width // LANES
    pole_count = pole_rates.shape[0]
    rim_rows = tap_weights.shape[0] - 1
    prior_rows = shifted(projected[:, row_count - rim_rows :], "ctx", 1)
    extended = jnp.concatenate([prior_rows, projected], 1)
    mixed_input = (
        featurize(extended, tap_weights, 1, row_count) * featurize(extended, tap_weights, 2, row_count)
    ).astype(jnp.bfloat16)
    x = mixed_input.astype(jnp.float32)
    span = row_count // SEGMENTS

    decay = jnp.exp(-pole_rates)
    ends = run_end_state(x, decay)
    start = incoming_state(device_end(ends, pole_rates, span), pole_rates, row_count)
    starts = segment_starts(ends, start, pole_rates, span)
    ch_count = lax.axis_size("ch")
    groups = width // LANES
    if ch_count == 4 and groups >= 8:
        bounds = [split * groups // 8 * LANES for split in (0, 1, 3, 5, 8)]
    else:
        bounds = [0, width]
    pieces = len(bounds) - 1
    gated = []
    far = []
    x_next = x
    for index in range(pieces):
        cols = slice(bounds[index], bounds[index + 1])
        group_count = (cols.stop - cols.start) // LANES
        long_part = run_recurrence(x_next, decay, residues, starts, cols.start // LANES, group_count)
        long_mix = long_part.astype(jnp.bfloat16)
        stream0 = featurize(extended[:, :, cols], tap_weights[:, :, cols], 0, row_count)
        gated_mix = stream0 * (
            long_mix.astype(jnp.float32) + long_bias[None, cols] * mixed_input[:, cols].astype(jnp.float32)
        )
        gated_mix = gated_mix.astype(jnp.bfloat16)
        if index + 1 < pieces:
            x_next, gated_mix = lax.optimization_barrier((x, gated_mix))
        gated.append(gated_mix)
        if pieces > 1:
            far.append(lax.ppermute(gated_mix, "ch", [(i, i ^ 2) for i in range(ch_count)]))
        if index + 1 < pieces and index >= 1:
            x_next, far[index - 1] = lax.optimization_barrier((x_next, far[index - 1]))
    if pieces == 1:
        return project(gated[0], out_weight).astype(jnp.bfloat16)
    return project_pieces(gated, far, out_weight).astype(jnp.bfloat16)


def project_pieces(gated, far, out_weight):
    ch_count = lax.axis_size("ch")
    offsets = [0]
    for value in gated:
        offsets.append(offsets[-1] + value.shape[1])
    width = offsets[-1]
    here = lax.axis_index("ch")
    other_core = [(i, i ^ 1) for i in range(ch_count)]
    other_chip = [(i, i ^ 2) for i in range(ch_count)]

    def part(value, owner, index):
        rows = lax.dynamic_slice_in_dim(out_weight, owner * width + offsets[index], value.shape[1], 0)
        return jnp.dot(value, rows, preferred_element_type=jnp.float32)

    far = list(far)
    own = jnp.concatenate(gated, 1)
    early = len(far) - 1
    own, early_far = lax.optimization_barrier((own, far[:early]))
    far[:early] = early_far
    near = lax.ppermute(own, "ch", other_core)
    near_far = [lax.ppermute(f, "ch", other_core) for f in far[:early]]
    rows_own = lax.dynamic_slice_in_dim(out_weight, here * width, width, 0)
    rows_near = lax.dynamic_slice_in_dim(out_weight, (here ^ 1) * width, width, 0)
    total = jnp.dot(own, rows_own, preferred_element_type=jnp.float32)
    for index in range(early):
        total = total + part(far[index], here ^ 2, index)
    total = total + jnp.dot(near, rows_near, preferred_element_type=jnp.float32)
    for index in range(early):
        total = total + part(near_far[index], here ^ 3, index)
    last = far[early]
    last, total = lax.optimization_barrier((last, total))
    near_last = lax.ppermute(last, "ch", other_core)
    total = total + part(last, here ^ 2, early)
    total = total + part(near_last, here ^ 3, early)
    return total


def solution(mesh):
    in_specs = (
        P(None, "ctx", "ch"),
        P(None, None, "ch"),
        P(None, "ch"),
        P(None, "ch"),
        P("ch"),
        P(None, "ch"),
    )
    out_specs = P("ctx", "ch")
    return jax.shard_map(shards, mesh=mesh, in_specs=in_specs, out_specs=out_specs, check_vma=False)
```

```python
import jax
import jax.numpy as jnp
from jax import lax
from jax.experimental import pallas as pl
from jax.experimental.pallas import tpu as pltpu
from jax.sharding import PartitionSpec as P

LANES = 128
SEGMENTS = 8


def shifted(value, axis, steps):
    count = lax.axis_size(axis)
    initial, last = (max(0, -steps), min(count, count - steps))
    return lax.ppermute(value, axis, [(source, source + steps) for source in range(initial, last)])


def segment_pass(x_ref, decay_ref, residue_ref, start_ref, y_ref, end_ref):
    pole_count = decay_ref.shape[0]
    segments = SEGMENTS
    span = x_ref.shape[0] // segments
    lanes = x_ref.shape[1]
    decays = [jnp.broadcast_to(decay_ref[p : p + 1, :], (segments, lanes)) for p in range(pole_count)]
    if residue_ref is not None:
        residues = [jnp.broadcast_to(residue_ref[p : p + 1, :], (segments, lanes)) for p in range(pole_count)]
    if start_ref is None:
        states = tuple(jnp.zeros((segments, lanes), jnp.float32) for _ in range(pole_count))
    else:
        states = tuple(start_ref[p] for p in range(pole_count))

    def body(t, states):
        x = x_ref[pl.ds(t, segments, stride=span), :]
        updated = []
        total = None
        for p in range(pole_count):
            h = decays[p] * states[p] + x
            updated.append(h)
            if y_ref is not None:
                term = residues[p] * h
                total = term if total is None else total + term
        if y_ref is not None:
            y_ref[pl.ds(t, segments, stride=span), :] = total
        return tuple(updated)

    states = lax.fori_loop(0, span, body, states, unroll=8)
    if end_ref is not None:
        for p in range(pole_count):
            end_ref[p] = states[p]


def end_state_kernel(x_ref, decay_ref, end_ref):
    segment_pass(x_ref, decay_ref, None, None, None, end_ref)


def recurrence_kernel(x_ref, decay_ref, residue_ref, start_ref, y_ref):
    segment_pass(x_ref, decay_ref, residue_ref, start_ref, y_ref, None)


def run_end_state(x, decay):
    length, width = x.shape
    pole_count = decay.shape[0]
    return pl.pallas_call(
        end_state_kernel,
        grid=(width // LANES,),
        in_specs=[
            pl.BlockSpec((length, LANES), lambda g: (0, g)),
            pl.BlockSpec((pole_count, LANES), lambda g: (0, g)),
        ],
        out_specs=pl.BlockSpec((pole_count, SEGMENTS, LANES), lambda g: (0, 0, g)),
        out_shape=jax.ShapeDtypeStruct((pole_count, SEGMENTS, width), jnp.float32),
    )(x, decay)


def run_recurrence(x, decay, residue, start, first_group, group_count):
    length = x.shape[0]
    pole_count = decay.shape[0]
    pole_spec = pl.BlockSpec((pole_count, LANES), lambda g: (0, g + first_group))
    return pl.pallas_call(
        recurrence_kernel,
        grid=(group_count,),
        in_specs=[
            pl.BlockSpec((length, LANES), lambda g: (0, g + first_group)),
            pole_spec,
            pole_spec,
            pl.BlockSpec((pole_count, SEGMENTS, LANES), lambda g: (0, 0, g + first_group)),
        ],
        out_specs=pl.BlockSpec((length, LANES), lambda g: (0, g)),
        out_shape=jax.ShapeDtypeStruct((length, group_count * LANES), jnp.float32),
    )(x, decay, residue, start)


def segment_starts(ends, incoming, pole_rates, span):
    segments = ends.shape[1]
    index = jnp.arange(segments, dtype=jnp.int32)
    gaps = (index[:, None] - 1 - index[None, :]).astype(jnp.float32)
    weights = jnp.where(
        (index[None, :] < index[:, None])[:, :, None, None],
        jnp.exp(-pole_rates[None, None] * (jnp.float32(span) * jnp.maximum(gaps, 0.0))[:, :, None, None]),
        jnp.float32(0.0),
    )
    carried = jnp.einsum("abpc,pbc->pac", weights, ends, precision=lax.Precision.HIGHEST)
    lead = jnp.exp(-pole_rates[:, None, :] * (jnp.float32(span) * index.astype(jnp.float32))[None, :, None])
    return carried + lead * incoming[:, None, :]


def device_end(ends, pole_rates, span):
    segments = ends.shape[1]
    index = jnp.arange(segments, dtype=jnp.float32)
    weights = jnp.exp(-pole_rates[:, None, :] * (jnp.float32(span) * (segments - 1 - index))[None, :, None])
    return jnp.sum(weights * ends, axis=1)


def incoming_state(local_end, pole_rates, row_count):
    ctx_count = lax.axis_size("ctx")
    total = jnp.zeros_like(local_end)
    for distance in range(1, ctx_count):
        received = shifted(local_end, "ctx", distance)
        total = total + jnp.exp(-pole_rates * jnp.float32(row_count * (distance - 1))) * received
    return total


def featurize(extended, tap_weights, stream, count):
    taps = tap_weights.shape[0]
    total = None
    for tap_index in range(taps):
        lead_row = taps - 1 - tap_index
        term = tap_weights[tap_index, stream].astype(jnp.float32)[None, :] * extended[
            stream, lead_row : lead_row + count
        ].astype(jnp.float32)
        total = term if total is None else total + term
    return total


def project(gated_mix, out_weight):
    ch_count = lax.axis_size("ch")
    width = gated_mix.shape[1]
    if ch_count != 4:
        gathered = lax.all_gather(gated_mix, "ch", axis=1, tiled=True)
        return jnp.dot(gathered, out_weight, preferred_element_type=jnp.float32)
    here = lax.axis_index("ch")

    def part(piece, owner):
        rows = lax.dynamic_slice_in_dim(out_weight, owner * width, width, 0)
        return jnp.dot(piece, rows, preferred_element_type=jnp.float32)

    far = lax.ppermute(gated_mix, "ch", [(i, i ^ 2) for i in range(ch_count)])
    near = lax.ppermute(gated_mix, "ch", [(i, i ^ 1) for i in range(ch_count)])
    total = part(gated_mix, here) + part(near, here ^ 1)
    far, total = lax.optimization_barrier((far, total))
    near_far = lax.ppermute(far, "ch", [(i, i ^ 1) for i in range(ch_count)])
    total = total + part(far, here ^ 2)
    return total + part(near_far, here ^ 3)


def shards(projected, tap_weights, pole_rates, residues, long_bias, out_weight):
    row_count = projected.shape[1]
    width = projected.shape[2]
    rows = width // LANES
    pole_count = pole_rates.shape[0]
    rim_rows = tap_weights.shape[0] - 1
    prior_rows = shifted(projected[:, row_count - rim_rows :], "ctx", 1)
    extended = jnp.concatenate([prior_rows, projected], 1)
    mixed_input = (
        featurize(extended, tap_weights, 1, row_count) * featurize(extended, tap_weights, 2, row_count)
    ).astype(jnp.bfloat16)
    x = mixed_input.astype(jnp.float32)
    span = row_count // SEGMENTS

    decay = jnp.exp(-pole_rates)
    ends = run_end_state(x, decay)
    start = incoming_state(device_end(ends, pole_rates, span), pole_rates, row_count)
    starts = segment_starts(ends, start, pole_rates, span)
    ch_count = lax.axis_size("ch")
    groups = width // LANES
    if ch_count == 4 and groups >= 8:
        bounds = [0, (2 * groups) // 8 * LANES, (5 * groups) // 8 * LANES, width]
    else:
        bounds = [0, width]
    pieces = len(bounds) - 1
    gated = []
    far = []
    x_next = x
    for index in range(pieces):
        cols = slice(bounds[index], bounds[index + 1])
        group_count = (cols.stop - cols.start) // LANES
        long_part = run_recurrence(x_next, decay, residues, starts, cols.start // LANES, group_count)
        long_mix = long_part.astype(jnp.bfloat16)
        stream0 = featurize(extended[:, :, cols], tap_weights[:, :, cols], 0, row_count)
        gated_mix = stream0 * (
            long_mix.astype(jnp.float32) + long_bias[None, cols] * mixed_input[:, cols].astype(jnp.float32)
        )
        gated_mix = gated_mix.astype(jnp.bfloat16)
        if index + 1 < pieces:
            x_next, gated_mix = lax.optimization_barrier((x, gated_mix))
        gated.append(gated_mix)
        if pieces > 1:
            far.append(lax.ppermute(gated_mix, "ch", [(i, i ^ 2) for i in range(ch_count)]))
        if index + 1 < pieces and index >= 1:
            x_next, far[index - 1] = lax.optimization_barrier((x_next, far[index - 1]))
    if pieces == 1:
        return project(gated[0], out_weight).astype(jnp.bfloat16)
    return project_pieces(gated, far, out_weight).astype(jnp.bfloat16)


def project_pieces(gated, far, out_weight):
    ch_count = lax.axis_size("ch")
    offsets = [0]
    for value in gated:
        offsets.append(offsets[-1] + value.shape[1])
    width = offsets[-1]
    here = lax.axis_index("ch")
    other_core = [(i, i ^ 1) for i in range(ch_count)]
    other_chip = [(i, i ^ 2) for i in range(ch_count)]

    def part(value, owner, index):
        rows = lax.dynamic_slice_in_dim(out_weight, owner * width + offsets[index], value.shape[1], 0)
        return jnp.dot(value, rows, preferred_element_type=jnp.float32)

    far = list(far)
    own = jnp.concatenate(gated, 1)
    early = len(far) - 1
    own, early_far = lax.optimization_barrier((own, far[:early]))
    far[:early] = early_far
    near = lax.ppermute(own, "ch", other_core)
    near_far = [lax.ppermute(f, "ch", other_core) for f in far[:early]]
    rows_own = lax.dynamic_slice_in_dim(out_weight, here * width, width, 0)
    rows_near = lax.dynamic_slice_in_dim(out_weight, (here ^ 1) * width, width, 0)
    total = jnp.dot(own, rows_own, preferred_element_type=jnp.float32)
    for index in range(early):
        total = total + part(far[index], here ^ 2, index)
    total = total + jnp.dot(near, rows_near, preferred_element_type=jnp.float32)
    for index in range(early):
        total = total + part(near_far[index], here ^ 3, index)
    last = far[early]
    last, total = lax.optimization_barrier((last, total))
    near_last = lax.ppermute(last, "ch", other_core)
    total = total + part(last, here ^ 2, early)
    total = total + part(near_last, here ^ 3, early)
    return total


def solution(mesh):
    in_specs = (
        P(None, "ctx", "ch"),
        P(None, None, "ch"),
        P(None, "ch"),
        P(None, "ch"),
        P("ch"),
        P(None, "ch"),
    )
    out_specs = P("ctx", "ch")
    return jax.shard_map(shards, mesh=mesh, in_specs=in_specs, out_specs=out_specs, check_vma=False)
```

```python
import jax
import jax.numpy as jnp
from jax import lax
from jax.experimental import pallas as pl
from jax.experimental.pallas import tpu as pltpu
from jax.sharding import PartitionSpec as P

LANES = 128
SEGMENTS = 8


def shifted(value, axis, steps):
    count = lax.axis_size(axis)
    initial, last = (max(0, -steps), min(count, count - steps))
    return lax.ppermute(value, axis, [(source, source + steps) for source in range(initial, last)])


def segment_pass(x_ref, decay_ref, residue_ref, start_ref, y_ref, end_ref):
    pole_count = decay_ref.shape[0]
    segments = SEGMENTS
    span = x_ref.shape[0] // segments
    lanes = x_ref.shape[1]
    decays = [jnp.broadcast_to(decay_ref[p : p + 1, :], (segments, lanes)) for p in range(pole_count)]
    if residue_ref is not None:
        residues = [jnp.broadcast_to(residue_ref[p : p + 1, :], (segments, lanes)) for p in range(pole_count)]
    if start_ref is None:
        states = tuple(jnp.zeros((segments, lanes), jnp.float32) for _ in range(pole_count))
    else:
        states = tuple(start_ref[p] for p in range(pole_count))

    def body(t, states):
        x = x_ref[pl.ds(t, segments, stride=span), :]
        updated = []
        total = None
        for p in range(pole_count):
            h = decays[p] * states[p] + x
            updated.append(h)
            if y_ref is not None:
                term = residues[p] * h
                total = term if total is None else total + term
        if y_ref is not None:
            y_ref[pl.ds(t, segments, stride=span), :] = total
        return tuple(updated)

    states = lax.fori_loop(0, span, body, states, unroll=16)
    if end_ref is not None:
        for p in range(pole_count):
            end_ref[p] = states[p]


def end_state_kernel(x_ref, decay_ref, end_ref):
    segment_pass(x_ref, decay_ref, None, None, None, end_ref)


def recurrence_kernel(x_ref, decay_ref, residue_ref, start_ref, y_ref):
    segment_pass(x_ref, decay_ref, residue_ref, start_ref, y_ref, None)


def run_end_state(x, decay):
    length, width = x.shape
    pole_count = decay.shape[0]
    return pl.pallas_call(
        end_state_kernel,
        grid=(width // LANES,),
        in_specs=[
            pl.BlockSpec((length, LANES), lambda g: (0, g)),
            pl.BlockSpec((pole_count, LANES), lambda g: (0, g)),
        ],
        out_specs=pl.BlockSpec((pole_count, SEGMENTS, LANES), lambda g: (0, 0, g)),
        out_shape=jax.ShapeDtypeStruct((pole_count, SEGMENTS, width), jnp.float32),
    )(x, decay)


def run_recurrence(x, decay, residue, start, first_group, group_count):
    length = x.shape[0]
    pole_count = decay.shape[0]
    pole_spec = pl.BlockSpec((pole_count, LANES), lambda g: (0, g + first_group))
    return pl.pallas_call(
        recurrence_kernel,
        grid=(group_count,),
        in_specs=[
            pl.BlockSpec((length, LANES), lambda g: (0, g + first_group)),
            pole_spec,
            pole_spec,
            pl.BlockSpec((pole_count, SEGMENTS, LANES), lambda g: (0, 0, g + first_group)),
        ],
        out_specs=pl.BlockSpec((length, LANES), lambda g: (0, g)),
        out_shape=jax.ShapeDtypeStruct((length, group_count * LANES), jnp.float32),
    )(x, decay, residue, start)


def segment_starts(ends, incoming, pole_rates, span):
    segments = ends.shape[1]
    index = jnp.arange(segments, dtype=jnp.int32)
    gaps = (index[:, None] - 1 - index[None, :]).astype(jnp.float32)
    weights = jnp.where(
        (index[None, :] < index[:, None])[:, :, None, None],
        jnp.exp(-pole_rates[None, None] * (jnp.float32(span) * jnp.maximum(gaps, 0.0))[:, :, None, None]),
        jnp.float32(0.0),
    )
    carried = jnp.einsum("abpc,pbc->pac", weights, ends, precision=lax.Precision.HIGHEST)
    lead = jnp.exp(-pole_rates[:, None, :] * (jnp.float32(span) * index.astype(jnp.float32))[None, :, None])
    return carried + lead * incoming[:, None, :]


def device_end(ends, pole_rates, span):
    segments = ends.shape[1]
    index = jnp.arange(segments, dtype=jnp.float32)
    weights = jnp.exp(-pole_rates[:, None, :] * (jnp.float32(span) * (segments - 1 - index))[None, :, None])
    return jnp.sum(weights * ends, axis=1)


def incoming_state(local_end, pole_rates, row_count):
    ctx_count = lax.axis_size("ctx")
    total = jnp.zeros_like(local_end)
    for distance in range(1, ctx_count):
        received = shifted(local_end, "ctx", distance)
        total = total + jnp.exp(-pole_rates * jnp.float32(row_count * (distance - 1))) * received
    return total


def featurize(extended, tap_weights, stream, count):
    taps = tap_weights.shape[0]
    total = None
    for tap_index in range(taps):
        lead_row = taps - 1 - tap_index
        term = tap_weights[tap_index, stream].astype(jnp.float32)[None, :] * extended[
            stream, lead_row : lead_row + count
        ].astype(jnp.float32)
        total = term if total is None else total + term
    return total


def project(gated_mix, out_weight):
    ch_count = lax.axis_size("ch")
    width = gated_mix.shape[1]
    if ch_count != 4:
        gathered = lax.all_gather(gated_mix, "ch", axis=1, tiled=True)
        return jnp.dot(gathered, out_weight, preferred_element_type=jnp.float32)
    here = lax.axis_index("ch")

    def part(piece, owner):
        rows = lax.dynamic_slice_in_dim(out_weight, owner * width, width, 0)
        return jnp.dot(piece, rows, preferred_element_type=jnp.float32)

    far = lax.ppermute(gated_mix, "ch", [(i, i ^ 2) for i in range(ch_count)])
    near = lax.ppermute(gated_mix, "ch", [(i, i ^ 1) for i in range(ch_count)])
    total = part(gated_mix, here) + part(near, here ^ 1)
    far, total = lax.optimization_barrier((far, total))
    near_far = lax.ppermute(far, "ch", [(i, i ^ 1) for i in range(ch_count)])
    total = total + part(far, here ^ 2)
    return total + part(near_far, here ^ 3)


def shards(projected, tap_weights, pole_rates, residues, long_bias, out_weight):
    row_count = projected.shape[1]
    width = projected.shape[2]
    rows = width // LANES
    pole_count = pole_rates.shape[0]
    rim_rows = tap_weights.shape[0] - 1
    prior_rows = shifted(projected[:, row_count - rim_rows :], "ctx", 1)
    extended = jnp.concatenate([prior_rows, projected], 1)
    mixed_input = (
        featurize(extended, tap_weights, 1, row_count) * featurize(extended, tap_weights, 2, row_count)
    ).astype(jnp.bfloat16)
    x = mixed_input.astype(jnp.float32)
    span = row_count // SEGMENTS

    decay = jnp.exp(-pole_rates)
    ends = run_end_state(x, decay)
    start = incoming_state(device_end(ends, pole_rates, span), pole_rates, row_count)
    starts = segment_starts(ends, start, pole_rates, span)
    ch_count = lax.axis_size("ch")
    groups = width // LANES
    if ch_count == 4 and groups >= 8:
        bounds = [0, (2 * groups) // 8 * LANES, (5 * groups) // 8 * LANES, width]
    else:
        bounds = [0, width]
    pieces = len(bounds) - 1
    gated = []
    far = []
    x_next = x
    for index in range(pieces):
        cols = slice(bounds[index], bounds[index + 1])
        group_count = (cols.stop - cols.start) // LANES
        long_part = run_recurrence(x_next, decay, residues, starts, cols.start // LANES, group_count)
        long_mix = long_part.astype(jnp.bfloat16)
        stream0 = featurize(extended[:, :, cols], tap_weights[:, :, cols], 0, row_count)
        gated_mix = stream0 * (
            long_mix.astype(jnp.float32) + long_bias[None, cols] * mixed_input[:, cols].astype(jnp.float32)
        )
        gated_mix = gated_mix.astype(jnp.bfloat16)
        if index + 1 < pieces:
            x_next, gated_mix = lax.optimization_barrier((x, gated_mix))
        gated.append(gated_mix)
        if pieces > 1:
            far.append(lax.ppermute(gated_mix, "ch", [(i, i ^ 2) for i in range(ch_count)]))
        if index + 1 < pieces and index >= 1:
            x_next, far[index - 1] = lax.optimization_barrier((x_next, far[index - 1]))
    if pieces == 1:
        return project(gated[0], out_weight).astype(jnp.bfloat16)
    return project_pieces(gated, far, out_weight).astype(jnp.bfloat16)


def project_pieces(gated, far, out_weight):
    ch_count = lax.axis_size("ch")
    offsets = [0]
    for value in gated:
        offsets.append(offsets[-1] + value.shape[1])
    width = offsets[-1]
    here = lax.axis_index("ch")
    other_core = [(i, i ^ 1) for i in range(ch_count)]
    other_chip = [(i, i ^ 2) for i in range(ch_count)]

    def part(value, owner, index):
        rows = lax.dynamic_slice_in_dim(out_weight, owner * width + offsets[index], value.shape[1], 0)
        return jnp.dot(value, rows, preferred_element_type=jnp.float32)

    far = list(far)
    own = jnp.concatenate(gated, 1)
    early = len(far) - 1
    own, early_far = lax.optimization_barrier((own, far[:early]))
    far[:early] = early_far
    near = lax.ppermute(own, "ch", other_core)
    near_far = [lax.ppermute(f, "ch", other_core) for f in far[:early]]
    rows_own = lax.dynamic_slice_in_dim(out_weight, here * width, width, 0)
    rows_near = lax.dynamic_slice_in_dim(out_weight, (here ^ 1) * width, width, 0)
    total = jnp.dot(own, rows_own, preferred_element_type=jnp.float32)
    for index in range(early):
        total = total + part(far[index], here ^ 2, index)
    total = total + jnp.dot(near, rows_near, preferred_element_type=jnp.float32)
    for index in range(early):
        total = total + part(near_far[index], here ^ 3, index)
    last = far[early]
    last, total = lax.optimization_barrier((last, total))
    near_last = lax.ppermute(last, "ch", other_core)
    total = total + part(last, here ^ 2, early)
    total = total + part(near_last, here ^ 3, early)
    return total


def solution(mesh):
    in_specs = (
        P(None, "ctx", "ch"),
        P(None, None, "ch"),
        P(None, "ch"),
        P(None, "ch"),
        P("ch"),
        P(None, "ch"),
    )
    out_specs = P("ctx", "ch")
    return jax.shard_map(shards, mesh=mesh, in_specs=in_specs, out_specs=out_specs, check_vma=False)
```

```python
import jax
import jax.numpy as jnp
from jax import lax
from jax.experimental import pallas as pl
from jax.experimental.pallas import tpu as pltpu
from jax.sharding import PartitionSpec as P

LANES = 128
SEGMENTS = 8


def shifted(value, axis, steps):
    count = lax.axis_size(axis)
    initial, last = (max(0, -steps), min(count, count - steps))
    return lax.ppermute(value, axis, [(source, source + steps) for source in range(initial, last)])


def segment_pass(x_ref, decay_ref, residue_ref, start_ref, y_ref, end_ref):
    pole_count = decay_ref.shape[0]
    segments = SEGMENTS
    span = x_ref.shape[0] // segments
    lanes = x_ref.shape[1]
    decays = [jnp.broadcast_to(decay_ref[p : p + 1, :], (segments, lanes)) for p in range(pole_count)]
    if residue_ref is not None:
        residues = [jnp.broadcast_to(residue_ref[p : p + 1, :], (segments, lanes)) for p in range(pole_count)]
    if start_ref is None:
        states = tuple(jnp.zeros((segments, lanes), jnp.float32) for _ in range(pole_count))
    else:
        states = tuple(start_ref[p] for p in range(pole_count))

    def body(t, states):
        x = x_ref[pl.ds(t, segments, stride=span), :]
        updated = []
        terms = []
        for p in range(pole_count):
            h = decays[p] * states[p] + x
            updated.append(h)
            if y_ref is not None:
                terms.append(residues[p] * h)
        if y_ref is not None:
            while len(terms) > 1:
                terms = [terms[i] + terms[i + 1] if i + 1 < len(terms) else terms[i] for i in range(0, len(terms), 2)]
            y_ref[pl.ds(t, segments, stride=span), :] = terms[0]
        return tuple(updated)

    states = lax.fori_loop(0, span, body, states, unroll=16)
    if end_ref is not None:
        for p in range(pole_count):
            end_ref[p] = states[p]


def end_state_kernel(x_ref, decay_ref, end_ref):
    segment_pass(x_ref, decay_ref, None, None, None, end_ref)


def recurrence_kernel(x_ref, decay_ref, residue_ref, start_ref, y_ref):
    segment_pass(x_ref, decay_ref, residue_ref, start_ref, y_ref, None)


def run_end_state(x, decay):
    length, width = x.shape
    pole_count = decay.shape[0]
    return pl.pallas_call(
        end_state_kernel,
        grid=(width // LANES,),
        in_specs=[
            pl.BlockSpec((length, LANES), lambda g: (0, g)),
            pl.BlockSpec((pole_count, LANES), lambda g: (0, g)),
        ],
        out_specs=pl.BlockSpec((pole_count, SEGMENTS, LANES), lambda g: (0, 0, g)),
        out_shape=jax.ShapeDtypeStruct((pole_count, SEGMENTS, width), jnp.float32),
    )(x, decay)


def run_recurrence(x, decay, residue, start, first_group, group_count):
    length = x.shape[0]
    pole_count = decay.shape[0]
    pole_spec = pl.BlockSpec((pole_count, LANES), lambda g: (0, g + first_group))
    return pl.pallas_call(
        recurrence_kernel,
        grid=(group_count,),
        in_specs=[
            pl.BlockSpec((length, LANES), lambda g: (0, g + first_group)),
            pole_spec,
            pole_spec,
            pl.BlockSpec((pole_count, SEGMENTS, LANES), lambda g: (0, 0, g + first_group)),
        ],
        out_specs=pl.BlockSpec((length, LANES), lambda g: (0, g)),
        out_shape=jax.ShapeDtypeStruct((length, group_count * LANES), jnp.float32),
    )(x, decay, residue, start)


def segment_starts(ends, incoming, pole_rates, span):
    segments = ends.shape[1]
    index = jnp.arange(segments, dtype=jnp.int32)
    gaps = (index[:, None] - 1 - index[None, :]).astype(jnp.float32)
    weights = jnp.where(
        (index[None, :] < index[:, None])[:, :, None, None],
        jnp.exp(-pole_rates[None, None] * (jnp.float32(span) * jnp.maximum(gaps, 0.0))[:, :, None, None]),
        jnp.float32(0.0),
    )
    carried = jnp.einsum("abpc,pbc->pac", weights, ends, precision=lax.Precision.HIGHEST)
    lead = jnp.exp(-pole_rates[:, None, :] * (jnp.float32(span) * index.astype(jnp.float32))[None, :, None])
    return carried + lead * incoming[:, None, :]


def device_end(ends, pole_rates, span):
    segments = ends.shape[1]
    index = jnp.arange(segments, dtype=jnp.float32)
    weights = jnp.exp(-pole_rates[:, None, :] * (jnp.float32(span) * (segments - 1 - index))[None, :, None])
    return jnp.sum(weights * ends, axis=1)


def incoming_state(local_end, pole_rates, row_count):
    ctx_count = lax.axis_size("ctx")
    total = jnp.zeros_like(local_end)
    for distance in range(1, ctx_count):
        received = shifted(local_end, "ctx", distance)
        total = total + jnp.exp(-pole_rates * jnp.float32(row_count * (distance - 1))) * received
    return total


def featurize(extended, tap_weights, stream, count):
    taps = tap_weights.shape[0]
    total = None
    for tap_index in range(taps):
        lead_row = taps - 1 - tap_index
        term = tap_weights[tap_index, stream].astype(jnp.float32)[None, :] * extended[
            stream, lead_row : lead_row + count
        ].astype(jnp.float32)
        total = term if total is None else total + term
    return total


def project(gated_mix, out_weight):
    ch_count = lax.axis_size("ch")
    width = gated_mix.shape[1]
    if ch_count != 4:
        gathered = lax.all_gather(gated_mix, "ch", axis=1, tiled=True)
        return jnp.dot(gathered, out_weight, preferred_element_type=jnp.float32)
    here = lax.axis_index("ch")

    def part(piece, owner):
        rows = lax.dynamic_slice_in_dim(out_weight, owner * width, width, 0)
        return jnp.dot(piece, rows, preferred_element_type=jnp.float32)

    far = lax.ppermute(gated_mix, "ch", [(i, i ^ 2) for i in range(ch_count)])
    near = lax.ppermute(gated_mix, "ch", [(i, i ^ 1) for i in range(ch_count)])
    total = part(gated_mix, here) + part(near, here ^ 1)
    far, total = lax.optimization_barrier((far, total))
    near_far = lax.ppermute(far, "ch", [(i, i ^ 1) for i in range(ch_count)])
    total = total + part(far, here ^ 2)
    return total + part(near_far, here ^ 3)


def shards(projected, tap_weights, pole_rates, residues, long_bias, out_weight):
    row_count = projected.shape[1]
    width = projected.shape[2]
    rows = width // LANES
    pole_count = pole_rates.shape[0]
    rim_rows = tap_weights.shape[0] - 1
    prior_rows = shifted(projected[:, row_count - rim_rows :], "ctx", 1)
    extended = jnp.concatenate([prior_rows, projected], 1)
    mixed_input = (
        featurize(extended, tap_weights, 1, row_count) * featurize(extended, tap_weights, 2, row_count)
    ).astype(jnp.bfloat16)
    x = mixed_input.astype(jnp.float32)
    span = row_count // SEGMENTS

    decay = jnp.exp(-pole_rates)
    ends = run_end_state(x, decay)
    start = incoming_state(device_end(ends, pole_rates, span), pole_rates, row_count)
    starts = segment_starts(ends, start, pole_rates, span)
    ch_count = lax.axis_size("ch")
    groups = width // LANES
    if ch_count == 4 and groups >= 8:
        bounds = [0, (2 * groups) // 8 * LANES, (5 * groups) // 8 * LANES, width]
    else:
        bounds = [0, width]
    pieces = len(bounds) - 1
    gated = []
    far = []
    x_next = x
    for index in range(pieces):
        cols = slice(bounds[index], bounds[index + 1])
        group_count = (cols.stop - cols.start) // LANES
        long_part = run_recurrence(x_next, decay, residues, starts, cols.start // LANES, group_count)
        long_mix = long_part.astype(jnp.bfloat16)
        stream0 = featurize(extended[:, :, cols], tap_weights[:, :, cols], 0, row_count)
        gated_mix = stream0 * (
            long_mix.astype(jnp.float32) + long_bias[None, cols] * mixed_input[:, cols].astype(jnp.float32)
        )
        gated_mix = gated_mix.astype(jnp.bfloat16)
        if index + 1 < pieces:
            x_next, gated_mix = lax.optimization_barrier((x, gated_mix))
        gated.append(gated_mix)
        if pieces > 1:
            far.append(lax.ppermute(gated_mix, "ch", [(i, i ^ 2) for i in range(ch_count)]))
        if index + 1 < pieces and index >= 1:
            x_next, far[index - 1] = lax.optimization_barrier((x_next, far[index - 1]))
    if pieces == 1:
        return project(gated[0], out_weight).astype(jnp.bfloat16)
    return project_pieces(gated, far, out_weight).astype(jnp.bfloat16)


def project_pieces(gated, far, out_weight):
    ch_count = lax.axis_size("ch")
    offsets = [0]
    for value in gated:
        offsets.append(offsets[-1] + value.shape[1])
    width = offsets[-1]
    here = lax.axis_index("ch")
    other_core = [(i, i ^ 1) for i in range(ch_count)]
    other_chip = [(i, i ^ 2) for i in range(ch_count)]

    def part(value, owner, index):
        rows = lax.dynamic_slice_in_dim(out_weight, owner * width + offsets[index], value.shape[1], 0)
        return jnp.dot(value, rows, preferred_element_type=jnp.float32)

    far = list(far)
    own = jnp.concatenate(gated, 1)
    early = len(far) - 1
    own, early_far = lax.optimization_barrier((own, far[:early]))
    far[:early] = early_far
    near = lax.ppermute(own, "ch", other_core)
    near_far = [lax.ppermute(f, "ch", other_core) for f in far[:early]]
    rows_own = lax.dynamic_slice_in_dim(out_weight, here * width, width, 0)
    rows_near = lax.dynamic_slice_in_dim(out_weight, (here ^ 1) * width, width, 0)
    total = jnp.dot(own, rows_own, preferred_element_type=jnp.float32)
    for index in range(early):
        total = total + part(far[index], here ^ 2, index)
    total = total + jnp.dot(near, rows_near, preferred_element_type=jnp.float32)
    for index in range(early):
        total = total + part(near_far[index], here ^ 3, index)
    last = far[early]
    last, total = lax.optimization_barrier((last, total))
    near_last = lax.ppermute(last, "ch", other_core)
    total = total + part(last, here ^ 2, early)
    total = total + part(near_last, here ^ 3, early)
    return total


def solution(mesh):
    in_specs = (
        P(None, "ctx", "ch"),
        P(None, None, "ch"),
        P(None, "ch"),
        P(None, "ch"),
        P("ch"),
        P(None, "ch"),
    )
    out_specs = P("ctx", "ch")
    return jax.shard_map(shards, mesh=mesh, in_specs=in_specs, out_specs=out_specs, check_vma=False)
```

```python
import jax
import jax.numpy as jnp
from jax import lax
from jax.experimental import pallas as pl
from jax.experimental.pallas import tpu as pltpu
from jax.sharding import PartitionSpec as P

LANES = 128
SEGMENTS = 8


def shifted(value, axis, steps):
    count = lax.axis_size(axis)
    initial, last = (max(0, -steps), min(count, count - steps))
    return lax.ppermute(value, axis, [(source, source + steps) for source in range(initial, last)])


def segment_pass(x_ref, decay_ref, residue_ref, start_ref, y_ref, end_ref):
    pole_count = decay_ref.shape[0]
    segments = SEGMENTS
    span = x_ref.shape[0] // segments
    lanes = x_ref.shape[1]
    decays = [jnp.broadcast_to(decay_ref[p : p + 1, :], (segments, lanes)) for p in range(pole_count)]
    if residue_ref is not None:
        residues = [jnp.broadcast_to(residue_ref[p : p + 1, :], (segments, lanes)) for p in range(pole_count)]
    if start_ref is None:
        states = tuple(jnp.zeros((segments, lanes), jnp.float32) for _ in range(pole_count))
    else:
        states = tuple(start_ref[p] for p in range(pole_count))

    def body(t, states):
        x = x_ref[pl.ds(t, segments, stride=span), :]
        updated = []
        total = None
        for p in range(pole_count):
            h = decays[p] * states[p] + x
            updated.append(h)
            if y_ref is not None:
                term = residues[p] * h
                total = term if total is None else total + term
        if y_ref is not None:
            y_ref[pl.ds(t, segments, stride=span), :] = total
        return tuple(updated)

    states = lax.fori_loop(0, span, body, states, unroll=16)
    if end_ref is not None:
        for p in range(pole_count):
            end_ref[p] = states[p]


def end_state_kernel(x_ref, decay_ref, end_ref):
    segment_pass(x_ref, decay_ref, None, None, None, end_ref)


def recurrence_kernel(x_ref, decay_ref, residue_ref, start_ref, y_ref):
    segment_pass(x_ref, decay_ref, residue_ref, start_ref, y_ref, None)


def run_end_state(x, decay):
    length, width = x.shape
    pole_count = decay.shape[0]
    return pl.pallas_call(
        end_state_kernel,
        grid=(width // LANES,),
        in_specs=[
            pl.BlockSpec((length, LANES), lambda g: (0, g)),
            pl.BlockSpec((pole_count, LANES), lambda g: (0, g)),
        ],
        out_specs=pl.BlockSpec((pole_count, SEGMENTS, LANES), lambda g: (0, 0, g)),
        out_shape=jax.ShapeDtypeStruct((pole_count, SEGMENTS, width), jnp.float32),
    )(x, decay)


def run_recurrence(x, decay, residue, start, first_group, group_count):
    length = x.shape[0]
    pole_count = decay.shape[0]
    pole_spec = pl.BlockSpec((pole_count, LANES), lambda g: (0, g + first_group))
    return pl.pallas_call(
        recurrence_kernel,
        grid=(group_count,),
        in_specs=[
            pl.BlockSpec((length, LANES), lambda g: (0, g + first_group)),
            pole_spec,
            pole_spec,
            pl.BlockSpec((pole_count, SEGMENTS, LANES), lambda g: (0, 0, g + first_group)),
        ],
        out_specs=pl.BlockSpec((length, LANES), lambda g: (0, g)),
        out_shape=jax.ShapeDtypeStruct((length, group_count * LANES), jnp.float32),
    )(x, decay, residue, start)


def segment_starts(ends, incoming, pole_rates, span):
    segments = ends.shape[1]
    index = jnp.arange(segments, dtype=jnp.int32)
    gaps = (index[:, None] - 1 - index[None, :]).astype(jnp.float32)
    weights = jnp.where(
        (index[None, :] < index[:, None])[:, :, None, None],
        jnp.exp(-pole_rates[None, None] * (jnp.float32(span) * jnp.maximum(gaps, 0.0))[:, :, None, None]),
        jnp.float32(0.0),
    )
    carried = jnp.einsum("abpc,pbc->pac", weights, ends, precision=lax.Precision.HIGHEST)
    lead = jnp.exp(-pole_rates[:, None, :] * (jnp.float32(span) * index.astype(jnp.float32))[None, :, None])
    return carried + lead * incoming[:, None, :]


def device_end(ends, pole_rates, span):
    segments = ends.shape[1]
    index = jnp.arange(segments, dtype=jnp.float32)
    weights = jnp.exp(-pole_rates[:, None, :] * (jnp.float32(span) * (segments - 1 - index))[None, :, None])
    return jnp.sum(weights * ends, axis=1)


def incoming_state(local_end, pole_rates, row_count):
    ctx_count = lax.axis_size("ctx")
    total = jnp.zeros_like(local_end)
    for distance in range(1, ctx_count):
        received = shifted(local_end, "ctx", distance)
        total = total + jnp.exp(-pole_rates * jnp.float32(row_count * (distance - 1))) * received
    return total


def featurize(extended, tap_weights, stream, count):
    taps = tap_weights.shape[0]
    total = None
    for tap_index in range(taps):
        lead_row = taps - 1 - tap_index
        term = tap_weights[tap_index, stream].astype(jnp.float32)[None, :] * extended[
            stream, lead_row : lead_row + count
        ].astype(jnp.float32)
        total = term if total is None else total + term
    return total


def project(gated_mix, out_weight):
    ch_count = lax.axis_size("ch")
    width = gated_mix.shape[1]
    if ch_count != 4:
        gathered = lax.all_gather(gated_mix, "ch", axis=1, tiled=True)
        return jnp.dot(gathered, out_weight, preferred_element_type=jnp.float32)
    here = lax.axis_index("ch")

    def part(piece, owner):
        rows = lax.dynamic_slice_in_dim(out_weight, owner * width, width, 0)
        return jnp.dot(piece, rows, preferred_element_type=jnp.float32)

    far = lax.ppermute(gated_mix, "ch", [(i, i ^ 2) for i in range(ch_count)])
    near = lax.ppermute(gated_mix, "ch", [(i, i ^ 1) for i in range(ch_count)])
    total = part(gated_mix, here) + part(near, here ^ 1)
    far, total = lax.optimization_barrier((far, total))
    near_far = lax.ppermute(far, "ch", [(i, i ^ 1) for i in range(ch_count)])
    total = total + part(far, here ^ 2)
    return total + part(near_far, here ^ 3)


def shards(projected, tap_weights, pole_rates, residues, long_bias, out_weight):
    row_count = projected.shape[1]
    width = projected.shape[2]
    rows = width // LANES
    pole_count = pole_rates.shape[0]
    rim_rows = tap_weights.shape[0] - 1
    prior_rows = shifted(projected[:, row_count - rim_rows :], "ctx", 1)
    extended = jnp.concatenate([prior_rows, projected], 1)
    widened = lax.optimization_barrier(extended[1:3].astype(jnp.float32))
    mixed_input = (
        featurize(widened, tap_weights[:, 1:3], 0, row_count) * featurize(widened, tap_weights[:, 1:3], 1, row_count)
    ).astype(jnp.bfloat16)
    x = mixed_input.astype(jnp.float32)
    span = row_count // SEGMENTS

    decay = jnp.exp(-pole_rates)
    ends = run_end_state(x, decay)
    start = incoming_state(device_end(ends, pole_rates, span), pole_rates, row_count)
    starts = segment_starts(ends, start, pole_rates, span)
    ch_count = lax.axis_size("ch")
    groups = width // LANES
    if ch_count == 4 and groups >= 8:
        bounds = [0, (2 * groups) // 8 * LANES, (5 * groups) // 8 * LANES, width]
    else:
        bounds = [0, width]
    pieces = len(bounds) - 1
    gated = []
    far = []
    x_next = x
    for index in range(pieces):
        cols = slice(bounds[index], bounds[index + 1])
        group_count = (cols.stop - cols.start) // LANES
        long_part = run_recurrence(x_next, decay, residues, starts, cols.start // LANES, group_count)
        long_mix = long_part.astype(jnp.bfloat16)
        stream0 = featurize(extended[:, :, cols], tap_weights[:, :, cols], 0, row_count)
        gated_mix = stream0 * (
            long_mix.astype(jnp.float32) + long_bias[None, cols] * mixed_input[:, cols].astype(jnp.float32)
        )
        gated_mix = gated_mix.astype(jnp.bfloat16)
        if index + 1 < pieces:
            x_next, gated_mix = lax.optimization_barrier((x, gated_mix))
        gated.append(gated_mix)
        if pieces > 1:
            far.append(lax.ppermute(gated_mix, "ch", [(i, i ^ 2) for i in range(ch_count)]))
        if index + 1 < pieces and index >= 1:
            x_next, far[index - 1] = lax.optimization_barrier((x_next, far[index - 1]))
    if pieces == 1:
        return project(gated[0], out_weight).astype(jnp.bfloat16)
    return project_pieces(gated, far, out_weight).astype(jnp.bfloat16)


def project_pieces(gated, far, out_weight):
    ch_count = lax.axis_size("ch")
    offsets = [0]
    for value in gated:
        offsets.append(offsets[-1] + value.shape[1])
    width = offsets[-1]
    here = lax.axis_index("ch")
    other_core = [(i, i ^ 1) for i in range(ch_count)]
    other_chip = [(i, i ^ 2) for i in range(ch_count)]

    def part(value, owner, index):
        rows = lax.dynamic_slice_in_dim(out_weight, owner * width + offsets[index], value.shape[1], 0)
        return jnp.dot(value, rows, preferred_element_type=jnp.float32)

    far = list(far)
    own = jnp.concatenate(gated, 1)
    early = len(far) - 1
    own, early_far = lax.optimization_barrier((own, far[:early]))
    far[:early] = early_far
    near = lax.ppermute(own, "ch", other_core)
    near_far = [lax.ppermute(f, "ch", other_core) for f in far[:early]]
    rows_own = lax.dynamic_slice_in_dim(out_weight, here * width, width, 0)
    rows_near = lax.dynamic_slice_in_dim(out_weight, (here ^ 1) * width, width, 0)
    total = jnp.dot(own, rows_own, preferred_element_type=jnp.float32)
    for index in range(early):
        total = total + part(far[index], here ^ 2, index)
    total = total + jnp.dot(near, rows_near, preferred_element_type=jnp.float32)
    for index in range(early):
        total = total + part(near_far[index], here ^ 3, index)
    last = far[early]
    last, total = lax.optimization_barrier((last, total))
    near_last = lax.ppermute(last, "ch", other_core)
    total = total + part(last, here ^ 2, early)
    total = total + part(near_last, here ^ 3, early)
    return total


def solution(mesh):
    in_specs = (
        P(None, "ctx", "ch"),
        P(None, None, "ch"),
        P(None, "ch"),
        P(None, "ch"),
        P("ch"),
        P(None, "ch"),
    )
    out_specs = P("ctx", "ch")
    return jax.shard_map(shards, mesh=mesh, in_specs=in_specs, out_specs=out_specs, check_vma=False)
```

```python
import jax
import jax.numpy as jnp
from jax import lax
from jax.experimental import pallas as pl
from jax.experimental.pallas import tpu as pltpu
from jax.sharding import PartitionSpec as P

LANES = 128
SEGMENTS = 8


def shifted(value, axis, steps):
    count = lax.axis_size(axis)
    initial, last = (max(0, -steps), min(count, count - steps))
    return lax.ppermute(value, axis, [(source, source + steps) for source in range(initial, last)])


def segment_pass(x_ref, decay_ref, residue_ref, start_ref, y_ref, end_ref):
    pole_count = decay_ref.shape[0]
    segments = SEGMENTS
    span = x_ref.shape[0] // segments
    lanes = x_ref.shape[1]
    decays = [jnp.broadcast_to(decay_ref[p : p + 1, :], (segments, lanes)) for p in range(pole_count)]
    if residue_ref is not None:
        residues = [jnp.broadcast_to(residue_ref[p : p + 1, :], (segments, lanes)) for p in range(pole_count)]
    if start_ref is None:
        states = tuple(jnp.zeros((segments, lanes), jnp.float32) for _ in range(pole_count))
    else:
        states = tuple(start_ref[p] for p in range(pole_count))

    def body(t, states):
        x = x_ref[pl.ds(t, segments, stride=span), :]
        updated = []
        total = None
        for p in range(pole_count):
            h = decays[p] * states[p] + x
            updated.append(h)
            if y_ref is not None:
                term = residues[p] * h
                total = term if total is None else total + term
        if y_ref is not None:
            y_ref[pl.ds(t, segments, stride=span), :] = total
        return tuple(updated)

    states = lax.fori_loop(0, span, body, states, unroll=16)
    if end_ref is not None:
        for p in range(pole_count):
            end_ref[p] = states[p]


def end_state_kernel(x_ref, decay_ref, end_ref):
    segment_pass(x_ref, decay_ref, None, None, None, end_ref)


def recurrence_kernel(x_ref, decay_ref, residue_ref, start_ref, y_ref):
    segment_pass(x_ref, decay_ref, residue_ref, start_ref, y_ref, None)


def run_end_state(x, decay):
    length, width = x.shape
    pole_count = decay.shape[0]
    return pl.pallas_call(
        end_state_kernel,
        grid=(width // LANES,),
        in_specs=[
            pl.BlockSpec((length, LANES), lambda g: (0, g)),
            pl.BlockSpec((pole_count, LANES), lambda g: (0, g)),
        ],
        out_specs=pl.BlockSpec((pole_count, SEGMENTS, LANES), lambda g: (0, 0, g)),
        out_shape=jax.ShapeDtypeStruct((pole_count, SEGMENTS, width), jnp.float32),
    )(x, decay)


def run_recurrence(x, decay, residue, start, first_group, group_count):
    length = x.shape[0]
    pole_count = decay.shape[0]
    pole_spec = pl.BlockSpec((pole_count, LANES), lambda g: (0, g + first_group))
    return pl.pallas_call(
        recurrence_kernel,
        grid=(group_count,),
        in_specs=[
            pl.BlockSpec((length, LANES), lambda g: (0, g + first_group)),
            pole_spec,
            pole_spec,
            pl.BlockSpec((pole_count, SEGMENTS, LANES), lambda g: (0, 0, g + first_group)),
        ],
        out_specs=pl.BlockSpec((length, LANES), lambda g: (0, g)),
        out_shape=jax.ShapeDtypeStruct((length, group_count * LANES), jnp.float32),
    )(x, decay, residue, start)


def segment_starts(ends, incoming, pole_rates, span):
    segments = ends.shape[1]
    index = jnp.arange(segments, dtype=jnp.int32)
    gaps = (index[:, None] - 1 - index[None, :]).astype(jnp.float32)
    weights = jnp.where(
        (index[None, :] < index[:, None])[:, :, None, None],
        jnp.exp(-pole_rates[None, None] * (jnp.float32(span) * jnp.maximum(gaps, 0.0))[:, :, None, None]),
        jnp.float32(0.0),
    )
    carried = jnp.einsum("abpc,pbc->pac", weights, ends, precision=lax.Precision.HIGHEST)
    lead = jnp.exp(-pole_rates[:, None, :] * (jnp.float32(span) * index.astype(jnp.float32))[None, :, None])
    return carried + lead * incoming[:, None, :]


def device_end(ends, pole_rates, span):
    segments = ends.shape[1]
    index = jnp.arange(segments, dtype=jnp.float32)
    weights = jnp.exp(-pole_rates[:, None, :] * (jnp.float32(span) * (segments - 1 - index))[None, :, None])
    return jnp.sum(weights * ends, axis=1)


def incoming_state(local_end, pole_rates, row_count):
    ctx_count = lax.axis_size("ctx")
    total = jnp.zeros_like(local_end)
    for distance in range(1, ctx_count):
        received = shifted(local_end, "ctx", distance)
        total = total + jnp.exp(-pole_rates * jnp.float32(row_count * (distance - 1))) * received
    return total


def featurize(extended, tap_weights, stream, count):
    taps = tap_weights.shape[0]
    total = None
    for tap_index in range(taps):
        lead_row = taps - 1 - tap_index
        term = tap_weights[tap_index, stream].astype(jnp.float32)[None, :] * extended[
            stream, lead_row : lead_row + count
        ].astype(jnp.float32)
        total = term if total is None else total + term
    return total


def project(gated_mix, out_weight):
    ch_count = lax.axis_size("ch")
    width = gated_mix.shape[1]
    if ch_count != 4:
        gathered = lax.all_gather(gated_mix, "ch", axis=1, tiled=True)
        return jnp.dot(gathered, out_weight, preferred_element_type=jnp.float32)
    here = lax.axis_index("ch")

    def part(piece, owner):
        rows = lax.dynamic_slice_in_dim(out_weight, owner * width, width, 0)
        return jnp.dot(piece, rows, preferred_element_type=jnp.float32)

    far = lax.ppermute(gated_mix, "ch", [(i, i ^ 2) for i in range(ch_count)])
    near = lax.ppermute(gated_mix, "ch", [(i, i ^ 1) for i in range(ch_count)])
    total = part(gated_mix, here) + part(near, here ^ 1)
    far, total = lax.optimization_barrier((far, total))
    near_far = lax.ppermute(far, "ch", [(i, i ^ 1) for i in range(ch_count)])
    total = total + part(far, here ^ 2)
    return total + part(near_far, here ^ 3)


def shards(projected, tap_weights, pole_rates, residues, long_bias, out_weight):
    row_count = projected.shape[1]
    width = projected.shape[2]
    rows = width // LANES
    pole_count = pole_rates.shape[0]
    rim_rows = tap_weights.shape[0] - 1
    prior_rows = shifted(projected[:, row_count - rim_rows :], "ctx", 1)
    extended = jnp.concatenate([prior_rows, projected], 1)
    widened = lax.optimization_barrier(extended[1:3].astype(jnp.float32))
    mixed_input = (
        featurize(widened, tap_weights[:, 1:3], 0, row_count) * featurize(widened, tap_weights[:, 1:3], 1, row_count)
    ).astype(jnp.bfloat16)
    x = mixed_input.astype(jnp.float32)
    span = row_count // SEGMENTS

    decay = jnp.exp(-pole_rates)
    ends = run_end_state(x, decay)
    start = incoming_state(device_end(ends, pole_rates, span), pole_rates, row_count)
    starts = segment_starts(ends, start, pole_rates, span)
    ch_count = lax.axis_size("ch")
    groups = width // LANES
    if ch_count == 4 and groups >= 8:
        bounds = [0, (2 * groups) // 8 * LANES, (5 * groups) // 8 * LANES, width]
    else:
        bounds = [0, width]
    pieces = len(bounds) - 1
    widened0 = lax.optimization_barrier(extended[0:1].astype(jnp.float32))
    gated = []
    far = []
    x_next = x
    for index in range(pieces):
        cols = slice(bounds[index], bounds[index + 1])
        group_count = (cols.stop - cols.start) // LANES
        long_part = run_recurrence(x_next, decay, residues, starts, cols.start // LANES, group_count)
        long_mix = long_part.astype(jnp.bfloat16)
        stream0 = featurize(widened0[:, :, cols], tap_weights[:, 0:1, cols], 0, row_count)
        gated_mix = stream0 * (
            long_mix.astype(jnp.float32) + long_bias[None, cols] * mixed_input[:, cols].astype(jnp.float32)
        )
        gated_mix = gated_mix.astype(jnp.bfloat16)
        if index + 1 < pieces:
            x_next, gated_mix = lax.optimization_barrier((x, gated_mix))
        gated.append(gated_mix)
        if pieces > 1:
            far.append(lax.ppermute(gated_mix, "ch", [(i, i ^ 2) for i in range(ch_count)]))
        if index + 1 < pieces and index >= 1:
            x_next, far[index - 1] = lax.optimization_barrier((x_next, far[index - 1]))
    if pieces == 1:
        return project(gated[0], out_weight).astype(jnp.bfloat16)
    return project_pieces(gated, far, out_weight).astype(jnp.bfloat16)


def project_pieces(gated, far, out_weight):
    ch_count = lax.axis_size("ch")
    offsets = [0]
    for value in gated:
        offsets.append(offsets[-1] + value.shape[1])
    width = offsets[-1]
    here = lax.axis_index("ch")
    other_core = [(i, i ^ 1) for i in range(ch_count)]
    other_chip = [(i, i ^ 2) for i in range(ch_count)]

    def part(value, owner, index):
        rows = lax.dynamic_slice_in_dim(out_weight, owner * width + offsets[index], value.shape[1], 0)
        return jnp.dot(value, rows, preferred_element_type=jnp.float32)

    far = list(far)
    own = jnp.concatenate(gated, 1)
    early = len(far) - 1
    own, early_far = lax.optimization_barrier((own, far[:early]))
    far[:early] = early_far
    near = lax.ppermute(own, "ch", other_core)
    near_far = [lax.ppermute(f, "ch", other_core) for f in far[:early]]
    rows_own = lax.dynamic_slice_in_dim(out_weight, here * width, width, 0)
    rows_near = lax.dynamic_slice_in_dim(out_weight, (here ^ 1) * width, width, 0)
    total = jnp.dot(own, rows_own, preferred_element_type=jnp.float32)
    for index in range(early):
        total = total + part(far[index], here ^ 2, index)
    total = total + jnp.dot(near, rows_near, preferred_element_type=jnp.float32)
    for index in range(early):
        total = total + part(near_far[index], here ^ 3, index)
    last = far[early]
    last, total = lax.optimization_barrier((last, total))
    near_last = lax.ppermute(last, "ch", other_core)
    total = total + part(last, here ^ 2, early)
    total = total + part(near_last, here ^ 3, early)
    return total


def solution(mesh):
    in_specs = (
        P(None, "ctx", "ch"),
        P(None, None, "ch"),
        P(None, "ch"),
        P(None, "ch"),
        P("ch"),
        P(None, "ch"),
    )
    out_specs = P("ctx", "ch")
    return jax.shard_map(shards, mesh=mesh, in_specs=in_specs, out_specs=out_specs, check_vma=False)
```

```python
import jax
import jax.numpy as jnp
from jax import lax
from jax.experimental import pallas as pl
from jax.experimental.pallas import tpu as pltpu
from jax.sharding import PartitionSpec as P

LANES = 128
SEGMENTS = 8


def shifted(value, axis, steps):
    count = lax.axis_size(axis)
    initial, last = (max(0, -steps), min(count, count - steps))
    return lax.ppermute(value, axis, [(source, source + steps) for source in range(initial, last)])


def segment_pass(x_ref, decay_ref, residue_ref, start_ref, y_ref, end_ref):
    pole_count = decay_ref.shape[0]
    segments = SEGMENTS
    span = x_ref.shape[0] // segments
    lanes = x_ref.shape[1]
    decays = [jnp.broadcast_to(decay_ref[p : p + 1, :], (segments, lanes)) for p in range(pole_count)]
    if residue_ref is not None:
        residues = [jnp.broadcast_to(residue_ref[p : p + 1, :], (segments, lanes)) for p in range(pole_count)]
    if start_ref is None:
        states = tuple(jnp.zeros((segments, lanes), jnp.float32) for _ in range(pole_count))
    else:
        states = tuple(start_ref[p] for p in range(pole_count))

    def body(t, states):
        x = x_ref[pl.ds(t, segments, stride=span), :]
        updated = []
        total = None
        for p in range(pole_count):
            h = decays[p] * states[p] + x
            updated.append(h)
            if y_ref is not None:
                term = residues[p] * h
                total = term if total is None else total + term
        if y_ref is not None:
            y_ref[pl.ds(t, segments, stride=span), :] = total
        return tuple(updated)

    states = lax.fori_loop(0, span, body, states, unroll=32)
    if end_ref is not None:
        for p in range(pole_count):
            end_ref[p] = states[p]


def end_state_kernel(x_ref, decay_ref, end_ref):
    segment_pass(x_ref, decay_ref, None, None, None, end_ref)


def recurrence_kernel(x_ref, decay_ref, residue_ref, start_ref, y_ref):
    segment_pass(x_ref, decay_ref, residue_ref, start_ref, y_ref, None)


def run_end_state(x, decay):
    length, width = x.shape
    pole_count = decay.shape[0]
    return pl.pallas_call(
        end_state_kernel,
        grid=(width // LANES,),
        in_specs=[
            pl.BlockSpec((length, LANES), lambda g: (0, g)),
            pl.BlockSpec((pole_count, LANES), lambda g: (0, g)),
        ],
        out_specs=pl.BlockSpec((pole_count, SEGMENTS, LANES), lambda g: (0, 0, g)),
        out_shape=jax.ShapeDtypeStruct((pole_count, SEGMENTS, width), jnp.float32),
    )(x, decay)


def run_recurrence(x, decay, residue, start, first_group, group_count):
    length = x.shape[0]
    pole_count = decay.shape[0]
    pole_spec = pl.BlockSpec((pole_count, LANES), lambda g: (0, g + first_group))
    return pl.pallas_call(
        recurrence_kernel,
        grid=(group_count,),
        in_specs=[
            pl.BlockSpec((length, LANES), lambda g: (0, g + first_group)),
            pole_spec,
            pole_spec,
            pl.BlockSpec((pole_count, SEGMENTS, LANES), lambda g: (0, 0, g + first_group)),
        ],
        out_specs=pl.BlockSpec((length, LANES), lambda g: (0, g)),
        out_shape=jax.ShapeDtypeStruct((length, group_count * LANES), jnp.float32),
    )(x, decay, residue, start)


def segment_starts(ends, incoming, pole_rates, span):
    segments = ends.shape[1]
    index = jnp.arange(segments, dtype=jnp.int32)
    gaps = (index[:, None] - 1 - index[None, :]).astype(jnp.float32)
    weights = jnp.where(
        (index[None, :] < index[:, None])[:, :, None, None],
        jnp.exp(-pole_rates[None, None] * (jnp.float32(span) * jnp.maximum(gaps, 0.0))[:, :, None, None]),
        jnp.float32(0.0),
    )
    carried = jnp.einsum("abpc,pbc->pac", weights, ends, precision=lax.Precision.HIGHEST)
    lead = jnp.exp(-pole_rates[:, None, :] * (jnp.float32(span) * index.astype(jnp.float32))[None, :, None])
    return carried + lead * incoming[:, None, :]


def device_end(ends, pole_rates, span):
    segments = ends.shape[1]
    index = jnp.arange(segments, dtype=jnp.float32)
    weights = jnp.exp(-pole_rates[:, None, :] * (jnp.float32(span) * (segments - 1 - index))[None, :, None])
    return jnp.sum(weights * ends, axis=1)


def incoming_state(local_end, pole_rates, row_count):
    ctx_count = lax.axis_size("ctx")
    total = jnp.zeros_like(local_end)
    for distance in range(1, ctx_count):
        received = shifted(local_end, "ctx", distance)
        total = total + jnp.exp(-pole_rates * jnp.float32(row_count * (distance - 1))) * received
    return total


def featurize(extended, tap_weights, stream, count):
    taps = tap_weights.shape[0]
    total = None
    for tap_index in range(taps):
        lead_row = taps - 1 - tap_index
        term = tap_weights[tap_index, stream].astype(jnp.float32)[None, :] * extended[
            stream, lead_row : lead_row + count
        ].astype(jnp.float32)
        total = term if total is None else total + term
    return total


def project(gated_mix, out_weight):
    ch_count = lax.axis_size("ch")
    width = gated_mix.shape[1]
    if ch_count != 4:
        gathered = lax.all_gather(gated_mix, "ch", axis=1, tiled=True)
        return jnp.dot(gathered, out_weight, preferred_element_type=jnp.float32)
    here = lax.axis_index("ch")

    def part(piece, owner):
        rows = lax.dynamic_slice_in_dim(out_weight, owner * width, width, 0)
        return jnp.dot(piece, rows, preferred_element_type=jnp.float32)

    far = lax.ppermute(gated_mix, "ch", [(i, i ^ 2) for i in range(ch_count)])
    near = lax.ppermute(gated_mix, "ch", [(i, i ^ 1) for i in range(ch_count)])
    total = part(gated_mix, here) + part(near, here ^ 1)
    far, total = lax.optimization_barrier((far, total))
    near_far = lax.ppermute(far, "ch", [(i, i ^ 1) for i in range(ch_count)])
    total = total + part(far, here ^ 2)
    return total + part(near_far, here ^ 3)


def shards(projected, tap_weights, pole_rates, residues, long_bias, out_weight):
    row_count = projected.shape[1]
    width = projected.shape[2]
    rows = width // LANES
    pole_count = pole_rates.shape[0]
    rim_rows = tap_weights.shape[0] - 1
    prior_rows = shifted(projected[:, row_count - rim_rows :], "ctx", 1)
    extended = jnp.concatenate([prior_rows, projected], 1)
    widened = lax.optimization_barrier(extended[1:3].astype(jnp.float32))
    mixed_input = (
        featurize(widened, tap_weights[:, 1:3], 0, row_count) * featurize(widened, tap_weights[:, 1:3], 1, row_count)
    ).astype(jnp.bfloat16)
    x = mixed_input.astype(jnp.float32)
    span = row_count // SEGMENTS

    decay = jnp.exp(-pole_rates)
    ends = run_end_state(x, decay)
    start = incoming_state(device_end(ends, pole_rates, span), pole_rates, row_count)
    starts = segment_starts(ends, start, pole_rates, span)
    ch_count = lax.axis_size("ch")
    groups = width // LANES
    if ch_count == 4 and groups >= 8:
        bounds = [0, (2 * groups) // 8 * LANES, (5 * groups) // 8 * LANES, width]
    else:
        bounds = [0, width]
    pieces = len(bounds) - 1
    gated = []
    far = []
    x_next = x
    for index in range(pieces):
        cols = slice(bounds[index], bounds[index + 1])
        group_count = (cols.stop - cols.start) // LANES
        long_part = run_recurrence(x_next, decay, residues, starts, cols.start // LANES, group_count)
        long_mix = long_part.astype(jnp.bfloat16)
        stream0 = featurize(extended[:, :, cols], tap_weights[:, :, cols], 0, row_count)
        gated_mix = stream0 * (
            long_mix.astype(jnp.float32) + long_bias[None, cols] * mixed_input[:, cols].astype(jnp.float32)
        )
        gated_mix = gated_mix.astype(jnp.bfloat16)
        if index + 1 < pieces:
            x_next, gated_mix = lax.optimization_barrier((x, gated_mix))
        gated.append(gated_mix)
        if pieces > 1:
            far.append(lax.ppermute(gated_mix, "ch", [(i, i ^ 2) for i in range(ch_count)]))
        if index + 1 < pieces and index >= 1:
            x_next, far[index - 1] = lax.optimization_barrier((x_next, far[index - 1]))
    if pieces == 1:
        return project(gated[0], out_weight).astype(jnp.bfloat16)
    return project_pieces(gated, far, out_weight).astype(jnp.bfloat16)


def project_pieces(gated, far, out_weight):
    ch_count = lax.axis_size("ch")
    offsets = [0]
    for value in gated:
        offsets.append(offsets[-1] + value.shape[1])
    width = offsets[-1]
    here = lax.axis_index("ch")
    other_core = [(i, i ^ 1) for i in range(ch_count)]
    other_chip = [(i, i ^ 2) for i in range(ch_count)]

    def part(value, owner, index):
        rows = lax.dynamic_slice_in_dim(out_weight, owner * width + offsets[index], value.shape[1], 0)
        return jnp.dot(value, rows, preferred_element_type=jnp.float32)

    far = list(far)
    own = jnp.concatenate(gated, 1)
    early = len(far) - 1
    own, early_far = lax.optimization_barrier((own, far[:early]))
    far[:early] = early_far
    near = lax.ppermute(own, "ch", other_core)
    near_far = [lax.ppermute(f, "ch", other_core) for f in far[:early]]
    rows_own = lax.dynamic_slice_in_dim(out_weight, here * width, width, 0)
    rows_near = lax.dynamic_slice_in_dim(out_weight, (here ^ 1) * width, width, 0)
    total = jnp.dot(own, rows_own, preferred_element_type=jnp.float32)
    for index in range(early):
        total = total + part(far[index], here ^ 2, index)
    total = total + jnp.dot(near, rows_near, preferred_element_type=jnp.float32)
    for index in range(early):
        total = total + part(near_far[index], here ^ 3, index)
    last = far[early]
    last, total = lax.optimization_barrier((last, total))
    near_last = lax.ppermute(last, "ch", other_core)
    total = total + part(last, here ^ 2, early)
    total = total + part(near_last, here ^ 3, early)
    return total


def solution(mesh):
    in_specs = (
        P(None, "ctx", "ch"),
        P(None, None, "ch"),
        P(None, "ch"),
        P(None, "ch"),
        P("ch"),
        P(None, "ch"),
    )
    out_specs = P("ctx", "ch")
    return jax.shard_map(shards, mesh=mesh, in_specs=in_specs, out_specs=out_specs, check_vma=False)
```

```python
import jax
import jax.numpy as jnp
from jax import lax
from jax.experimental import pallas as pl
from jax.experimental.pallas import tpu as pltpu
from jax.sharding import PartitionSpec as P

LANES = 128
SEGMENTS = 8


def shifted(value, axis, steps):
    count = lax.axis_size(axis)
    initial, last = (max(0, -steps), min(count, count - steps))
    return lax.ppermute(value, axis, [(source, source + steps) for source in range(initial, last)])


def segment_pass(x_ref, decay_ref, residue_ref, start_ref, y_ref, end_ref):
    pole_count = decay_ref.shape[0]
    segments = SEGMENTS
    span = x_ref.shape[0] // segments
    lanes = x_ref.shape[1]
    decays = [jnp.broadcast_to(decay_ref[p : p + 1, :], (segments, lanes)) for p in range(pole_count)]
    if residue_ref is not None:
        residues = [jnp.broadcast_to(residue_ref[p : p + 1, :], (segments, lanes)) for p in range(pole_count)]
    if start_ref is None:
        states = tuple(jnp.zeros((segments, lanes), jnp.float32) for _ in range(pole_count))
    else:
        states = tuple(start_ref[p] for p in range(pole_count))

    def body(t, states):
        x = x_ref[pl.ds(t, segments, stride=span), :]
        updated = []
        total = None
        for p in range(pole_count):
            h = decays[p] * states[p] + x
            updated.append(h)
            if y_ref is not None:
                term = residues[p] * h
                total = term if total is None else total + term
        if y_ref is not None:
            y_ref[pl.ds(t, segments, stride=span), :] = total
        return tuple(updated)

    states = lax.fori_loop(0, span, body, states, unroll=128)
    if end_ref is not None:
        for p in range(pole_count):
            end_ref[p] = states[p]


def end_state_kernel(x_ref, decay_ref, end_ref):
    segment_pass(x_ref, decay_ref, None, None, None, end_ref)


def recurrence_kernel(x_ref, decay_ref, residue_ref, start_ref, y_ref):
    segment_pass(x_ref, decay_ref, residue_ref, start_ref, y_ref, None)


def run_end_state(x, decay):
    length, width = x.shape
    pole_count = decay.shape[0]
    return pl.pallas_call(
        end_state_kernel,
        grid=(width // LANES,),
        in_specs=[
            pl.BlockSpec((length, LANES), lambda g: (0, g)),
            pl.BlockSpec((pole_count, LANES), lambda g: (0, g)),
        ],
        out_specs=pl.BlockSpec((pole_count, SEGMENTS, LANES), lambda g: (0, 0, g)),
        out_shape=jax.ShapeDtypeStruct((pole_count, SEGMENTS, width), jnp.float32),
    )(x, decay)


def run_recurrence(x, decay, residue, start, first_group, group_count):
    length = x.shape[0]
    pole_count = decay.shape[0]
    pole_spec = pl.BlockSpec((pole_count, LANES), lambda g: (0, g + first_group))
    return pl.pallas_call(
        recurrence_kernel,
        grid=(group_count,),
        in_specs=[
            pl.BlockSpec((length, LANES), lambda g: (0, g + first_group)),
            pole_spec,
            pole_spec,
            pl.BlockSpec((pole_count, SEGMENTS, LANES), lambda g: (0, 0, g + first_group)),
        ],
        out_specs=pl.BlockSpec((length, LANES), lambda g: (0, g)),
        out_shape=jax.ShapeDtypeStruct((length, group_count * LANES), jnp.float32),
    )(x, decay, residue, start)


def segment_starts(ends, incoming, pole_rates, span):
    segments = ends.shape[1]
    index = jnp.arange(segments, dtype=jnp.int32)
    gaps = (index[:, None] - 1 - index[None, :]).astype(jnp.float32)
    weights = jnp.where(
        (index[None, :] < index[:, None])[:, :, None, None],
        jnp.exp(-pole_rates[None, None] * (jnp.float32(span) * jnp.maximum(gaps, 0.0))[:, :, None, None]),
        jnp.float32(0.0),
    )
    carried = jnp.einsum("abpc,pbc->pac", weights, ends, precision=lax.Precision.HIGHEST)
    lead = jnp.exp(-pole_rates[:, None, :] * (jnp.float32(span) * index.astype(jnp.float32))[None, :, None])
    return carried + lead * incoming[:, None, :]


def device_end(ends, pole_rates, span):
    segments = ends.shape[1]
    index = jnp.arange(segments, dtype=jnp.float32)
    weights = jnp.exp(-pole_rates[:, None, :] * (jnp.float32(span) * (segments - 1 - index))[None, :, None])
    return jnp.sum(weights * ends, axis=1)


def incoming_state(local_end, pole_rates, row_count):
    ctx_count = lax.axis_size("ctx")
    total = jnp.zeros_like(local_end)
    for distance in range(1, ctx_count):
        received = shifted(local_end, "ctx", distance)
        total = total + jnp.exp(-pole_rates * jnp.float32(row_count * (distance - 1))) * received
    return total


def featurize(extended, tap_weights, stream, count):
    taps = tap_weights.shape[0]
    total = None
    for tap_index in range(taps):
        lead_row = taps - 1 - tap_index
        term = tap_weights[tap_index, stream].astype(jnp.float32)[None, :] * extended[
            stream, lead_row : lead_row + count
        ].astype(jnp.float32)
        total = term if total is None else total + term
    return total


def project(gated_mix, out_weight):
    ch_count = lax.axis_size("ch")
    width = gated_mix.shape[1]
    if ch_count != 4:
        gathered = lax.all_gather(gated_mix, "ch", axis=1, tiled=True)
        return jnp.dot(gathered, out_weight, preferred_element_type=jnp.float32)
    here = lax.axis_index("ch")

    def part(piece, owner):
        rows = lax.dynamic_slice_in_dim(out_weight, owner * width, width, 0)
        return jnp.dot(piece, rows, preferred_element_type=jnp.float32)

    far = lax.ppermute(gated_mix, "ch", [(i, i ^ 2) for i in range(ch_count)])
    near = lax.ppermute(gated_mix, "ch", [(i, i ^ 1) for i in range(ch_count)])
    total = part(gated_mix, here) + part(near, here ^ 1)
    far, total = lax.optimization_barrier((far, total))
    near_far = lax.ppermute(far, "ch", [(i, i ^ 1) for i in range(ch_count)])
    total = total + part(far, here ^ 2)
    return total + part(near_far, here ^ 3)


def shards(projected, tap_weights, pole_rates, residues, long_bias, out_weight):
    row_count = projected.shape[1]
    width = projected.shape[2]
    rows = width // LANES
    pole_count = pole_rates.shape[0]
    rim_rows = tap_weights.shape[0] - 1
    prior_rows = shifted(projected[:, row_count - rim_rows :], "ctx", 1)
    extended = jnp.concatenate([prior_rows, projected], 1)
    widened = lax.optimization_barrier(extended[1:3].astype(jnp.float32))
    mixed_input = (
        featurize(widened, tap_weights[:, 1:3], 0, row_count) * featurize(widened, tap_weights[:, 1:3], 1, row_count)
    ).astype(jnp.bfloat16)
    x = mixed_input.astype(jnp.float32)
    span = row_count // SEGMENTS

    decay = jnp.exp(-pole_rates)
    ends = run_end_state(x, decay)
    start = incoming_state(device_end(ends, pole_rates, span), pole_rates, row_count)
    starts = segment_starts(ends, start, pole_rates, span)
    ch_count = lax.axis_size("ch")
    groups = width // LANES
    if ch_count == 4 and groups >= 8:
        bounds = [0, (2 * groups) // 8 * LANES, (5 * groups) // 8 * LANES, width]
    else:
        bounds = [0, width]
    pieces = len(bounds) - 1
    gated = []
    far = []
    x_next = x
    for index in range(pieces):
        cols = slice(bounds[index], bounds[index + 1])
        group_count = (cols.stop - cols.start) // LANES
        long_part = run_recurrence(x_next, decay, residues, starts, cols.start // LANES, group_count)
        long_mix = long_part.astype(jnp.bfloat16)
        stream0 = featurize(extended[:, :, cols], tap_weights[:, :, cols], 0, row_count)
        gated_mix = stream0 * (
            long_mix.astype(jnp.float32) + long_bias[None, cols] * mixed_input[:, cols].astype(jnp.float32)
        )
        gated_mix = gated_mix.astype(jnp.bfloat16)
        if index + 1 < pieces:
            x_next, gated_mix = lax.optimization_barrier((x, gated_mix))
        gated.append(gated_mix)
        if pieces > 1:
            far.append(lax.ppermute(gated_mix, "ch", [(i, i ^ 2) for i in range(ch_count)]))
        if index + 1 < pieces and index >= 1:
            x_next, far[index - 1] = lax.optimization_barrier((x_next, far[index - 1]))
    if pieces == 1:
        return project(gated[0], out_weight).astype(jnp.bfloat16)
    return project_pieces(gated, far, out_weight).astype(jnp.bfloat16)


def project_pieces(gated, far, out_weight):
    ch_count = lax.axis_size("ch")
    offsets = [0]
    for value in gated:
        offsets.append(offsets[-1] + value.shape[1])
    width = offsets[-1]
    here = lax.axis_index("ch")
    other_core = [(i, i ^ 1) for i in range(ch_count)]
    other_chip = [(i, i ^ 2) for i in range(ch_count)]

    def part(value, owner, index):
        rows = lax.dynamic_slice_in_dim(out_weight, owner * width + offsets[index], value.shape[1], 0)
        return jnp.dot(value, rows, preferred_element_type=jnp.float32)

    far = list(far)
    own = jnp.concatenate(gated, 1)
    early = len(far) - 1
    own, early_far = lax.optimization_barrier((own, far[:early]))
    far[:early] = early_far
    near = lax.ppermute(own, "ch", other_core)
    near_far = [lax.ppermute(f, "ch", other_core) for f in far[:early]]
    rows_own = lax.dynamic_slice_in_dim(out_weight, here * width, width, 0)
    rows_near = lax.dynamic_slice_in_dim(out_weight, (here ^ 1) * width, width, 0)
    total = jnp.dot(own, rows_own, preferred_element_type=jnp.float32)
    for index in range(early):
        total = total + part(far[index], here ^ 2, index)
    total = total + jnp.dot(near, rows_near, preferred_element_type=jnp.float32)
    for index in range(early):
        total = total + part(near_far[index], here ^ 3, index)
    last = far[early]
    last, total = lax.optimization_barrier((last, total))
    near_last = lax.ppermute(last, "ch", other_core)
    total = total + part(last, here ^ 2, early)
    total = total + part(near_last, here ^ 3, early)
    return total


def solution(mesh):
    in_specs = (
        P(None, "ctx", "ch"),
        P(None, None, "ch"),
        P(None, "ch"),
        P(None, "ch"),
        P("ch"),
        P(None, "ch"),
    )
    out_specs = P("ctx", "ch")
    return jax.shard_map(shards, mesh=mesh, in_specs=in_specs, out_specs=out_specs, check_vma=False)
```

```python
import jax
import jax.numpy as jnp
from jax import lax
from jax.experimental import pallas as pl
from jax.experimental.pallas import tpu as pltpu
from jax.sharding import PartitionSpec as P

LANES = 128
SEGMENTS = 8


def shifted(value, axis, steps):
    count = lax.axis_size(axis)
    initial, last = (max(0, -steps), min(count, count - steps))
    return lax.ppermute(value, axis, [(source, source + steps) for source in range(initial, last)])


def segment_pass(x_ref, decay_ref, residue_ref, start_ref, y_ref, end_ref, unroll):
    pole_count = decay_ref.shape[0]
    segments = SEGMENTS
    span = x_ref.shape[0] // segments
    lanes = x_ref.shape[1]
    decays = [jnp.broadcast_to(decay_ref[p : p + 1, :], (segments, lanes)) for p in range(pole_count)]
    if residue_ref is not None:
        residues = [jnp.broadcast_to(residue_ref[p : p + 1, :], (segments, lanes)) for p in range(pole_count)]
    if start_ref is None:
        states = tuple(jnp.zeros((segments, lanes), jnp.float32) for _ in range(pole_count))
    else:
        states = tuple(start_ref[p] for p in range(pole_count))

    def body(t, states):
        x = x_ref[pl.ds(t, segments, stride=span), :]
        updated = []
        total = None
        for p in range(pole_count):
            h = decays[p] * states[p] + x
            updated.append(h)
            if y_ref is not None:
                term = residues[p] * h
                total = term if total is None else total + term
        if y_ref is not None:
            y_ref[pl.ds(t, segments, stride=span), :] = total
        return tuple(updated)

    states = lax.fori_loop(0, span, body, states, unroll=min(unroll, span))
    if end_ref is not None:
        for p in range(pole_count):
            end_ref[p] = states[p]


def end_state_kernel(x_ref, decay_ref, end_ref):
    segment_pass(x_ref, decay_ref, None, None, None, end_ref, 32)


def recurrence_kernel(x_ref, decay_ref, residue_ref, start_ref, y_ref):
    segment_pass(x_ref, decay_ref, residue_ref, start_ref, y_ref, None, 128)


def run_end_state(x, decay):
    length, width = x.shape
    pole_count = decay.shape[0]
    return pl.pallas_call(
        end_state_kernel,
        grid=(width // LANES,),
        in_specs=[
            pl.BlockSpec((length, LANES), lambda g: (0, g)),
            pl.BlockSpec((pole_count, LANES), lambda g: (0, g)),
        ],
        out_specs=pl.BlockSpec((pole_count, SEGMENTS, LANES), lambda g: (0, 0, g)),
        out_shape=jax.ShapeDtypeStruct((pole_count, SEGMENTS, width), jnp.float32),
    )(x, decay)


def run_recurrence(x, decay, residue, start, first_group, group_count):
    length = x.shape[0]
    pole_count = decay.shape[0]
    pole_spec = pl.BlockSpec((pole_count, LANES), lambda g: (0, g + first_group))
    return pl.pallas_call(
        recurrence_kernel,
        grid=(group_count,),
        in_specs=[
            pl.BlockSpec((length, LANES), lambda g: (0, g + first_group)),
            pole_spec,
            pole_spec,
            pl.BlockSpec((pole_count, SEGMENTS, LANES), lambda g: (0, 0, g + first_group)),
        ],
        out_specs=pl.BlockSpec((length, LANES), lambda g: (0, g)),
        out_shape=jax.ShapeDtypeStruct((length, group_count * LANES), jnp.float32),
    )(x, decay, residue, start)


def segment_starts(ends, incoming, pole_rates, span):
    segments = ends.shape[1]
    index = jnp.arange(segments, dtype=jnp.int32)
    gaps = (index[:, None] - 1 - index[None, :]).astype(jnp.float32)
    weights = jnp.where(
        (index[None, :] < index[:, None])[:, :, None, None],
        jnp.exp(-pole_rates[None, None] * (jnp.float32(span) * jnp.maximum(gaps, 0.0))[:, :, None, None]),
        jnp.float32(0.0),
    )
    carried = jnp.einsum("abpc,pbc->pac", weights, ends, precision=lax.Precision.HIGHEST)
    lead = jnp.exp(-pole_rates[:, None, :] * (jnp.float32(span) * index.astype(jnp.float32))[None, :, None])
    return carried + lead * incoming[:, None, :]


def device_end(ends, pole_rates, span):
    segments = ends.shape[1]
    index = jnp.arange(segments, dtype=jnp.float32)
    weights = jnp.exp(-pole_rates[:, None, :] * (jnp.float32(span) * (segments - 1 - index))[None, :, None])
    return jnp.sum(weights * ends, axis=1)


def incoming_state(local_end, pole_rates, row_count):
    ctx_count = lax.axis_size("ctx")
    total = jnp.zeros_like(local_end)
    for distance in range(1, ctx_count):
        received = shifted(local_end, "ctx", distance)
        total = total + jnp.exp(-pole_rates * jnp.float32(row_count * (distance - 1))) * received
    return total


def featurize(extended, tap_weights, stream, count):
    taps = tap_weights.shape[0]
    total = None
    for tap_index in range(taps):
        lead_row = taps - 1 - tap_index
        term = tap_weights[tap_index, stream].astype(jnp.float32)[None, :] * extended[
            stream, lead_row : lead_row + count
        ].astype(jnp.float32)
        total = term if total is None else total + term
    return total


def project(gated_mix, out_weight):
    ch_count = lax.axis_size("ch")
    width = gated_mix.shape[1]
    if ch_count != 4:
        gathered = lax.all_gather(gated_mix, "ch", axis=1, tiled=True)
        return jnp.dot(gathered, out_weight, preferred_element_type=jnp.float32)
    here = lax.axis_index("ch")

    def part(piece, owner):
        rows = lax.dynamic_slice_in_dim(out_weight, owner * width, width, 0)
        return jnp.dot(piece, rows, preferred_element_type=jnp.float32)

    far = lax.ppermute(gated_mix, "ch", [(i, i ^ 2) for i in range(ch_count)])
    near = lax.ppermute(gated_mix, "ch", [(i, i ^ 1) for i in range(ch_count)])
    total = part(gated_mix, here) + part(near, here ^ 1)
    far, total = lax.optimization_barrier((far, total))
    near_far = lax.ppermute(far, "ch", [(i, i ^ 1) for i in range(ch_count)])
    total = total + part(far, here ^ 2)
    return total + part(near_far, here ^ 3)


def shards(projected, tap_weights, pole_rates, residues, long_bias, out_weight):
    row_count = projected.shape[1]
    width = projected.shape[2]
    rows = width // LANES
    pole_count = pole_rates.shape[0]
    rim_rows = tap_weights.shape[0] - 1
    prior_rows = shifted(projected[:, row_count - rim_rows :], "ctx", 1)
    extended = jnp.concatenate([prior_rows, projected], 1)
    widened = lax.optimization_barrier(extended[1:3].astype(jnp.float32))
    mixed_input = (
        featurize(widened, tap_weights[:, 1:3], 0, row_count) * featurize(widened, tap_weights[:, 1:3], 1, row_count)
    ).astype(jnp.bfloat16)
    x = mixed_input.astype(jnp.float32)
    span = row_count // SEGMENTS

    decay = jnp.exp(-pole_rates)
    ends = run_end_state(x, decay)
    start = incoming_state(device_end(ends, pole_rates, span), pole_rates, row_count)
    starts = segment_starts(ends, start, pole_rates, span)
    ch_count = lax.axis_size("ch")
    groups = width // LANES
    if ch_count == 4 and groups >= 8:
        bounds = [0, (2 * groups) // 8 * LANES, (5 * groups) // 8 * LANES, width]
    else:
        bounds = [0, width]
    pieces = len(bounds) - 1
    gated = []
    far = []
    x_next = x
    for index in range(pieces):
        cols = slice(bounds[index], bounds[index + 1])
        group_count = (cols.stop - cols.start) // LANES
        long_part = run_recurrence(x_next, decay, residues, starts, cols.start // LANES, group_count)
        long_mix = long_part.astype(jnp.bfloat16)
        stream0 = featurize(extended[:, :, cols], tap_weights[:, :, cols], 0, row_count)
        gated_mix = stream0 * (
            long_mix.astype(jnp.float32) + long_bias[None, cols] * mixed_input[:, cols].astype(jnp.float32)
        )
        gated_mix = gated_mix.astype(jnp.bfloat16)
        if index + 1 < pieces:
            x_next, gated_mix = lax.optimization_barrier((x, gated_mix))
        gated.append(gated_mix)
        if pieces > 1:
            far.append(lax.ppermute(gated_mix, "ch", [(i, i ^ 2) for i in range(ch_count)]))
        if index + 1 < pieces and index >= 1:
            x_next, far[index - 1] = lax.optimization_barrier((x_next, far[index - 1]))
    if pieces == 1:
        return project(gated[0], out_weight).astype(jnp.bfloat16)
    return project_pieces(gated, far, out_weight).astype(jnp.bfloat16)


def project_pieces(gated, far, out_weight):
    ch_count = lax.axis_size("ch")
    offsets = [0]
    for value in gated:
        offsets.append(offsets[-1] + value.shape[1])
    width = offsets[-1]
    here = lax.axis_index("ch")
    other_core = [(i, i ^ 1) for i in range(ch_count)]
    other_chip = [(i, i ^ 2) for i in range(ch_count)]

    def part(value, owner, index):
        rows = lax.dynamic_slice_in_dim(out_weight, owner * width + offsets[index], value.shape[1], 0)
        return jnp.dot(value, rows, preferred_element_type=jnp.float32)

    far = list(far)
    own = jnp.concatenate(gated, 1)
    early = len(far) - 1
    own, early_far = lax.optimization_barrier((own, far[:early]))
    far[:early] = early_far
    near = lax.ppermute(own, "ch", other_core)
    near_far = [lax.ppermute(f, "ch", other_core) for f in far[:early]]
    rows_own = lax.dynamic_slice_in_dim(out_weight, here * width, width, 0)
    rows_near = lax.dynamic_slice_in_dim(out_weight, (here ^ 1) * width, width, 0)
    total = jnp.dot(own, rows_own, preferred_element_type=jnp.float32)
    for index in range(early):
        total = total + part(far[index], here ^ 2, index)
    total = total + jnp.dot(near, rows_near, preferred_element_type=jnp.float32)
    for index in range(early):
        total = total + part(near_far[index], here ^ 3, index)
    last = far[early]
    last, total = lax.optimization_barrier((last, total))
    near_last = lax.ppermute(last, "ch", other_core)
    total = total + part(last, here ^ 2, early)
    total = total + part(near_last, here ^ 3, early)
    return total


def solution(mesh):
    in_specs = (
        P(None, "ctx", "ch"),
        P(None, None, "ch"),
        P(None, "ch"),
        P(None, "ch"),
        P("ch"),
        P(None, "ch"),
    )
    out_specs = P("ctx", "ch")
    return jax.shard_map(shards, mesh=mesh, in_specs=in_specs, out_specs=out_specs, check_vma=False)
```

```python
import jax
import jax.numpy as jnp
from jax import lax
from jax.experimental import pallas as pl
from jax.experimental.pallas import tpu as pltpu
from jax.sharding import PartitionSpec as P

LANES = 128
SEGMENTS = 8


def shifted(value, axis, steps):
    count = lax.axis_size(axis)
    initial, last = (max(0, -steps), min(count, count - steps))
    return lax.ppermute(value, axis, [(source, source + steps) for source in range(initial, last)])


def segment_pass(x_ref, decay_ref, residue_ref, start_ref, y_ref, end_ref, unroll):
    pole_count = decay_ref.shape[0]
    segments = SEGMENTS
    span = x_ref.shape[0] // segments
    lanes = x_ref.shape[1]
    decays = [jnp.broadcast_to(decay_ref[p : p + 1, :], (segments, lanes)) for p in range(pole_count)]
    if residue_ref is not None:
        residues = [jnp.broadcast_to(residue_ref[p : p + 1, :], (segments, lanes)) for p in range(pole_count)]
    if start_ref is None:
        states = tuple(jnp.zeros((segments, lanes), jnp.float32) for _ in range(pole_count))
    else:
        states = tuple(start_ref[p] for p in range(pole_count))

    def body(t, states):
        x = x_ref[pl.ds(t, segments, stride=span), :]
        updated = []
        total = None
        for p in range(pole_count):
            h = decays[p] * states[p] + x
            updated.append(h)
            if y_ref is not None:
                term = residues[p] * h
                total = term if total is None else total + term
        if y_ref is not None:
            y_ref[pl.ds(t, segments, stride=span), :] = total
        return tuple(updated)

    states = lax.fori_loop(0, span, body, states, unroll=min(unroll, span))
    if end_ref is not None:
        for p in range(pole_count):
            end_ref[p] = states[p]


def end_state_kernel(x_ref, decay_ref, end_ref):
    segment_pass(x_ref, decay_ref, None, None, None, end_ref, 64)


def recurrence_kernel(x_ref, decay_ref, residue_ref, start_ref, y_ref):
    segment_pass(x_ref, decay_ref, residue_ref, start_ref, y_ref, None, 128)


def run_end_state(x, decay):
    length, width = x.shape
    pole_count = decay.shape[0]
    return pl.pallas_call(
        end_state_kernel,
        grid=(width // LANES,),
        in_specs=[
            pl.BlockSpec((length, LANES), lambda g: (0, g)),
            pl.BlockSpec((pole_count, LANES), lambda g: (0, g)),
        ],
        out_specs=pl.BlockSpec((pole_count, SEGMENTS, LANES), lambda g: (0, 0, g)),
        out_shape=jax.ShapeDtypeStruct((pole_count, SEGMENTS, width), jnp.float32),
    )(x, decay)


def run_recurrence(x, decay, residue, start, first_group, group_count):
    length = x.shape[0]
    pole_count = decay.shape[0]
    pole_spec = pl.BlockSpec((pole_count, LANES), lambda g: (0, g + first_group))
    return pl.pallas_call(
        recurrence_kernel,
        grid=(group_count,),
        in_specs=[
            pl.BlockSpec((length, LANES), lambda g: (0, g + first_group)),
            pole_spec,
            pole_spec,
            pl.BlockSpec((pole_count, SEGMENTS, LANES), lambda g: (0, 0, g + first_group)),
        ],
        out_specs=pl.BlockSpec((length, LANES), lambda g: (0, g)),
        out_shape=jax.ShapeDtypeStruct((length, group_count * LANES), jnp.float32),
    )(x, decay, residue, start)


def segment_starts(ends, incoming, pole_rates, span):
    segments = ends.shape[1]
    index = jnp.arange(segments, dtype=jnp.int32)
    gaps = (index[:, None] - 1 - index[None, :]).astype(jnp.float32)
    weights = jnp.where(
        (index[None, :] < index[:, None])[:, :, None, None],
        jnp.exp(-pole_rates[None, None] * (jnp.float32(span) * jnp.maximum(gaps, 0.0))[:, :, None, None]),
        jnp.float32(0.0),
    )
    carried = jnp.einsum("abpc,pbc->pac", weights, ends, precision=lax.Precision.HIGHEST)
    lead = jnp.exp(-pole_rates[:, None, :] * (jnp.float32(span) * index.astype(jnp.float32))[None, :, None])
    return carried + lead * incoming[:, None, :]


def device_end(ends, pole_rates, span):
    segments = ends.shape[1]
    index = jnp.arange(segments, dtype=jnp.float32)
    weights = jnp.exp(-pole_rates[:, None, :] * (jnp.float32(span) * (segments - 1 - index))[None, :, None])
    return jnp.sum(weights * ends, axis=1)


def incoming_state(local_end, pole_rates, row_count):
    ctx_count = lax.axis_size("ctx")
    total = jnp.zeros_like(local_end)
    for distance in range(1, ctx_count):
        received = shifted(local_end, "ctx", distance)
        total = total + jnp.exp(-pole_rates * jnp.float32(row_count * (distance - 1))) * received
    return total


def featurize(extended, tap_weights, stream, count):
    taps = tap_weights.shape[0]
    total = None
    for tap_index in range(taps):
        lead_row = taps - 1 - tap_index
        term = tap_weights[tap_index, stream].astype(jnp.float32)[None, :] * extended[
            stream, lead_row : lead_row + count
        ].astype(jnp.float32)
        total = term if total is None else total + term
    return total


def project(gated_mix, out_weight):
    ch_count = lax.axis_size("ch")
    width = gated_mix.shape[1]
    if ch_count != 4:
        gathered = lax.all_gather(gated_mix, "ch", axis=1, tiled=True)
        return jnp.dot(gathered, out_weight, preferred_element_type=jnp.float32)
    here = lax.axis_index("ch")

    def part(piece, owner):
        rows = lax.dynamic_slice_in_dim(out_weight, owner * width, width, 0)
        return jnp.dot(piece, rows, preferred_element_type=jnp.float32)

    far = lax.ppermute(gated_mix, "ch", [(i, i ^ 2) for i in range(ch_count)])
    near = lax.ppermute(gated_mix, "ch", [(i, i ^ 1) for i in range(ch_count)])
    total = part(gated_mix, here) + part(near, here ^ 1)
    far, total = lax.optimization_barrier((far, total))
    near_far = lax.ppermute(far, "ch", [(i, i ^ 1) for i in range(ch_count)])
    total = total + part(far, here ^ 2)
    return total + part(near_far, here ^ 3)


def shards(projected, tap_weights, pole_rates, residues, long_bias, out_weight):
    row_count = projected.shape[1]
    width = projected.shape[2]
    rows = width // LANES
    pole_count = pole_rates.shape[0]
    rim_rows = tap_weights.shape[0] - 1
    prior_rows = shifted(projected[:, row_count - rim_rows :], "ctx", 1)
    extended = jnp.concatenate([prior_rows, projected], 1)
    widened = lax.optimization_barrier(extended[1:3].astype(jnp.float32))
    mixed_input = (
        featurize(widened, tap_weights[:, 1:3], 0, row_count) * featurize(widened, tap_weights[:, 1:3], 1, row_count)
    ).astype(jnp.bfloat16)
    x = mixed_input.astype(jnp.float32)
    span = row_count // SEGMENTS

    decay = jnp.exp(-pole_rates)
    ends = run_end_state(x, decay)
    start = incoming_state(device_end(ends, pole_rates, span), pole_rates, row_count)
    starts = segment_starts(ends, start, pole_rates, span)
    ch_count = lax.axis_size("ch")
    groups = width // LANES
    if ch_count == 4 and groups >= 8:
        bounds = [0, (2 * groups) // 8 * LANES, (5 * groups) // 8 * LANES, width]
    else:
        bounds = [0, width]
    pieces = len(bounds) - 1
    gated = []
    far = []
    x_next = x
    for index in range(pieces):
        cols = slice(bounds[index], bounds[index + 1])
        group_count = (cols.stop - cols.start) // LANES
        long_part = run_recurrence(x_next, decay, residues, starts, cols.start // LANES, group_count)
        long_mix = long_part.astype(jnp.bfloat16)
        stream0 = featurize(extended[:, :, cols], tap_weights[:, :, cols], 0, row_count)
        gated_mix = stream0 * (
            long_mix.astype(jnp.float32) + long_bias[None, cols] * mixed_input[:, cols].astype(jnp.float32)
        )
        gated_mix = gated_mix.astype(jnp.bfloat16)
        if index + 1 < pieces:
            x_next, gated_mix = lax.optimization_barrier((x, gated_mix))
        gated.append(gated_mix)
        if pieces > 1:
            far.append(lax.ppermute(gated_mix, "ch", [(i, i ^ 2) for i in range(ch_count)]))
        if index + 1 < pieces and index >= 1:
            x_next, far[index - 1] = lax.optimization_barrier((x_next, far[index - 1]))
    if pieces == 1:
        return project(gated[0], out_weight).astype(jnp.bfloat16)
    return project_pieces(gated, far, out_weight).astype(jnp.bfloat16)


def project_pieces(gated, far, out_weight):
    ch_count = lax.axis_size("ch")
    offsets = [0]
    for value in gated:
        offsets.append(offsets[-1] + value.shape[1])
    width = offsets[-1]
    here = lax.axis_index("ch")
    other_core = [(i, i ^ 1) for i in range(ch_count)]
    other_chip = [(i, i ^ 2) for i in range(ch_count)]

    def part(value, owner, index):
        rows = lax.dynamic_slice_in_dim(out_weight, owner * width + offsets[index], value.shape[1], 0)
        return jnp.dot(value, rows, preferred_element_type=jnp.float32)

    far = list(far)
    own = jnp.concatenate(gated, 1)
    early = len(far) - 1
    own, early_far = lax.optimization_barrier((own, far[:early]))
    far[:early] = early_far
    near = lax.ppermute(own, "ch", other_core)
    near_far = [lax.ppermute(f, "ch", other_core) for f in far[:early]]
    rows_own = lax.dynamic_slice_in_dim(out_weight, here * width, width, 0)
    rows_near = lax.dynamic_slice_in_dim(out_weight, (here ^ 1) * width, width, 0)
    total = jnp.dot(own, rows_own, preferred_element_type=jnp.float32)
    for index in range(early):
        total = total + part(far[index], here ^ 2, index)
    total = total + jnp.dot(near, rows_near, preferred_element_type=jnp.float32)
    for index in range(early):
        total = total + part(near_far[index], here ^ 3, index)
    last = far[early]
    last, total = lax.optimization_barrier((last, total))
    near_last = lax.ppermute(last, "ch", other_core)
    total = total + part(last, here ^ 2, early)
    total = total + part(near_last, here ^ 3, early)
    return total


def solution(mesh):
    in_specs = (
        P(None, "ctx", "ch"),
        P(None, None, "ch"),
        P(None, "ch"),
        P(None, "ch"),
        P("ch"),
        P(None, "ch"),
    )
    out_specs = P("ctx", "ch")
    return jax.shard_map(shards, mesh=mesh, in_specs=in_specs, out_specs=out_specs, check_vma=False)
```

```python
import jax
import jax.numpy as jnp
from jax import lax
from jax.experimental import pallas as pl
from jax.experimental.pallas import tpu as pltpu
from jax.sharding import PartitionSpec as P

LANES = 128
SEGMENTS = 8


def shifted(value, axis, steps):
    count = lax.axis_size(axis)
    initial, last = (max(0, -steps), min(count, count - steps))
    return lax.ppermute(value, axis, [(source, source + steps) for source in range(initial, last)])


def segment_pass(x_ref, decay_ref, residue_ref, start_ref, y_ref, end_ref, unroll):
    pole_count = decay_ref.shape[0]
    segments = SEGMENTS
    span = x_ref.shape[0] // segments
    lanes = x_ref.shape[1]
    decays = [jnp.broadcast_to(decay_ref[p : p + 1, :], (segments, lanes)) for p in range(pole_count)]
    if residue_ref is not None:
        residues = [jnp.broadcast_to(residue_ref[p : p + 1, :], (segments, lanes)) for p in range(pole_count)]
    if start_ref is None:
        states = tuple(jnp.zeros((segments, lanes), jnp.float32) for _ in range(pole_count))
    else:
        states = tuple(start_ref[p] for p in range(pole_count))

    def body(t, states):
        x = x_ref[pl.ds(t, segments, stride=span), :]
        updated = []
        total = None
        for p in range(pole_count):
            h = decays[p] * states[p] + x
            updated.append(h)
            if y_ref is not None:
                term = residues[p] * h
                total = term if total is None else total + term
        if y_ref is not None:
            y_ref[pl.ds(t, segments, stride=span), :] = total
        return tuple(updated)

    states = lax.fori_loop(0, span, body, states, unroll=min(unroll, span))
    if end_ref is not None:
        for p in range(pole_count):
            end_ref[p] = states[p]


def end_state_kernel(x_ref, decay_ref, end_ref):
    segment_pass(x_ref, decay_ref, None, None, None, end_ref, 32)


def recurrence_kernel(x_ref, decay_ref, residue_ref, start_ref, y_ref):
    segment_pass(x_ref, decay_ref, residue_ref, start_ref, y_ref, None, 64)


def run_end_state(x, decay):
    length, width = x.shape
    pole_count = decay.shape[0]
    return pl.pallas_call(
        end_state_kernel,
        grid=(width // LANES,),
        in_specs=[
            pl.BlockSpec((length, LANES), lambda g: (0, g)),
            pl.BlockSpec((pole_count, LANES), lambda g: (0, g)),
        ],
        out_specs=pl.BlockSpec((pole_count, SEGMENTS, LANES), lambda g: (0, 0, g)),
        out_shape=jax.ShapeDtypeStruct((pole_count, SEGMENTS, width), jnp.float32),
    )(x, decay)


def run_recurrence(x, decay, residue, start, first_group, group_count):
    length = x.shape[0]
    pole_count = decay.shape[0]
    pole_spec = pl.BlockSpec((pole_count, LANES), lambda g: (0, g + first_group))
    return pl.pallas_call(
        recurrence_kernel,
        grid=(group_count,),
        in_specs=[
            pl.BlockSpec((length, LANES), lambda g: (0, g + first_group)),
            pole_spec,
            pole_spec,
            pl.BlockSpec((pole_count, SEGMENTS, LANES), lambda g: (0, 0, g + first_group)),
        ],
        out_specs=pl.BlockSpec((length, LANES), lambda g: (0, g)),
        out_shape=jax.ShapeDtypeStruct((length, group_count * LANES), jnp.float32),
    )(x, decay, residue, start)


def segment_starts(ends, incoming, pole_rates, span):
    segments = ends.shape[1]
    index = jnp.arange(segments, dtype=jnp.int32)
    gaps = (index[:, None] - 1 - index[None, :]).astype(jnp.float32)
    weights = jnp.where(
        (index[None, :] < index[:, None])[:, :, None, None],
        jnp.exp(-pole_rates[None, None] * (jnp.float32(span) * jnp.maximum(gaps, 0.0))[:, :, None, None]),
        jnp.float32(0.0),
    )
    carried = jnp.einsum("abpc,pbc->pac", weights, ends, precision=lax.Precision.HIGHEST)
    lead = jnp.exp(-pole_rates[:, None, :] * (jnp.float32(span) * index.astype(jnp.float32))[None, :, None])
    return carried + lead * incoming[:, None, :]


def device_end(ends, pole_rates, span):
    segments = ends.shape[1]
    index = jnp.arange(segments, dtype=jnp.float32)
    weights = jnp.exp(-pole_rates[:, None, :] * (jnp.float32(span) * (segments - 1 - index))[None, :, None])
    return jnp.sum(weights * ends, axis=1)


def incoming_state(local_end, pole_rates, row_count):
    ctx_count = lax.axis_size("ctx")
    total = jnp.zeros_like(local_end)
    for distance in range(1, ctx_count):
        received = shifted(local_end, "ctx", distance)
        total = total + jnp.exp(-pole_rates * jnp.float32(row_count * (distance - 1))) * received
    return total


def featurize(extended, tap_weights, stream, count):
    taps = tap_weights.shape[0]
    total = None
    for tap_index in range(taps):
        lead_row = taps - 1 - tap_index
        term = tap_weights[tap_index, stream].astype(jnp.float32)[None, :] * extended[
            stream, lead_row : lead_row + count
        ].astype(jnp.float32)
        total = term if total is None else total + term
    return total


def project(gated_mix, out_weight):
    ch_count = lax.axis_size("ch")
    width = gated_mix.shape[1]
    if ch_count != 4:
        gathered = lax.all_gather(gated_mix, "ch", axis=1, tiled=True)
        return jnp.dot(gathered, out_weight, preferred_element_type=jnp.float32)
    here = lax.axis_index("ch")

    def part(piece, owner):
        rows = lax.dynamic_slice_in_dim(out_weight, owner * width, width, 0)
        return jnp.dot(piece, rows, preferred_element_type=jnp.float32)

    far = lax.ppermute(gated_mix, "ch", [(i, i ^ 2) for i in range(ch_count)])
    near = lax.ppermute(gated_mix, "ch", [(i, i ^ 1) for i in range(ch_count)])
    total = part(gated_mix, here) + part(near, here ^ 1)
    far, total = lax.optimization_barrier((far, total))
    near_far = lax.ppermute(far, "ch", [(i, i ^ 1) for i in range(ch_count)])
    total = total + part(far, here ^ 2)
    return total + part(near_far, here ^ 3)


def shards(projected, tap_weights, pole_rates, residues, long_bias, out_weight):
    row_count = projected.shape[1]
    width = projected.shape[2]
    rows = width // LANES
    pole_count = pole_rates.shape[0]
    rim_rows = tap_weights.shape[0] - 1
    prior_rows = shifted(projected[:, row_count - rim_rows :], "ctx", 1)
    extended = jnp.concatenate([prior_rows, projected], 1)
    widened = lax.optimization_barrier(extended[1:3].astype(jnp.float32))
    mixed_input = (
        featurize(widened, tap_weights[:, 1:3], 0, row_count) * featurize(widened, tap_weights[:, 1:3], 1, row_count)
    ).astype(jnp.bfloat16)
    x = mixed_input.astype(jnp.float32)
    span = row_count // SEGMENTS

    decay = jnp.exp(-pole_rates)
    ends = run_end_state(x, decay)
    start = incoming_state(device_end(ends, pole_rates, span), pole_rates, row_count)
    starts = segment_starts(ends, start, pole_rates, span)
    ch_count = lax.axis_size("ch")
    groups = width // LANES
    if ch_count == 4 and groups >= 8:
        bounds = [0, (2 * groups) // 8 * LANES, (5 * groups) // 8 * LANES, width]
    else:
        bounds = [0, width]
    pieces = len(bounds) - 1
    gated = []
    far = []
    x_next = x
    for index in range(pieces):
        cols = slice(bounds[index], bounds[index + 1])
        group_count = (cols.stop - cols.start) // LANES
        long_part = run_recurrence(x_next, decay, residues, starts, cols.start // LANES, group_count)
        long_mix = long_part.astype(jnp.bfloat16)
        stream0 = featurize(extended[:, :, cols], tap_weights[:, :, cols], 0, row_count)
        gated_mix = stream0 * (
            long_mix.astype(jnp.float32) + long_bias[None, cols] * mixed_input[:, cols].astype(jnp.float32)
        )
        gated_mix = gated_mix.astype(jnp.bfloat16)
        if index + 1 < pieces:
            x_next, gated_mix = lax.optimization_barrier((x, gated_mix))
        gated.append(gated_mix)
        if pieces > 1:
            far.append(lax.ppermute(gated_mix, "ch", [(i, i ^ 2) for i in range(ch_count)]))
        if index + 1 < pieces and index >= 1:
            x_next, far[index - 1] = lax.optimization_barrier((x_next, far[index - 1]))
    if pieces == 1:
        return project(gated[0], out_weight).astype(jnp.bfloat16)
    return project_pieces(gated, far, out_weight).astype(jnp.bfloat16)


def project_pieces(gated, far, out_weight):
    ch_count = lax.axis_size("ch")
    offsets = [0]
    for value in gated:
        offsets.append(offsets[-1] + value.shape[1])
    width = offsets[-1]
    here = lax.axis_index("ch")
    other_core = [(i, i ^ 1) for i in range(ch_count)]
    other_chip = [(i, i ^ 2) for i in range(ch_count)]

    def part(value, owner, index):
        rows = lax.dynamic_slice_in_dim(out_weight, owner * width + offsets[index], value.shape[1], 0)
        return jnp.dot(value, rows, preferred_element_type=jnp.float32)

    far = list(far)
    own = jnp.concatenate(gated, 1)
    early = len(far) - 1
    own, early_far = lax.optimization_barrier((own, far[:early]))
    far[:early] = early_far
    near = lax.ppermute(own, "ch", other_core)
    near_far = [lax.ppermute(f, "ch", other_core) for f in far[:early]]
    rows_own = lax.dynamic_slice_in_dim(out_weight, here * width, width, 0)
    rows_near = lax.dynamic_slice_in_dim(out_weight, (here ^ 1) * width, width, 0)
    total = jnp.dot(own, rows_own, preferred_element_type=jnp.float32)
    for index in range(early):
        total = total + part(far[index], here ^ 2, index)
    total = total + jnp.dot(near, rows_near, preferred_element_type=jnp.float32)
    for index in range(early):
        total = total + part(near_far[index], here ^ 3, index)
    last = far[early]
    last, total = lax.optimization_barrier((last, total))
    near_last = lax.ppermute(last, "ch", other_core)
    total = total + part(last, here ^ 2, early)
    total = total + part(near_last, here ^ 3, early)
    return total


def solution(mesh):
    in_specs = (
        P(None, "ctx", "ch"),
        P(None, None, "ch"),
        P(None, "ch"),
        P(None, "ch"),
        P("ch"),
        P(None, "ch"),
    )
    out_specs = P("ctx", "ch")
    return jax.shard_map(shards, mesh=mesh, in_specs=in_specs, out_specs=out_specs, check_vma=False)
```
